32 devices in a mesh: segment: 8 (over z, y), head: 4 (over x, core).
Axes of the slice: x: 2, y: 2, z: 4, core: 2. Of those that a mesh axis runs over, the one named last changes fastest.
Arguments:
- entering_deriv: bfloat16 [1024, 3072], P('segment'), may hold values from -6 to 6
- objective_derivs: bfloat16 [128, 3072], replicated, may hold values from -6 to 6
- content_projection: bfloat16 [24576, 3072], P('segment', 'head'), may hold values from -0.109375 to 0.109375
- asker_projection: bfloat16 [1024, 3072], P('segment', 'head'), may hold values from -0.5 to 0.5
- lookup_projection: bfloat16 [1024, 3072], P('segment', 'head'), may hold values from -0.5 to 0.5
- softness: float32 [8, 24], P('segment', 'head'), may hold values from 15 to 50
- window_inputs: bfloat16 [5120, 128], P('segment'), may hold values from -6 to 6
- digest_inputs: bfloat16 [256, 128], replicated, may hold values from -6 to 6
- digest_pointer: int32 [16, 2], P('segment'), may hold values from 0 to 1
- initial_segment: int32 [1], replicated, may hold values from 512 to 520
- prior_content_derivs: bfloat16 [2048, 3072], P('segment', 'head'), may hold values from -3 to 3
Outputs:
- outgoing: bfloat16 [1024, 3072], P('segment', 'head')
- summary_grads: bfloat16 [2048, 3072], P('segment', 'head')
The draws below stay inside these ranges and needn't reach their ends.
All inputs are finite; a program needn't handle non-finite values.
Results may differ from the reference program's by a relative error of at most 0.01.
Values may be sent and summed in bfloat16 or wider, within the bound.
No kernel may reach another device: no remote copies, remote signals or barrier semaphores. Data moves between devices by JAX's collectives and lax.ppermute only.
A program may use at most 64 MiB of HBM per device.

```python
import math
import jax
import jax.numpy as jnp
from jax import lax

ATTENDER_TOTAL = 24
CHANNEL_WIDTH = 128
D = 3072
FEAT = 128
BLOCK = 128
BAND = 4
GLOB = 2
SUMMARY = 2
SEQ_BLOCKS = 1024
TICKS = 2
N_SEGMENT = 8
N_HEAD = 4


def plant(drawn, rng, least, top_value):
    longest = drawn.shape.index(max(drawn.shape))
    spots = []
    for shift in (0, 1):
        where = [jax.random.randint(jax.random.fold_in(rng, axis), (), 0, length) for axis, length in enumerate(drawn.shape)]
        where[longest] = (where[longest] + shift) % drawn.shape[longest]
        spots.append(tuple(where))
    return drawn.at[spots[0]].set(least).at[spots[1]].set(top_value)


def levels(own_key, shape, pieces, low, high):
    def one(dim, shards_of):
        draws = jax.random.uniform(jax.random.fold_in(jax.random.fold_in(own_key, 6), dim), (shards_of,), jnp.float32, low / len(pieces), high / len(pieces))
        return jnp.repeat(jnp.exp(draws), shape[dim] // shards_of).reshape((-1,) + (1,) * (len(shape) - dim - 1))

    loudness = one(*pieces[0])
    for cut in pieces[1:]:
        loudness = loudness * one(*cut)
    return loudness


def normal_values(rng, shape, spread, reach, shards=(), kind=jnp.bfloat16):
    values = spread * jax.random.normal(rng, shape, jnp.float32)
    if shards:
        values = values * levels(rng, shape, shards, -0.22, 0.18)
    return jnp.clip(values, -reach, reach).astype(kind)


def setup_inputs(seed: int = 0) -> dict:
    keys = jax.random.split(jax.random.key(seed), 12)
    return {
        "entering_deriv": normal_values(keys[0], (N_SEGMENT * BLOCK, D), 1.0, 6.0, ((0, 8),)),
        "objective_derivs": normal_values(keys[1], ((TICKS - 1) * BLOCK, D), 1.0, 6.0),
        "content_projection": normal_values(keys[2], (N_SEGMENT * D, D), D ** -0.5, 0.109375, ((0, 8), (1, 4))),
        "asker_projection": normal_values(keys[3], (N_SEGMENT * FEAT, D), FEAT ** -0.5, 0.5, ((0, 8), (1, 4))),
        "lookup_projection": normal_values(keys[4], (N_SEGMENT * FEAT, D), FEAT ** -0.5, 0.5, ((0, 8), (1, 4))),
        "softness": jnp.clip(jnp.exp(math.log(50.0) - 1.2039728 * jax.random.uniform(keys[5], (N_SEGMENT, ATTENDER_TOTAL), jnp.float32) ** levels(keys[5], (N_SEGMENT, ATTENDER_TOTAL), ((0, 8), (1, 4)), -0.2, 0.2)), 15.0, 50.0),
        "window_inputs": normal_values(keys[6], (N_SEGMENT * (TICKS + BAND - 1) * BLOCK, FEAT), 1.0, 6.0, ((0, 8),)),
        "digest_inputs": normal_values(keys[7], (SUMMARY * BLOCK, FEAT), 1.0, 6.0),
        "digest_pointer": plant(jax.random.randint(keys[8], (N_SEGMENT * TICKS, GLOB), 0, SUMMARY), jax.random.fold_in(keys[8], 1), 0, SUMMARY - 1).astype(jnp.int32),
        "initial_segment": jax.random.randint(keys[9], (1,), SEQ_BLOCKS // 2, SEQ_BLOCKS // 2 + N_SEGMENT + TICKS - 1).astype(jnp.int32),
        "prior_content_derivs": normal_values(keys[10], (N_SEGMENT * TICKS * BLOCK, D), 0.5, 3.0, ((0, 8), (1, 4))),
    }


EPS = 1e-06

def row_norm(values):
    return values * lax.rsqrt(lax.optimization_barrier(jnp.mean(values * values, axis=-1, keepdims=True)) + EPS)

def reference(entering_deriv, objective_derivs, content_projection, asker_projection, lookup_projection, softness, window_inputs, digest_inputs, digest_pointer, initial_segment, prior_content_derivs):
    keys_total = (BAND + GLOB) * BLOCK
    group_width = D // N_HEAD
    contents_per_moment = content_projection.reshape(N_SEGMENT, D, D)
    askers_per_moment = asker_projection.reshape(N_SEGMENT, FEAT, D)
    lookups_per_moment = lookup_projection.reshape(N_SEGMENT, FEAT, D)
    inputs_per_moment = window_inputs.reshape(N_SEGMENT, (TICKS + BAND - 1) * BLOCK, FEAT)
    digests_per_moment = digest_pointer.reshape(N_SEGMENT, TICKS, GLOB)
    summary_blocks = digest_inputs.reshape(SUMMARY, BLOCK, FEAT)
    loss_all = objective_derivs.reshape(TICKS - 1, BLOCK, D)
    forwarded_derivs = prior_content_derivs.reshape(N_SEGMENT, TICKS * BLOCK, D).astype(jnp.float32)
    digest_running = jnp.zeros((N_SEGMENT, SUMMARY * BLOCK, D), jnp.float32)
    derivative_array = entering_deriv.reshape(N_SEGMENT, BLOCK, D)
    period_labels = jnp.arange(N_SEGMENT, dtype=jnp.int32)
    row_ids = jnp.arange(BLOCK, dtype=jnp.int32)
    causal = row_ids[None, :] <= row_ids[:, None]
    band_open = jnp.ones((BLOCK, (BAND - 1) * BLOCK), dtype=bool)
    summary_ids = jnp.arange(SUMMARY, dtype=jnp.int32)
    for tick_index in range(TICKS):

        def one_period(bundled):
            period_label, arriving_deriv, loop_state, running_total, content_weights, asker_weights, lookup_weights, attender_scales, temporal_inputs, digest_rows = bundled
            position = initial_segment[0] - period_label - tick_index
            live_count = jnp.minimum(GLOB, 1 + GLOB * position // SEQ_BLOCKS)
            own_rows = temporal_inputs[tick_index * BLOCK:(tick_index + 1) * BLOCK]
            band_rows = temporal_inputs[tick_index * BLOCK:(tick_index + BAND) * BLOCK]
            slot_ids = digest_rows[tick_index]
            glob_rows = summary_blocks[slot_ids].reshape(GLOB * BLOCK, FEAT)
            key_rows = jnp.concatenate([band_rows, glob_rows], axis=0)
            queries = row_norm(jnp.dot(own_rows, asker_weights, preferred_element_type=jnp.float32).reshape(BLOCK, ATTENDER_TOTAL, CHANNEL_WIDTH))
            keyvecs = row_norm(jnp.dot(key_rows, lookup_weights, preferred_element_type=jnp.float32).reshape(keys_total, ATTENDER_TOTAL, CHANNEL_WIDTH))
            affinities = jnp.einsum('ihc,jhc->hij', queries, keyvecs, precision=lax.Precision.HIGHEST)
            affinities = affinities * (attender_scales / CHANNEL_WIDTH)[:, None, None]
            slot_live = jnp.arange(GLOB, dtype=jnp.int32) < live_count
            glob_open = jnp.broadcast_to(jnp.repeat(slot_live, BLOCK)[None, :], (BLOCK, GLOB * BLOCK))
            admitted = jnp.concatenate([causal, band_open, glob_open], axis=1)
            expo = jnp.where(admitted[None], jnp.exp(affinities), 0.0)
            attention = (expo / lax.optimization_barrier(jnp.sum(expo, axis=-1, keepdims=True))).astype(jnp.bfloat16)
            grad_heads = arriving_deriv.astype(jnp.float32).reshape(BLOCK, ATTENDER_TOTAL, CHANNEL_WIDTH)
            contrib = jnp.einsum('hij,ihc->jhc', attention.astype(jnp.float32), grad_heads, precision=lax.Precision.HIGHEST).reshape(keys_total, D)
            own_sum = loop_state[tick_index * BLOCK:(tick_index + 1) * BLOCK] + contrib[:BLOCK]
            for offset in range(1, BAND):
                if tick_index + offset < TICKS:
                    lower = (tick_index + offset) * BLOCK
                    loop_state = loop_state.at[lower:lower + BLOCK].add(contrib[offset * BLOCK:(offset + 1) * BLOCK])
            glob_contrib = contrib[BAND * BLOCK:].reshape(GLOB, BLOCK, D)
            selector = (slot_ids[:, None] == summary_ids[None, :]).astype(jnp.float32)
            running_total = running_total + lax.optimization_barrier(jnp.sum(selector[:, :, None, None] * glob_contrib[:, None], axis=0)).reshape(SUMMARY * BLOCK, D)
            value_grad = own_sum.astype(jnp.bfloat16)
            parts = jnp.einsum('rgc,dgc->grd', value_grad.astype(jnp.float32).reshape(BLOCK, N_HEAD, group_width), content_weights.astype(jnp.float32).reshape(D, N_HEAD, group_width), precision=lax.Precision.HIGHEST)
            parts = parts.astype(jnp.bfloat16)
            grad_out = (arriving_deriv.astype(jnp.float32) + lax.optimization_barrier(jnp.sum(parts.astype(jnp.float32), axis=0))).astype(jnp.bfloat16)
            return (grad_out, loop_state, running_total)
        result_derivs, forwarded_derivs, digest_running = lax.map(one_period, (period_labels, derivative_array, forwarded_derivs, digest_running, contents_per_moment, askers_per_moment, lookups_per_moment, softness, inputs_per_moment, digests_per_moment))
        if tick_index + 1 < TICKS:
            derivative_array = jnp.concatenate([result_derivs[1:], loss_all[tick_index][None]], axis=0)
    outgoing = result_derivs.reshape(N_SEGMENT * BLOCK, D)
    summary_grads = digest_running.astype(jnp.bfloat16).reshape(N_SEGMENT * SUMMARY * BLOCK, D)
    return (outgoing, summary_grads)
```

```python
import jax
import jax.numpy as jnp
from jax import lax
from jax.sharding import PartitionSpec as P

CHANNEL_WIDTH = 128
BAND = 4
GLOB = 2
SUMMARY = 2
SEQ_BLOCKS = 1024
TICKS = 2


EPS = 1e-06


def shifted(value, axis, steps):
    count = lax.axis_size(axis)
    first, last = (max(0, -steps), min(count, count - steps))
    return lax.ppermute(value, axis, [(source, source + steps) for source in range(first, last)])


def row_norm(values):
    return values * lax.rsqrt(jnp.mean(values * values, axis=-1, keepdims=True) + EPS)


def tick_attention(
    tick_index,
    position,
    window_inputs,
    summary_blocks,
    slot_ids,
    asker_projection,
    lookup_projection,
    attender_scales,
):
    block_rows = summary_blocks.shape[1]
    local_width = asker_projection.shape[1]
    heads_local = local_width // CHANNEL_WIDTH
    keys_total = (BAND + GLOB) * block_rows
    own_rows = window_inputs[tick_index * block_rows : (tick_index + 1) * block_rows]
    band_rows = window_inputs[tick_index * block_rows : (tick_index + BAND) * block_rows]
    summary_ids = jnp.arange(SUMMARY, dtype=jnp.int32)
    selector = (slot_ids[:, None] == summary_ids[None, :]).astype(jnp.bfloat16)
    glob_rows = jnp.einsum(
        "gm,mbf->gbf", selector, summary_blocks, preferred_element_type=jnp.float32
    )
    glob_rows = glob_rows.astype(jnp.bfloat16).reshape(GLOB * block_rows, window_inputs.shape[1])
    key_rows = jnp.concatenate([band_rows, glob_rows], axis=0)
    queries = row_norm(
        jnp.dot(own_rows, asker_projection, preferred_element_type=jnp.float32).reshape(
            block_rows, heads_local, CHANNEL_WIDTH
        )
    )
    keyvecs = row_norm(
        jnp.dot(key_rows, lookup_projection, preferred_element_type=jnp.float32).reshape(
            keys_total, heads_local, CHANNEL_WIDTH
        )
    )
    affinities = jnp.einsum("ihc,jhc->hij", queries, keyvecs, precision=lax.Precision.HIGHEST)
    affinities = affinities * (attender_scales / CHANNEL_WIDTH)[:, None, None]
    live_count = jnp.minimum(GLOB, 1 + GLOB * position // SEQ_BLOCKS)
    row_ids = jnp.arange(block_rows, dtype=jnp.int32)
    causal = row_ids[None, :] <= row_ids[:, None]
    band_open = jnp.ones((block_rows, (BAND - 1) * block_rows), dtype=bool)
    slot_live = jnp.arange(GLOB, dtype=jnp.int32) < live_count
    glob_open = jnp.broadcast_to(
        jnp.repeat(slot_live, block_rows)[None, :], (block_rows, GLOB * block_rows)
    )
    admitted = jnp.concatenate([causal, band_open, glob_open], axis=1)
    expo = jnp.where(admitted[None], jnp.exp(affinities), 0.0)
    return (expo / jnp.sum(expo, axis=-1, keepdims=True)).astype(jnp.bfloat16)


def local(
    entering_deriv,
    objective_derivs,
    content_projection,
    asker_projection,
    lookup_projection,
    softness,
    window_inputs,
    digest_inputs,
    digest_pointer,
    initial_segment,
    prior_content_derivs,
):
    period_label = lax.axis_index("segment")
    phases = lax.axis_size("segment")
    head_group = lax.axis_index("head")
    block_rows = entering_deriv.shape[0]
    local_width = content_projection.shape[1]
    heads_local = local_width // CHANNEL_WIDTH
    keys_total = (BAND + GLOB) * block_rows
    summary_blocks = digest_inputs.reshape(SUMMARY, block_rows, digest_inputs.shape[1])
    attender_scales = softness[0]
    forwarded_derivs = prior_content_derivs.astype(jnp.float32)
    digest_running = jnp.zeros((SUMMARY * block_rows, local_width), jnp.float32)
    own_grad = lax.dynamic_slice_in_dim(entering_deriv, head_group * local_width, local_width, 1)
    result = own_grad
    for tick_index in range(TICKS):
        position = initial_segment[0] - period_label - tick_index
        attention = tick_attention(
            tick_index,
            position,
            window_inputs,
            summary_blocks,
            digest_pointer[tick_index],
            asker_projection,
            lookup_projection,
            attender_scales,
        )
        contrib = jnp.einsum(
            "hij,ihc->jhc",
            attention,
            own_grad.reshape(block_rows, heads_local, CHANNEL_WIDTH),
            preferred_element_type=jnp.float32,
        )
        contrib = contrib.reshape(keys_total, local_width)
        own_sum = (
            forwarded_derivs[tick_index * block_rows : (tick_index + 1) * block_rows]
            + contrib[:block_rows]
        )
        for offset in range(1, BAND):
            if tick_index + offset < TICKS:
                lower = (tick_index + offset) * block_rows
                forwarded_derivs = forwarded_derivs.at[lower : lower + block_rows].add(
                    contrib[offset * block_rows : (offset + 1) * block_rows]
                )
        glob_contrib = contrib[BAND * block_rows :].reshape(GLOB, block_rows, local_width)
        selector = (
            digest_pointer[tick_index][:, None] == jnp.arange(SUMMARY, dtype=jnp.int32)[None, :]
        ).astype(jnp.float32)
        digest_running = digest_running + jnp.sum(
            selector[:, :, None, None] * glob_contrib[:, None], axis=0
        ).reshape(SUMMARY * block_rows, local_width)
        value_grad = own_sum.astype(jnp.bfloat16)
        partial_value = lax.dot_general(
            value_grad,
            content_projection,
            (((1,), (1,)), ((), ())),
            preferred_element_type=jnp.float32,
        )
        summed = lax.psum_scatter(
            partial_value.astype(jnp.bfloat16), "head", scatter_dimension=1, tiled=True
        ).astype(jnp.float32)
        result = (own_grad.astype(jnp.float32) + summed).astype(jnp.bfloat16)
        if tick_index + 1 < TICKS:
            fresh_rows = lax.dynamic_slice_in_dim(
                objective_derivs[tick_index * block_rows : (tick_index + 1) * block_rows],
                head_group * local_width,
                local_width,
                1,
            )
            passed = shifted(result, "segment", -1)
            own_grad = jnp.where(period_label == phases - 1, fresh_rows, passed)
    return (result, digest_running.astype(jnp.bfloat16))


def solution(mesh):
    in_specs = (
        P("segment", None),
        P(),
        P("segment", "head"),
        P("segment", "head"),
        P("segment", "head"),
        P("segment", "head"),
        P("segment", None),
        P(),
        P("segment", None),
        P(),
        P("segment", "head"),
    )
    out_specs = (P("segment", "head"), P("segment", "head"))
    return jax.shard_map(local, mesh=mesh, in_specs=in_specs, out_specs=out_specs, check_vma=False)
```

```python
import jax
import jax.numpy as jnp
from jax import lax
from jax.sharding import PartitionSpec as P

CHANNEL_WIDTH = 128
BAND = 4
GLOB = 2
SUMMARY = 2
SEQ_BLOCKS = 1024
TICKS = 2


EPS = 1e-06


def shifted(value, axis, steps):
    count = lax.axis_size(axis)
    first, last = (max(0, -steps), min(count, count - steps))
    return lax.ppermute(value, axis, [(source, source + steps) for source in range(first, last)])


def head_reduce_scatter(partial, block_rows, local_width):
    head_group = lax.axis_index("head")
    heads = lax.axis_size("head")
    groups = heads // 2
    core = head_group % 2
    outer = head_group // 2
    pieces = partial.reshape(block_rows, groups, 2, local_width)
    keep = lax.dynamic_index_in_dim(pieces, core, 2, keepdims=False)
    send = lax.dynamic_index_in_dim(pieces, 1 - core, 2, keepdims=False)
    got = lax.ppermute(send, "head", [(h, h ^ 1) for h in range(heads)])
    halves = keep.astype(jnp.float32) + got.astype(jnp.float32)
    total = lax.dynamic_index_in_dim(halves, outer, 1, keepdims=False)
    for step in range(1, groups):
        target = (outer + step) % groups
        piece = lax.dynamic_index_in_dim(halves, target, 1, keepdims=False).astype(jnp.bfloat16)
        pairs = [(h, (((h // 2) + step) % groups) * 2 + h % 2) for h in range(heads)]
        total = total + lax.ppermute(piece, "head", pairs).astype(jnp.float32)
    return total


def row_norm(values):
    return values * lax.rsqrt(jnp.mean(values * values, axis=-1, keepdims=True) + EPS)


def tick_attention(
    tick_index,
    position,
    window_inputs,
    summary_blocks,
    slot_ids,
    asker_projection,
    lookup_projection,
    attender_scales,
):
    block_rows = summary_blocks.shape[1]
    local_width = asker_projection.shape[1]
    heads_local = local_width // CHANNEL_WIDTH
    keys_total = (BAND + GLOB) * block_rows
    own_rows = window_inputs[tick_index * block_rows : (tick_index + 1) * block_rows]
    band_rows = window_inputs[tick_index * block_rows : (tick_index + BAND) * block_rows]
    summary_ids = jnp.arange(SUMMARY, dtype=jnp.int32)
    selector = (slot_ids[:, None] == summary_ids[None, :]).astype(jnp.bfloat16)
    glob_rows = jnp.einsum(
        "gm,mbf->gbf", selector, summary_blocks, preferred_element_type=jnp.float32
    )
    glob_rows = glob_rows.astype(jnp.bfloat16).reshape(GLOB * block_rows, window_inputs.shape[1])
    key_rows = jnp.concatenate([band_rows, glob_rows], axis=0)
    queries = row_norm(
        jnp.dot(own_rows, asker_projection, preferred_element_type=jnp.float32).reshape(
            block_rows, heads_local, CHANNEL_WIDTH
        )
    )
    keyvecs = row_norm(
        jnp.dot(key_rows, lookup_projection, preferred_element_type=jnp.float32).reshape(
            keys_total, heads_local, CHANNEL_WIDTH
        )
    )
    affinities = jnp.einsum("ihc,jhc->hij", queries, keyvecs, precision=lax.Precision.HIGHEST)
    affinities = affinities * (attender_scales / CHANNEL_WIDTH)[:, None, None]
    live_count = jnp.minimum(GLOB, 1 + GLOB * position // SEQ_BLOCKS)
    row_ids = jnp.arange(block_rows, dtype=jnp.int32)
    causal = row_ids[None, :] <= row_ids[:, None]
    band_open = jnp.ones((block_rows, (BAND - 1) * block_rows), dtype=bool)
    slot_live = jnp.arange(GLOB, dtype=jnp.int32) < live_count
    glob_open = jnp.broadcast_to(
        jnp.repeat(slot_live, block_rows)[None, :], (block_rows, GLOB * block_rows)
    )
    admitted = jnp.concatenate([causal, band_open, glob_open], axis=1)
    expo = jnp.where(admitted[None], jnp.exp(affinities), 0.0)
    return (expo / jnp.sum(expo, axis=-1, keepdims=True)).astype(jnp.bfloat16)


def local(
    entering_deriv,
    objective_derivs,
    content_projection,
    asker_projection,
    lookup_projection,
    softness,
    window_inputs,
    digest_inputs,
    digest_pointer,
    initial_segment,
    prior_content_derivs,
):
    period_label = lax.axis_index("segment")
    phases = lax.axis_size("segment")
    head_group = lax.axis_index("head")
    block_rows = entering_deriv.shape[0]
    local_width = content_projection.shape[1]
    heads_local = local_width // CHANNEL_WIDTH
    keys_total = (BAND + GLOB) * block_rows
    summary_blocks = digest_inputs.reshape(SUMMARY, block_rows, digest_inputs.shape[1])
    attender_scales = softness[0]
    forwarded_derivs = prior_content_derivs.astype(jnp.float32)
    digest_running = jnp.zeros((SUMMARY * block_rows, local_width), jnp.float32)
    own_grad = lax.dynamic_slice_in_dim(entering_deriv, head_group * local_width, local_width, 1)
    result = own_grad
    for tick_index in range(TICKS):
        position = initial_segment[0] - period_label - tick_index
        attention = tick_attention(
            tick_index,
            position,
            window_inputs,
            summary_blocks,
            digest_pointer[tick_index],
            asker_projection,
            lookup_projection,
            attender_scales,
        )
        contrib = jnp.einsum(
            "hij,ihc->jhc",
            attention,
            own_grad.reshape(block_rows, heads_local, CHANNEL_WIDTH),
            preferred_element_type=jnp.float32,
        )
        contrib = contrib.reshape(keys_total, local_width)
        own_sum = (
            forwarded_derivs[tick_index * block_rows : (tick_index + 1) * block_rows]
            + contrib[:block_rows]
        )
        for offset in range(1, BAND):
            if tick_index + offset < TICKS:
                lower = (tick_index + offset) * block_rows
                forwarded_derivs = forwarded_derivs.at[lower : lower + block_rows].add(
                    contrib[offset * block_rows : (offset + 1) * block_rows]
                )
        glob_contrib = contrib[BAND * block_rows :].reshape(GLOB, block_rows, local_width)
        selector = (
            digest_pointer[tick_index][:, None] == jnp.arange(SUMMARY, dtype=jnp.int32)[None, :]
        ).astype(jnp.float32)
        digest_running = digest_running + jnp.sum(
            selector[:, :, None, None] * glob_contrib[:, None], axis=0
        ).reshape(SUMMARY * block_rows, local_width)
        value_grad = own_sum.astype(jnp.bfloat16)
        partial_value = lax.dot_general(
            value_grad,
            content_projection,
            (((1,), (1,)), ((), ())),
            preferred_element_type=jnp.float32,
        )
        summed = head_reduce_scatter(partial_value.astype(jnp.bfloat16), block_rows, local_width)
        result = (own_grad.astype(jnp.float32) + summed).astype(jnp.bfloat16)
        if tick_index + 1 < TICKS:
            fresh_rows = lax.dynamic_slice_in_dim(
                objective_derivs[tick_index * block_rows : (tick_index + 1) * block_rows],
                head_group * local_width,
                local_width,
                1,
            )
            passed = shifted(result, "segment", -1)
            own_grad = jnp.where(period_label == phases - 1, fresh_rows, passed)
    return (result, digest_running.astype(jnp.bfloat16))


def solution(mesh):
    in_specs = (
        P("segment", None),
        P(),
        P("segment", "head"),
        P("segment", "head"),
        P("segment", "head"),
        P("segment", "head"),
        P("segment", None),
        P(),
        P("segment", None),
        P(),
        P("segment", "head"),
    )
    out_specs = (P("segment", "head"), P("segment", "head"))
    return jax.shard_map(local, mesh=mesh, in_specs=in_specs, out_specs=out_specs, check_vma=False)
```

```python
import jax
import jax.numpy as jnp
from jax import lax
from jax.sharding import PartitionSpec as P

CHANNEL_WIDTH = 128
BAND = 4
GLOB = 2
SUMMARY = 2
SEQ_BLOCKS = 1024
TICKS = 2


EPS = 1e-06


def shifted(value, axis, steps):
    count = lax.axis_size(axis)
    first, last = (max(0, -steps), min(count, count - steps))
    return lax.ppermute(value, axis, [(source, source + steps) for source in range(first, last)])


def core_pair_sum(partial):
    head_group = lax.axis_index("head")
    heads = lax.axis_size("head")
    core = head_group % 2
    keep = lax.dynamic_index_in_dim(partial, core, 1, keepdims=False)
    send = lax.dynamic_index_in_dim(partial, 1 - core, 1, keepdims=False)
    got = lax.ppermute(send, "head", [(h, h ^ 1) for h in range(heads)])
    return keep.astype(jnp.float32) + got.astype(jnp.float32)


def across_groups_sum(halves):
    head_group = lax.axis_index("head")
    heads = lax.axis_size("head")
    groups = heads // 2
    outer = head_group // 2
    total = lax.dynamic_index_in_dim(halves, outer, 0, keepdims=False)
    for step in range(1, groups):
        target = (outer + step) % groups
        piece = lax.dynamic_index_in_dim(halves, target, 0, keepdims=False).astype(jnp.bfloat16)
        pairs = [(h, (((h // 2) + step) % groups) * 2 + h % 2) for h in range(heads)]
        total = total + lax.ppermute(piece, "head", pairs).astype(jnp.float32)
    return total


def shift_down_sum(halves, entering):
    head_group = lax.axis_index("head")
    heads = lax.axis_size("head")
    segments = lax.axis_size("segment")
    groups = heads // 2
    outer = head_group // 2
    total = None
    for step in range(groups):
        target = (outer + step) % groups
        piece = lax.dynamic_index_in_dim(halves, target, 0, keepdims=False)
        if step == 0:
            piece = piece + entering
        pairs = []
        for s in range(1, segments):
            for h in range(heads):
                dest = (((h // 2) + step) % groups) * 2 + h % 2
                pairs.append((s * heads + h, (s - 1) * heads + dest))
        got = lax.ppermute(piece.astype(jnp.bfloat16), ("segment", "head"), pairs).astype(jnp.float32)
        total = got if total is None else total + got
    return total


def row_norm(values):
    return values * lax.rsqrt(jnp.mean(values * values, axis=-1, keepdims=True) + EPS)


def tick_attention(
    tick_index,
    position,
    window_inputs,
    summary_blocks,
    slot_ids,
    asker_projection,
    lookup_projection,
    attender_scales,
):
    block_rows = summary_blocks.shape[1]
    local_width = asker_projection.shape[1]
    heads_local = local_width // CHANNEL_WIDTH
    keys_total = (BAND + GLOB) * block_rows
    own_rows = window_inputs[tick_index * block_rows : (tick_index + 1) * block_rows]
    band_rows = window_inputs[tick_index * block_rows : (tick_index + BAND) * block_rows]
    summary_ids = jnp.arange(SUMMARY, dtype=jnp.int32)
    selector = (slot_ids[:, None] == summary_ids[None, :]).astype(jnp.bfloat16)
    glob_rows = jnp.einsum(
        "gm,mbf->gbf", selector, summary_blocks, preferred_element_type=jnp.float32
    )
    glob_rows = glob_rows.astype(jnp.bfloat16).reshape(GLOB * block_rows, window_inputs.shape[1])
    key_rows = jnp.concatenate([band_rows, glob_rows], axis=0)
    queries = row_norm(
        jnp.dot(own_rows, asker_projection, preferred_element_type=jnp.float32).reshape(
            block_rows, heads_local, CHANNEL_WIDTH
        )
    )
    keyvecs = row_norm(
        jnp.dot(key_rows, lookup_projection, preferred_element_type=jnp.float32).reshape(
            keys_total, heads_local, CHANNEL_WIDTH
        )
    )
    affinities = jnp.einsum("ihc,jhc->hij", queries, keyvecs, precision=lax.Precision.HIGHEST)
    affinities = affinities * (attender_scales / CHANNEL_WIDTH)[:, None, None]
    live_count = jnp.minimum(GLOB, 1 + GLOB * position // SEQ_BLOCKS)
    row_ids = jnp.arange(block_rows, dtype=jnp.int32)
    causal = row_ids[None, :] <= row_ids[:, None]
    band_open = jnp.ones((block_rows, (BAND - 1) * block_rows), dtype=bool)
    slot_live = jnp.arange(GLOB, dtype=jnp.int32) < live_count
    glob_open = jnp.broadcast_to(
        jnp.repeat(slot_live, block_rows)[None, :], (block_rows, GLOB * block_rows)
    )
    admitted = jnp.concatenate([causal, band_open, glob_open], axis=1)
    expo = jnp.where(admitted[None], jnp.exp(affinities), 0.0)
    return (expo / jnp.sum(expo, axis=-1, keepdims=True)).astype(jnp.bfloat16)


def local(
    entering_deriv,
    objective_derivs,
    content_projection,
    asker_projection,
    lookup_projection,
    softness,
    window_inputs,
    digest_inputs,
    digest_pointer,
    initial_segment,
    prior_content_derivs,
):
    period_label = lax.axis_index("segment")
    phases = lax.axis_size("segment")
    head_group = lax.axis_index("head")
    heads = lax.axis_size("head")
    groups = heads // 2
    block_rows = entering_deriv.shape[0]
    local_width = content_projection.shape[1]
    heads_local = local_width // CHANNEL_WIDTH
    keys_total = (BAND + GLOB) * block_rows
    summary_blocks = digest_inputs.reshape(SUMMARY, block_rows, digest_inputs.shape[1])
    attender_scales = softness[0]
    weights = content_projection.reshape(groups, 2, local_width, local_width)
    forwarded_derivs = prior_content_derivs.astype(jnp.float32)
    digest_running = jnp.zeros((SUMMARY * block_rows, local_width), jnp.float32)
    own_grad = lax.dynamic_slice_in_dim(entering_deriv, head_group * local_width, local_width, 1)
    feats = (window_inputs, asker_projection, lookup_projection)
    result = own_grad
    for tick_index in range(TICKS):
        position = initial_segment[0] - period_label - tick_index
        attention = tick_attention(
            tick_index,
            position,
            feats[0],
            summary_blocks,
            digest_pointer[tick_index],
            feats[1],
            feats[2],
            attender_scales,
        )
        contrib = jnp.einsum(
            "hij,ihc->jhc",
            attention,
            own_grad.reshape(block_rows, heads_local, CHANNEL_WIDTH),
            preferred_element_type=jnp.float32,
        )
        contrib = contrib.reshape(keys_total, local_width)
        own_sum = (
            forwarded_derivs[tick_index * block_rows : (tick_index + 1) * block_rows]
            + contrib[:block_rows]
        )
        for offset in range(1, BAND):
            if tick_index + offset < TICKS:
                lower = (tick_index + offset) * block_rows
                forwarded_derivs = forwarded_derivs.at[lower : lower + block_rows].add(
                    contrib[offset * block_rows : (offset + 1) * block_rows]
                )
        glob_contrib = contrib[BAND * block_rows :].reshape(GLOB, block_rows, local_width)
        selector = (
            digest_pointer[tick_index][:, None] == jnp.arange(SUMMARY, dtype=jnp.int32)[None, :]
        ).astype(jnp.float32)
        digest_running = digest_running + jnp.sum(
            selector[:, :, None, None] * glob_contrib[:, None], axis=0
        ).reshape(SUMMARY * block_rows, local_width)
        value_grad = own_sum.astype(jnp.bfloat16)
        partial_value = jnp.einsum(
            "rk,gpdk->gprd", value_grad, weights, preferred_element_type=jnp.float32
        ).astype(jnp.bfloat16)
        if tick_index + 1 < TICKS:
            partial_value, feats = lax.optimization_barrier((partial_value, feats))
            halves = core_pair_sum(partial_value)
            fresh_rows = lax.dynamic_slice_in_dim(
                objective_derivs[tick_index * block_rows : (tick_index + 1) * block_rows],
                head_group * local_width,
                local_width,
                1,
            )
            passed = shift_down_sum(halves, own_grad.astype(jnp.float32)).astype(jnp.bfloat16)
            own_grad = jnp.where(period_label == phases - 1, fresh_rows, passed)
        else:
            summed = across_groups_sum(core_pair_sum(partial_value))
            result = (own_grad.astype(jnp.float32) + summed).astype(jnp.bfloat16)
    return (result, digest_running.astype(jnp.bfloat16))


def solution(mesh):
    in_specs = (
        P("segment", None),
        P(),
        P("segment", "head"),
        P("segment", "head"),
        P("segment", "head"),
        P("segment", "head"),
        P("segment", None),
        P(),
        P("segment", None),
        P(),
        P("segment", "head"),
    )
    out_specs = (P("segment", "head"), P("segment", "head"))
    return jax.shard_map(local, mesh=mesh, in_specs=in_specs, out_specs=out_specs, check_vma=False)
```

```python
import jax
import jax.numpy as jnp
from jax import lax
from jax.sharding import PartitionSpec as P
from jax.experimental import pallas as pl
from jax.experimental.pallas import tpu as pltpu
import functools

CHANNEL_WIDTH = 128
BAND = 4
GLOB = 2
SUMMARY = 2
SEQ_BLOCKS = 1024
TICKS = 2


EPS = 1e-06


def shifted(value, axis, steps):
    count = lax.axis_size(axis)
    first, last = (max(0, -steps), min(count, count - steps))
    return lax.ppermute(value, axis, [(source, source + steps) for source in range(first, last)])


def core_pair_sum(partial):
    head_group = lax.axis_index("head")
    heads = lax.axis_size("head")
    core = head_group % 2
    keep = lax.dynamic_index_in_dim(partial, core, 1, keepdims=False)
    send = lax.dynamic_index_in_dim(partial, 1 - core, 1, keepdims=False)
    got = lax.ppermute(send, "head", [(h, h ^ 1) for h in range(heads)])
    return keep.astype(jnp.float32) + got.astype(jnp.float32)


def across_groups_sum(halves):
    head_group = lax.axis_index("head")
    heads = lax.axis_size("head")
    groups = heads // 2
    outer = head_group // 2
    total = lax.dynamic_index_in_dim(halves, outer, 0, keepdims=False)
    for step in range(1, groups):
        target = (outer + step) % groups
        piece = lax.dynamic_index_in_dim(halves, target, 0, keepdims=False).astype(jnp.bfloat16)
        pairs = [(h, (((h // 2) + step) % groups) * 2 + h % 2) for h in range(heads)]
        total = total + lax.ppermute(piece, "head", pairs).astype(jnp.float32)
    return total


def shift_down_sum(halves, entering):
    head_group = lax.axis_index("head")
    heads = lax.axis_size("head")
    segments = lax.axis_size("segment")
    groups = heads // 2
    outer = head_group // 2
    total = None
    for step in range(groups):
        target = (outer + step) % groups
        piece = lax.dynamic_index_in_dim(halves, target, 0, keepdims=False)
        if step == 0:
            piece = piece + entering
        pairs = []
        for s in range(1, segments):
            for h in range(heads):
                dest = (((h // 2) + step) % groups) * 2 + h % 2
                pairs.append((s * heads + h, (s - 1) * heads + dest))
        got = lax.ppermute(piece.astype(jnp.bfloat16), ("segment", "head"), pairs).astype(jnp.float32)
        total = got if total is None else total + got
    return total


def row_norm(values):
    return values * lax.rsqrt(jnp.mean(values * values, axis=-1, keepdims=True) + EPS)


def _attention_kernel(meta_ref, scale_ref, win_ref, summ_ref, ask_ref, look_ref, grad_ref, out_ref, *, tick, heads_local, block):
    live = meta_ref[0]
    band_rows = BAND * block
    own = win_ref[tick * block : (tick + 1) * block, :]
    band = win_ref[tick * block : tick * block + band_rows, :]
    queries = jnp.dot(own, ask_ref[...], preferred_element_type=jnp.float32)
    band_keys = jnp.dot(band, look_ref[...], preferred_element_type=jnp.float32)
    glob_keys = [
        jnp.dot(summ_ref[meta_ref[1 + g]], look_ref[...], preferred_element_type=jnp.float32)
        for g in range(GLOB)
    ]
    key_ids = lax.broadcasted_iota(jnp.int32, (band_rows, block), 0)
    query_ids = lax.broadcasted_iota(jnp.int32, (band_rows, block), 1)
    band_open = (key_ids >= block) | (key_ids <= query_ids)
    live_vec = jnp.zeros((block, block), jnp.int32) + live
    contract = (((1,), (1,)), ((), ()))
    for h in range(heads_local):
        cols = slice(h * CHANNEL_WIDTH, (h + 1) * CHANNEL_WIDTH)
        scale = scale_ref[h]
        qh = row_norm(queries[:, cols])
        kb = row_norm(band_keys[:, cols])
        sb = lax.dot_general(kb, qh, contract, precision=lax.Precision.HIGHEST, preferred_element_type=jnp.float32) * scale
        eb = jnp.where(band_open, jnp.exp(sb), 0.0)
        denom = jnp.sum(eb, axis=0, keepdims=True)
        eg = []
        for g in range(GLOB):
            kg = row_norm(glob_keys[g][:, cols])
            sg = lax.dot_general(kg, qh, contract, precision=lax.Precision.HIGHEST, preferred_element_type=jnp.float32) * scale
            e = jnp.where(live_vec > g, jnp.exp(sg), 0.0)
            denom = denom + jnp.sum(e, axis=0, keepdims=True)
            eg.append(e)
        gh = grad_ref[:, cols]
        ab = (eb / denom).astype(jnp.bfloat16)
        out_ref[0:band_rows, cols] = jnp.dot(ab, gh, preferred_element_type=jnp.float32)
        for g in range(GLOB):
            ag = (eg[g] / denom).astype(jnp.bfloat16)
            lo = band_rows + g * block
            out_ref[lo : lo + block, cols] = jnp.dot(ag, gh, preferred_element_type=jnp.float32)


def attention_contrib(tick, meta, scales, window_inputs, summary_blocks, asker, lookup, grad):
    block = grad.shape[0]
    local_width = grad.shape[1]
    heads_local = local_width // CHANNEL_WIDTH
    keys_total = (BAND + GLOB) * block
    feat = window_inputs.shape[1]
    flops = 2 * feat * local_width * (block + keys_total) + 2 * 6 * keys_total * block * local_width + 2 * keys_total * block * local_width
    vmem = pl.BlockSpec(memory_space=pltpu.VMEM)
    smem = pl.BlockSpec(memory_space=pltpu.SMEM)
    return pl.pallas_call(
        functools.partial(_attention_kernel, tick=tick, heads_local=heads_local, block=block),
        out_shape=jax.ShapeDtypeStruct((keys_total, local_width), jnp.float32),
        in_specs=[smem, smem, vmem, vmem, vmem, vmem, vmem],
        out_specs=vmem,
        cost_estimate=pl.CostEstimate(flops=flops, transcendentals=keys_total * block * heads_local, bytes_accessed=keys_total * local_width * 4 + 4 * feat * local_width * 2),
    )(meta, scales, window_inputs, summary_blocks, asker, lookup, grad)


def tick_attention(
    tick_index,
    position,
    window_inputs,
    summary_blocks,
    slot_ids,
    asker_projection,
    lookup_projection,
    attender_scales,
):
    block_rows = summary_blocks.shape[1]
    local_width = asker_projection.shape[1]
    heads_local = local_width // CHANNEL_WIDTH
    keys_total = (BAND + GLOB) * block_rows
    own_rows = window_inputs[tick_index * block_rows : (tick_index + 1) * block_rows]
    band_rows = window_inputs[tick_index * block_rows : (tick_index + BAND) * block_rows]
    summary_ids = jnp.arange(SUMMARY, dtype=jnp.int32)
    selector = (slot_ids[:, None] == summary_ids[None, :]).astype(jnp.bfloat16)
    glob_rows = jnp.einsum(
        "gm,mbf->gbf", selector, summary_blocks, preferred_element_type=jnp.float32
    )
    glob_rows = glob_rows.astype(jnp.bfloat16).reshape(GLOB * block_rows, window_inputs.shape[1])
    key_rows = jnp.concatenate([band_rows, glob_rows], axis=0)
    queries = row_norm(
        jnp.dot(own_rows, asker_projection, preferred_element_type=jnp.float32).reshape(
            block_rows, heads_local, CHANNEL_WIDTH
        )
    )
    keyvecs = row_norm(
        jnp.dot(key_rows, lookup_projection, preferred_element_type=jnp.float32).reshape(
            keys_total, heads_local, CHANNEL_WIDTH
        )
    )
    affinities = jnp.einsum("ihc,jhc->hij", queries, keyvecs, precision=lax.Precision.HIGHEST)
    affinities = affinities * (attender_scales / CHANNEL_WIDTH)[:, None, None]
    live_count = jnp.minimum(GLOB, 1 + GLOB * position // SEQ_BLOCKS)
    row_ids = jnp.arange(block_rows, dtype=jnp.int32)
    causal = row_ids[None, :] <= row_ids[:, None]
    band_open = jnp.ones((block_rows, (BAND - 1) * block_rows), dtype=bool)
    slot_live = jnp.arange(GLOB, dtype=jnp.int32) < live_count
    glob_open = jnp.broadcast_to(
        jnp.repeat(slot_live, block_rows)[None, :], (block_rows, GLOB * block_rows)
    )
    admitted = jnp.concatenate([causal, band_open, glob_open], axis=1)
    expo = jnp.where(admitted[None], jnp.exp(affinities), 0.0)
    return (expo / jnp.sum(expo, axis=-1, keepdims=True)).astype(jnp.bfloat16)


def local(
    entering_deriv,
    objective_derivs,
    content_projection,
    asker_projection,
    lookup_projection,
    softness,
    window_inputs,
    digest_inputs,
    digest_pointer,
    initial_segment,
    prior_content_derivs,
):
    period_label = lax.axis_index("segment")
    phases = lax.axis_size("segment")
    head_group = lax.axis_index("head")
    heads = lax.axis_size("head")
    groups = heads // 2
    block_rows = entering_deriv.shape[0]
    local_width = content_projection.shape[1]
    heads_local = local_width // CHANNEL_WIDTH
    keys_total = (BAND + GLOB) * block_rows
    summary_blocks = digest_inputs.reshape(SUMMARY, block_rows, digest_inputs.shape[1])
    attender_scales = softness[0]
    weights = content_projection.reshape(groups, 2, local_width, local_width)
    forwarded_derivs = prior_content_derivs.astype(jnp.float32)
    digest_running = jnp.zeros((SUMMARY * block_rows, local_width), jnp.float32)
    own_grad = lax.dynamic_slice_in_dim(entering_deriv, head_group * local_width, local_width, 1)
    feats = (window_inputs, asker_projection, lookup_projection)
    result = own_grad
    for tick_index in range(TICKS):
        position = initial_segment[0] - period_label - tick_index
        live_count = jnp.minimum(GLOB, 1 + GLOB * position // SEQ_BLOCKS)
        meta = jnp.concatenate([live_count[None], digest_pointer[tick_index]]).astype(jnp.int32)
        contrib = attention_contrib(
            tick_index, meta, attender_scales / CHANNEL_WIDTH, feats[0], summary_blocks, feats[1], feats[2], own_grad
        )
        own_sum = (
            forwarded_derivs[tick_index * block_rows : (tick_index + 1) * block_rows]
            + contrib[:block_rows]
        )
        for offset in range(1, BAND):
            if tick_index + offset < TICKS:
                lower = (tick_index + offset) * block_rows
                forwarded_derivs = forwarded_derivs.at[lower : lower + block_rows].add(
                    contrib[offset * block_rows : (offset + 1) * block_rows]
                )
        glob_contrib = contrib[BAND * block_rows :].reshape(GLOB, block_rows, local_width)
        selector = (
            digest_pointer[tick_index][:, None] == jnp.arange(SUMMARY, dtype=jnp.int32)[None, :]
        ).astype(jnp.float32)
        digest_running = digest_running + jnp.sum(
            selector[:, :, None, None] * glob_contrib[:, None], axis=0
        ).reshape(SUMMARY * block_rows, local_width)
        value_grad = own_sum.astype(jnp.bfloat16)
        partial_value = jnp.einsum(
            "rk,gpdk->gprd", value_grad, weights, preferred_element_type=jnp.float32
        ).astype(jnp.bfloat16)
        if tick_index + 1 < TICKS:
            partial_value, feats = lax.optimization_barrier((partial_value, feats))
            halves = core_pair_sum(partial_value)
            fresh_rows = lax.dynamic_slice_in_dim(
                objective_derivs[tick_index * block_rows : (tick_index + 1) * block_rows],
                head_group * local_width,
                local_width,
                1,
            )
            passed = shift_down_sum(halves, own_grad.astype(jnp.float32)).astype(jnp.bfloat16)
            own_grad = jnp.where(period_label == phases - 1, fresh_rows, passed)
        else:
            summed = across_groups_sum(core_pair_sum(partial_value))
            result = (own_grad.astype(jnp.float32) + summed).astype(jnp.bfloat16)
    return (result, digest_running.astype(jnp.bfloat16))


def solution(mesh):
    in_specs = (
        P("segment", None),
        P(),
        P("segment", "head"),
        P("segment", "head"),
        P("segment", "head"),
        P("segment", "head"),
        P("segment", None),
        P(),
        P("segment", None),
        P(),
        P("segment", "head"),
    )
    out_specs = (P("segment", "head"), P("segment", "head"))
    return jax.shard_map(local, mesh=mesh, in_specs=in_specs, out_specs=out_specs, check_vma=False)
```

```python
import jax
import jax.numpy as jnp
from jax import lax
from jax.sharding import PartitionSpec as P
from jax.experimental import pallas as pl
from jax.experimental.pallas import tpu as pltpu
import functools

CHANNEL_WIDTH = 128
BAND = 4
GLOB = 2
SUMMARY = 2
SEQ_BLOCKS = 1024
TICKS = 2


EPS = 1e-06


def shifted(value, axis, steps):
    count = lax.axis_size(axis)
    first, last = (max(0, -steps), min(count, count - steps))
    return lax.ppermute(value, axis, [(source, source + steps) for source in range(first, last)])


def core_pair_sum(partial):
    head_group = lax.axis_index("head")
    heads = lax.axis_size("head")
    core = head_group % 2
    keep = lax.dynamic_index_in_dim(partial, core, 1, keepdims=False)
    send = lax.dynamic_index_in_dim(partial, 1 - core, 1, keepdims=False)
    got = lax.ppermute(send, "head", [(h, h ^ 1) for h in range(heads)])
    return keep.astype(jnp.float32) + got.astype(jnp.float32)


def across_groups_sum(halves):
    head_group = lax.axis_index("head")
    heads = lax.axis_size("head")
    groups = heads // 2
    outer = head_group // 2
    total = lax.dynamic_index_in_dim(halves, outer, 0, keepdims=False)
    for step in range(1, groups):
        target = (outer + step) % groups
        piece = lax.dynamic_index_in_dim(halves, target, 0, keepdims=False).astype(jnp.bfloat16)
        pairs = [(h, (((h // 2) + step) % groups) * 2 + h % 2) for h in range(heads)]
        total = total + lax.ppermute(piece, "head", pairs).astype(jnp.float32)
    return total


def shift_down_sum(halves, entering):
    head_group = lax.axis_index("head")
    heads = lax.axis_size("head")
    segments = lax.axis_size("segment")
    groups = heads // 2
    outer = head_group // 2
    total = None
    for step in range(groups):
        target = (outer + step) % groups
        piece = lax.dynamic_index_in_dim(halves, target, 0, keepdims=False)
        if step == 0:
            piece = piece + entering
        pairs = []
        for s in range(1, segments):
            for h in range(heads):
                dest = (((h // 2) + step) % groups) * 2 + h % 2
                pairs.append((s * heads + h, (s - 1) * heads + dest))
        got = lax.ppermute(piece.astype(jnp.bfloat16), ("segment", "head"), pairs).astype(jnp.float32)
        total = got if total is None else total + got
    return total


def row_norm(values):
    return values * lax.rsqrt(jnp.mean(values * values, axis=-1, keepdims=True) + EPS)


def _attention_weights(meta_ref, scale_ref, win_ref, summ_ref, ask_ref, look_ref, *, tick, heads_local, block):
    live = meta_ref[0]
    band_rows = BAND * block
    own = win_ref[tick * block : (tick + 1) * block, :]
    band = win_ref[tick * block : tick * block + band_rows, :]
    queries = jnp.dot(own, ask_ref[...], preferred_element_type=jnp.float32)
    band_keys = jnp.dot(band, look_ref[...], preferred_element_type=jnp.float32)
    glob_keys = [
        jnp.dot(summ_ref[meta_ref[1 + g]], look_ref[...], preferred_element_type=jnp.float32)
        for g in range(GLOB)
    ]
    key_ids = lax.broadcasted_iota(jnp.int32, (band_rows, block), 0)
    query_ids = lax.broadcasted_iota(jnp.int32, (band_rows, block), 1)
    band_open = (key_ids >= block) | (key_ids <= query_ids)
    live_vec = jnp.zeros((block, block), jnp.int32) + live
    contract = (((1,), (1,)), ((), ()))
    for h in range(heads_local):
        cols = slice(h * CHANNEL_WIDTH, (h + 1) * CHANNEL_WIDTH)
        scale = scale_ref[h]
        qh = row_norm(queries[:, cols])
        kb = row_norm(band_keys[:, cols])
        sb = lax.dot_general(kb, qh, contract, precision=lax.Precision.HIGHEST, preferred_element_type=jnp.float32) * scale
        eb = jnp.where(band_open, jnp.exp(sb), 0.0)
        denom = jnp.sum(eb, axis=0, keepdims=True)
        eg = []
        for g in range(GLOB):
            kg = row_norm(glob_keys[g][:, cols])
            sg = lax.dot_general(kg, qh, contract, precision=lax.Precision.HIGHEST, preferred_element_type=jnp.float32) * scale
            e = jnp.where(live_vec > g, jnp.exp(sg), 0.0)
            denom = denom + jnp.sum(e, axis=0, keepdims=True)
            eg.append(e)
        yield h, (eb / denom).astype(jnp.bfloat16), [(e / denom).astype(jnp.bfloat16) for e in eg]


def _attention_kernel(meta_ref, scale_ref, win_ref, summ_ref, ask_ref, look_ref, grad_ref, out_ref, *, tick, heads_local, block):
    band_rows = BAND * block
    for h, ab, ags in _attention_weights(
        meta_ref, scale_ref, win_ref, summ_ref, ask_ref, look_ref, tick=tick, heads_local=heads_local, block=block
    ):
        cols = slice(h * CHANNEL_WIDTH, (h + 1) * CHANNEL_WIDTH)
        gh = grad_ref[:, cols]
        out_ref[0:band_rows, cols] = jnp.dot(ab, gh, preferred_element_type=jnp.float32)
        for g, ag in enumerate(ags):
            lo = band_rows + g * block
            out_ref[lo : lo + block, cols] = jnp.dot(ag, gh, preferred_element_type=jnp.float32)


def _weights_kernel(meta_ref, scale_ref, win_ref, summ_ref, ask_ref, look_ref, out_ref, *, tick, heads_local, block):
    band_rows = BAND * block
    for h, ab, ags in _attention_weights(
        meta_ref, scale_ref, win_ref, summ_ref, ask_ref, look_ref, tick=tick, heads_local=heads_local, block=block
    ):
        out_ref[h, 0:band_rows, :] = ab
        for g, ag in enumerate(ags):
            lo = band_rows + g * block
            out_ref[h, lo : lo + block, :] = ag


def _contrib_kernel(att_ref, grad_ref, out_ref, *, heads_local):
    for h in range(heads_local):
        cols = slice(h * CHANNEL_WIDTH, (h + 1) * CHANNEL_WIDTH)
        out_ref[:, cols] = jnp.dot(att_ref[h], grad_ref[:, cols], preferred_element_type=jnp.float32)


def attention_weights(tick, meta, scales, window_inputs, summary_blocks, asker, lookup):
    block = summary_blocks.shape[1]
    local_width = asker.shape[1]
    heads_local = local_width // CHANNEL_WIDTH
    keys_total = (BAND + GLOB) * block
    feat = window_inputs.shape[1]
    flops = 2 * feat * local_width * (block + keys_total) + 2 * 6 * keys_total * block * local_width
    vmem = pl.BlockSpec(memory_space=pltpu.VMEM)
    smem = pl.BlockSpec(memory_space=pltpu.SMEM)
    return pl.pallas_call(
        functools.partial(_weights_kernel, tick=tick, heads_local=heads_local, block=block),
        out_shape=jax.ShapeDtypeStruct((heads_local, keys_total, block), jnp.bfloat16),
        in_specs=[smem, smem, vmem, vmem, vmem, vmem],
        out_specs=vmem,
        cost_estimate=pl.CostEstimate(flops=flops, transcendentals=keys_total * block * heads_local, bytes_accessed=keys_total * local_width * 2 + 4 * feat * local_width * 2),
    )(meta, scales, window_inputs, summary_blocks, asker, lookup)


def contrib_from(att, grad):
    heads_local, keys_total, block = att.shape
    local_width = grad.shape[1]
    vmem = pl.BlockSpec(memory_space=pltpu.VMEM)
    return pl.pallas_call(
        functools.partial(_contrib_kernel, heads_local=heads_local),
        out_shape=jax.ShapeDtypeStruct((keys_total, local_width), jnp.float32),
        in_specs=[vmem, vmem],
        out_specs=vmem,
        cost_estimate=pl.CostEstimate(flops=2 * keys_total * block * local_width, transcendentals=0, bytes_accessed=keys_total * local_width * 6),
    )(att, grad)


def attention_contrib(tick, meta, scales, window_inputs, summary_blocks, asker, lookup, grad):
    block = grad.shape[0]
    local_width = grad.shape[1]
    heads_local = local_width // CHANNEL_WIDTH
    keys_total = (BAND + GLOB) * block
    feat = window_inputs.shape[1]
    flops = 2 * feat * local_width * (block + keys_total) + 2 * 6 * keys_total * block * local_width + 2 * keys_total * block * local_width
    vmem = pl.BlockSpec(memory_space=pltpu.VMEM)
    smem = pl.BlockSpec(memory_space=pltpu.SMEM)
    return pl.pallas_call(
        functools.partial(_attention_kernel, tick=tick, heads_local=heads_local, block=block),
        out_shape=jax.ShapeDtypeStruct((keys_total, local_width), jnp.float32),
        in_specs=[smem, smem, vmem, vmem, vmem, vmem, vmem],
        out_specs=vmem,
        cost_estimate=pl.CostEstimate(flops=flops, transcendentals=keys_total * block * heads_local, bytes_accessed=keys_total * local_width * 4 + 4 * feat * local_width * 2),
    )(meta, scales, window_inputs, summary_blocks, asker, lookup, grad)


def tick_attention(
    tick_index,
    position,
    window_inputs,
    summary_blocks,
    slot_ids,
    asker_projection,
    lookup_projection,
    attender_scales,
):
    block_rows = summary_blocks.shape[1]
    local_width = asker_projection.shape[1]
    heads_local = local_width // CHANNEL_WIDTH
    keys_total = (BAND + GLOB) * block_rows
    own_rows = window_inputs[tick_index * block_rows : (tick_index + 1) * block_rows]
    band_rows = window_inputs[tick_index * block_rows : (tick_index + BAND) * block_rows]
    summary_ids = jnp.arange(SUMMARY, dtype=jnp.int32)
    selector = (slot_ids[:, None] == summary_ids[None, :]).astype(jnp.bfloat16)
    glob_rows = jnp.einsum(
        "gm,mbf->gbf", selector, summary_blocks, preferred_element_type=jnp.float32
    )
    glob_rows = glob_rows.astype(jnp.bfloat16).reshape(GLOB * block_rows, window_inputs.shape[1])
    key_rows = jnp.concatenate([band_rows, glob_rows], axis=0)
    queries = row_norm(
        jnp.dot(own_rows, asker_projection, preferred_element_type=jnp.float32).reshape(
            block_rows, heads_local, CHANNEL_WIDTH
        )
    )
    keyvecs = row_norm(
        jnp.dot(key_rows, lookup_projection, preferred_element_type=jnp.float32).reshape(
            keys_total, heads_local, CHANNEL_WIDTH
        )
    )
    affinities = jnp.einsum("ihc,jhc->hij", queries, keyvecs, precision=lax.Precision.HIGHEST)
    affinities = affinities * (attender_scales / CHANNEL_WIDTH)[:, None, None]
    live_count = jnp.minimum(GLOB, 1 + GLOB * position // SEQ_BLOCKS)
    row_ids = jnp.arange(block_rows, dtype=jnp.int32)
    causal = row_ids[None, :] <= row_ids[:, None]
    band_open = jnp.ones((block_rows, (BAND - 1) * block_rows), dtype=bool)
    slot_live = jnp.arange(GLOB, dtype=jnp.int32) < live_count
    glob_open = jnp.broadcast_to(
        jnp.repeat(slot_live, block_rows)[None, :], (block_rows, GLOB * block_rows)
    )
    admitted = jnp.concatenate([causal, band_open, glob_open], axis=1)
    expo = jnp.where(admitted[None], jnp.exp(affinities), 0.0)
    return (expo / jnp.sum(expo, axis=-1, keepdims=True)).astype(jnp.bfloat16)


def local(
    entering_deriv,
    objective_derivs,
    content_projection,
    asker_projection,
    lookup_projection,
    softness,
    window_inputs,
    digest_inputs,
    digest_pointer,
    initial_segment,
    prior_content_derivs,
):
    period_label = lax.axis_index("segment")
    phases = lax.axis_size("segment")
    head_group = lax.axis_index("head")
    heads = lax.axis_size("head")
    groups = heads // 2
    block_rows = entering_deriv.shape[0]
    local_width = content_projection.shape[1]
    heads_local = local_width // CHANNEL_WIDTH
    keys_total = (BAND + GLOB) * block_rows
    summary_blocks = digest_inputs.reshape(SUMMARY, block_rows, digest_inputs.shape[1])
    attender_scales = softness[0]
    weights = content_projection.reshape(groups, 2, local_width, local_width)
    forwarded_derivs = prior_content_derivs.astype(jnp.float32)
    digest_running = jnp.zeros((SUMMARY * block_rows, local_width), jnp.float32)
    own_grad = lax.dynamic_slice_in_dim(entering_deriv, head_group * local_width, local_width, 1)
    feats = (window_inputs, asker_projection, lookup_projection)
    result = own_grad
    for tick_index in range(TICKS):
        position = initial_segment[0] - period_label - tick_index
        live_count = jnp.minimum(GLOB, 1 + GLOB * position // SEQ_BLOCKS)
        meta = jnp.concatenate([live_count[None], digest_pointer[tick_index]]).astype(jnp.int32)
        if tick_index == 0:
            contrib = attention_contrib(
                tick_index, meta, attender_scales / CHANNEL_WIDTH, feats[0], summary_blocks, feats[1], feats[2], own_grad
            )
        else:
            contrib = contrib_from(later_att, own_grad)
        own_sum = (
            forwarded_derivs[tick_index * block_rows : (tick_index + 1) * block_rows]
            + contrib[:block_rows]
        )
        for offset in range(1, BAND):
            if tick_index + offset < TICKS:
                lower = (tick_index + offset) * block_rows
                forwarded_derivs = forwarded_derivs.at[lower : lower + block_rows].add(
                    contrib[offset * block_rows : (offset + 1) * block_rows]
                )
        glob_contrib = contrib[BAND * block_rows :].reshape(GLOB, block_rows, local_width)
        selector = (
            digest_pointer[tick_index][:, None] == jnp.arange(SUMMARY, dtype=jnp.int32)[None, :]
        ).astype(jnp.float32)
        digest_running = digest_running + jnp.sum(
            selector[:, :, None, None] * glob_contrib[:, None], axis=0
        ).reshape(SUMMARY * block_rows, local_width)
        value_grad = own_sum.astype(jnp.bfloat16)
        partial_value = jnp.einsum(
            "rk,gpdk->gprd", value_grad, weights, preferred_element_type=jnp.float32
        ).astype(jnp.bfloat16)
        if tick_index + 1 < TICKS:
            partial_value, feats = lax.optimization_barrier((partial_value, feats))
            later_position = initial_segment[0] - period_label - (tick_index + 1)
            later_live = jnp.minimum(GLOB, 1 + GLOB * later_position // SEQ_BLOCKS)
            later_meta = jnp.concatenate([later_live[None], digest_pointer[tick_index + 1]]).astype(jnp.int32)
            later_att = attention_weights(
                tick_index + 1, later_meta, attender_scales / CHANNEL_WIDTH, feats[0], summary_blocks, feats[1], feats[2]
            )
            halves = core_pair_sum(partial_value)
            fresh_rows = lax.dynamic_slice_in_dim(
                objective_derivs[tick_index * block_rows : (tick_index + 1) * block_rows],
                head_group * local_width,
                local_width,
                1,
            )
            passed = shift_down_sum(halves, own_grad.astype(jnp.float32)).astype(jnp.bfloat16)
            own_grad = jnp.where(period_label == phases - 1, fresh_rows, passed)
        else:
            summed = across_groups_sum(core_pair_sum(partial_value))
            result = (own_grad.astype(jnp.float32) + summed).astype(jnp.bfloat16)
    return (result, digest_running.astype(jnp.bfloat16))


def solution(mesh):
    in_specs = (
        P("segment", None),
        P(),
        P("segment", "head"),
        P("segment", "head"),
        P("segment", "head"),
        P("segment", "head"),
        P("segment", None),
        P(),
        P("segment", None),
        P(),
        P("segment", "head"),
    )
    out_specs = (P("segment", "head"), P("segment", "head"))
    return jax.shard_map(local, mesh=mesh, in_specs=in_specs, out_specs=out_specs, check_vma=False)
```

```python
import jax
import jax.numpy as jnp
from jax import lax
from jax.sharding import PartitionSpec as P
from jax.experimental import pallas as pl
from jax.experimental.pallas import tpu as pltpu
import functools

CHANNEL_WIDTH = 128
BAND = 4
GLOB = 2
SUMMARY = 2
SEQ_BLOCKS = 1024
TICKS = 2


EPS = 1e-06


def shifted(value, axis, steps):
    count = lax.axis_size(axis)
    first, last = (max(0, -steps), min(count, count - steps))
    return lax.ppermute(value, axis, [(source, source + steps) for source in range(first, last)])


def core_pair_sum(partial):
    head_group = lax.axis_index("head")
    heads = lax.axis_size("head")
    core = head_group % 2
    keep = lax.dynamic_index_in_dim(partial, core, 1, keepdims=False)
    send = lax.dynamic_index_in_dim(partial, 1 - core, 1, keepdims=False)
    got = lax.ppermute(send, "head", [(h, h ^ 1) for h in range(heads)])
    return keep.astype(jnp.float32) + got.astype(jnp.float32)


def across_groups_sum(halves):
    head_group = lax.axis_index("head")
    heads = lax.axis_size("head")
    groups = heads // 2
    outer = head_group // 2
    total = lax.dynamic_index_in_dim(halves, outer, 0, keepdims=False)
    for step in range(1, groups):
        target = (outer + step) % groups
        piece = lax.dynamic_index_in_dim(halves, target, 0, keepdims=False).astype(jnp.bfloat16)
        pairs = [(h, (((h // 2) + step) % groups) * 2 + h % 2) for h in range(heads)]
        total = total + lax.ppermute(piece, "head", pairs).astype(jnp.float32)
    return total


def shift_down_sum(halves, entering):
    head_group = lax.axis_index("head")
    heads = lax.axis_size("head")
    segments = lax.axis_size("segment")
    groups = heads // 2
    outer = head_group // 2
    total = []
    for step in range(groups):
        target = (outer + step) % groups
        piece = lax.dynamic_index_in_dim(halves, target, 0, keepdims=False)
        if step == 0:
            piece = piece + entering
        pairs = []
        for s in range(1, segments):
            for h in range(heads):
                dest = (((h // 2) + step) % groups) * 2 + h % 2
                pairs.append((s * heads + h, (s - 1) * heads + dest))
        total.append(lax.ppermute(piece.astype(jnp.bfloat16), ("segment", "head"), pairs))
    return total


def row_norm(values):
    return values * lax.rsqrt(jnp.mean(values * values, axis=-1, keepdims=True) + EPS)


def _attention_weights(meta_ref, scale_ref, win_ref, summ_ref, ask_ref, look_ref, *, tick, heads_local, block):
    live = meta_ref[0]
    band_rows = BAND * block
    own = win_ref[tick * block : (tick + 1) * block, :]
    band = win_ref[tick * block : tick * block + band_rows, :]
    queries = jnp.dot(own, ask_ref[...], preferred_element_type=jnp.float32)
    band_keys = jnp.dot(band, look_ref[...], preferred_element_type=jnp.float32)
    glob_keys = [
        jnp.dot(summ_ref[meta_ref[1 + g]], look_ref[...], preferred_element_type=jnp.float32)
        for g in range(GLOB)
    ]
    key_ids = lax.broadcasted_iota(jnp.int32, (band_rows, block), 0)
    query_ids = lax.broadcasted_iota(jnp.int32, (band_rows, block), 1)
    band_open = (key_ids >= block) | (key_ids <= query_ids)
    live_vec = jnp.zeros((block, block), jnp.int32) + live
    contract = (((1,), (1,)), ((), ()))
    for h in range(heads_local):
        cols = slice(h * CHANNEL_WIDTH, (h + 1) * CHANNEL_WIDTH)
        scale = scale_ref[h]
        qh = row_norm(queries[:, cols])
        kb = row_norm(band_keys[:, cols])
        sb = lax.dot_general(kb, qh, contract, precision=lax.Precision.HIGHEST, preferred_element_type=jnp.float32) * scale
        eb = jnp.where(band_open, jnp.exp(sb), 0.0)
        denom = jnp.sum(eb, axis=0, keepdims=True)
        eg = []
        for g in range(GLOB):
            kg = row_norm(glob_keys[g][:, cols])
            sg = lax.dot_general(kg, qh, contract, precision=lax.Precision.HIGHEST, preferred_element_type=jnp.float32) * scale
            e = jnp.where(live_vec > g, jnp.exp(sg), 0.0)
            denom = denom + jnp.sum(e, axis=0, keepdims=True)
            eg.append(e)
        yield h, (eb / denom).astype(jnp.bfloat16), [(e / denom).astype(jnp.bfloat16) for e in eg]


def _weights_kernel(meta_ref, scale_ref, win_ref, summ_ref, ask_ref, look_ref, out_ref, *, tick, heads_local, block):
    band_rows = BAND * block
    for h, ab, ags in _attention_weights(
        meta_ref, scale_ref, win_ref, summ_ref, ask_ref, look_ref, tick=tick, heads_local=heads_local, block=block
    ):
        out_ref[h, 0:band_rows, :] = ab
        for g, ag in enumerate(ags):
            lo = band_rows + g * block
            out_ref[h, lo : lo + block, :] = ag


def _partial_into(value_grad, w_ref, partial_ref):
    contract = (((1,), (1,)), ((), ()))
    for g in range(w_ref.shape[0]):
        for p in range(2):
            partial_ref[g, p] = lax.dot_general(
                value_grad, w_ref[g, p], contract, preferred_element_type=jnp.float32
            ).astype(partial_ref.dtype)


def _first_tick_kernel(
    sp_ref, scale_ref, win_ref, summ_ref, ask_ref, look_ref, ent_ref, prior_ref, w_ref,
    partial_ref, carried_ref, glob_ref, grad_out_ref, *, heads_local, block
):
    band_rows = BAND * block
    grad = ent_ref[...]
    grad_out_ref[...] = grad
    value_cols = []
    for h, ab, ags in _attention_weights(
        sp_ref.at[1:], scale_ref, win_ref, summ_ref, ask_ref, look_ref, tick=0, heads_local=heads_local, block=block
    ):
        cols = slice(h * CHANNEL_WIDTH, (h + 1) * CHANNEL_WIDTH)
        gh = grad[:, cols]
        band = jnp.dot(ab, gh, preferred_element_type=jnp.float32)
        own = prior_ref[0:block, cols].astype(jnp.float32) + band[0:block]
        value_cols.append(own.astype(jnp.bfloat16))
        carried_ref[:, cols] = prior_ref[block : 2 * block, cols].astype(jnp.float32) + band[block : 2 * block]
        for g, ag in enumerate(ags):
            glob_ref[g * block : (g + 1) * block, cols] = jnp.dot(ag, gh, preferred_element_type=jnp.float32)
    value_grad = value_cols[0] if len(value_cols) == 1 else jnp.concatenate(value_cols, axis=1)
    _partial_into(value_grad, w_ref, partial_ref)


def _last_tick_kernel(sp_ref, att_ref, fresh_ref, carried_ref, w_ref, *rest, heads_local, block, groups):
    pieces = rest[:groups]
    partial_ref, glob_ref, grad_out_ref = rest[groups:]
    band_rows = BAND * block
    arrived = pieces[0][...].astype(jnp.float32)
    for piece in pieces[1:]:
        arrived = arrived + piece[...].astype(jnp.float32)
    flag = jnp.zeros(arrived.shape, jnp.int32) + sp_ref[1]
    grad = jnp.where(flag > 0, fresh_ref[...], arrived.astype(jnp.bfloat16))
    grad_out_ref[...] = grad
    value_cols = []
    for h in range(heads_local):
        cols = slice(h * CHANNEL_WIDTH, (h + 1) * CHANNEL_WIDTH)
        gh = grad[:, cols]
        own = carried_ref[:, cols] + jnp.dot(att_ref[h, 0:block, :], gh, preferred_element_type=jnp.float32)
        value_cols.append(own.astype(jnp.bfloat16))
        for g in range(GLOB):
            lo = band_rows + g * block
            glob_ref[g * block : (g + 1) * block, cols] = jnp.dot(
                att_ref[h, lo : lo + block, :], gh, preferred_element_type=jnp.float32
            )
    value_grad = value_cols[0] if len(value_cols) == 1 else jnp.concatenate(value_cols, axis=1)
    _partial_into(value_grad, w_ref, partial_ref)


def _full(shape):
    return pl.BlockSpec(shape, lambda i, sp: (0,) * len(shape))


def first_tick(sp, scales, window_inputs, summary_blocks, asker, lookup, entering, prior, weights):
    block = summary_blocks.shape[1]
    local_width = asker.shape[1]
    heads_local = local_width // CHANNEL_WIDTH
    groups = weights.shape[0]
    keys_total = (BAND + GLOB) * block
    feat = window_inputs.shape[1]
    flops = 2 * feat * local_width * (block + keys_total) + 14 * keys_total * block * local_width + 2 * block * local_width * groups * 2 * local_width
    grid_spec = pltpu.PrefetchScalarGridSpec(
        num_scalar_prefetch=1,
        grid=(1,),
        in_specs=[
            pl.BlockSpec(memory_space=pltpu.SMEM),
            _full(window_inputs.shape),
            _full(summary_blocks.shape),
            _full(asker.shape),
            _full(lookup.shape),
            pl.BlockSpec((block, local_width), lambda i, sp: (0, sp[0])),
            _full(prior.shape),
            _full(weights.shape),
        ],
        out_specs=[
            _full((groups, 2, block, local_width)),
            _full((block, local_width)),
            _full((GLOB * block, local_width)),
            _full((block, local_width)),
        ],
    )
    return pl.pallas_call(
        functools.partial(_first_tick_kernel, heads_local=heads_local, block=block),
        grid_spec=grid_spec,
        out_shape=(
            jax.ShapeDtypeStruct((groups, 2, block, local_width), jnp.bfloat16),
            jax.ShapeDtypeStruct((block, local_width), jnp.float32),
            jax.ShapeDtypeStruct((GLOB * block, local_width), jnp.float32),
            jax.ShapeDtypeStruct((block, local_width), entering.dtype),
        ),
        compiler_params=pltpu.CompilerParams(vmem_limit_bytes=48 * 1024 * 1024),
        cost_estimate=pl.CostEstimate(flops=flops, transcendentals=keys_total * block * heads_local, bytes_accessed=weights.size * 2 + 8 * block * local_width * 4),
    )(sp, scales, window_inputs, summary_blocks, asker, lookup, entering, prior, weights)


def last_tick(sp, att, fresh, carried, weights, pieces):
    heads_local, keys_total, block = att.shape
    local_width = carried.shape[1]
    groups = weights.shape[0]
    flops = 2 * keys_total * block * local_width + 2 * block * local_width * groups * 2 * local_width
    grid_spec = pltpu.PrefetchScalarGridSpec(
        num_scalar_prefetch=1,
        grid=(1,),
        in_specs=[
            _full(att.shape),
            pl.BlockSpec((block, local_width), lambda i, sp: (0, sp[0])),
            _full(carried.shape),
            _full(weights.shape),
        ]
        + [_full(p.shape) for p in pieces],
        out_specs=[
            _full((groups, 2, block, local_width)),
            _full((GLOB * block, local_width)),
            _full((block, local_width)),
        ],
    )
    return pl.pallas_call(
        functools.partial(_last_tick_kernel, heads_local=heads_local, block=block, groups=len(pieces)),
        grid_spec=grid_spec,
        out_shape=(
            jax.ShapeDtypeStruct((groups, 2, block, local_width), jnp.bfloat16),
            jax.ShapeDtypeStruct((GLOB * block, local_width), jnp.float32),
            jax.ShapeDtypeStruct((block, local_width), fresh.dtype),
        ),
        compiler_params=pltpu.CompilerParams(vmem_limit_bytes=48 * 1024 * 1024),
        cost_estimate=pl.CostEstimate(flops=flops, transcendentals=0, bytes_accessed=weights.size * 2 + att.size * 2 + 8 * block * local_width * 4),
    )(sp, att, fresh, carried, weights, *pieces)


def attention_weights(tick, meta, scales, window_inputs, summary_blocks, asker, lookup):
    block = summary_blocks.shape[1]
    local_width = asker.shape[1]
    heads_local = local_width // CHANNEL_WIDTH
    keys_total = (BAND + GLOB) * block
    feat = window_inputs.shape[1]
    flops = 2 * feat * local_width * (block + keys_total) + 2 * 6 * keys_total * block * local_width
    vmem = pl.BlockSpec(memory_space=pltpu.VMEM)
    smem = pl.BlockSpec(memory_space=pltpu.SMEM)
    return pl.pallas_call(
        functools.partial(_weights_kernel, tick=tick, heads_local=heads_local, block=block),
        out_shape=jax.ShapeDtypeStruct((heads_local, keys_total, block), jnp.bfloat16),
        in_specs=[smem, smem, vmem, vmem, vmem, vmem],
        out_specs=vmem,
        cost_estimate=pl.CostEstimate(flops=flops, transcendentals=keys_total * block * heads_local, bytes_accessed=keys_total * local_width * 2 + 4 * feat * local_width * 2),
    )(meta, scales, window_inputs, summary_blocks, asker, lookup)


def local(
    entering_deriv,
    objective_derivs,
    content_projection,
    asker_projection,
    lookup_projection,
    softness,
    window_inputs,
    digest_inputs,
    digest_pointer,
    initial_segment,
    prior_content_derivs,
):
    period_label = lax.axis_index("segment")
    phases = lax.axis_size("segment")
    head_group = lax.axis_index("head")
    heads = lax.axis_size("head")
    groups = heads // 2
    block_rows = entering_deriv.shape[0]
    local_width = content_projection.shape[1]
    summary_blocks = digest_inputs.reshape(SUMMARY, block_rows, digest_inputs.shape[1])
    scales = softness[0] / CHANNEL_WIDTH
    weights = content_projection.reshape(groups, 2, local_width, local_width)
    summary_ids = jnp.arange(SUMMARY, dtype=jnp.int32)

    def live_of(tick_index):
        position = initial_segment[0] - period_label - tick_index
        return jnp.minimum(GLOB, 1 + GLOB * position // SEQ_BLOCKS)

    def digest_of(tick_index, glob):
        selector = (digest_pointer[tick_index][:, None] == summary_ids[None, :]).astype(jnp.float32)
        return jnp.sum(
            selector[:, :, None, None] * glob.reshape(GLOB, block_rows, local_width)[:, None], axis=0
        ).reshape(SUMMARY * block_rows, local_width)

    sp0 = jnp.concatenate(
        [head_group.astype(jnp.int32)[None], live_of(0)[None], digest_pointer[0]]
    ).astype(jnp.int32)
    partial0, carried, glob0, grad0 = first_tick(
        sp0, scales, window_inputs, summary_blocks, asker_projection, lookup_projection,
        entering_deriv, prior_content_derivs, weights,
    )
    partial0, feats = lax.optimization_barrier((partial0, (window_inputs, asker_projection, lookup_projection)))
    later_meta = jnp.concatenate([live_of(1)[None], digest_pointer[1]]).astype(jnp.int32)
    later_att = attention_weights(1, later_meta, scales, feats[0], summary_blocks, feats[1], feats[2])
    halves = core_pair_sum(partial0)
    pieces = shift_down_sum(halves, grad0.astype(jnp.float32))
    digest_running = digest_of(0, glob0)
    sp1 = jnp.stack([head_group.astype(jnp.int32), (period_label == phases - 1).astype(jnp.int32)])
    partial1, glob1, grad1 = last_tick(
        sp1, later_att, objective_derivs[0:block_rows], carried, weights, pieces
    )
    digest_running = digest_running + digest_of(1, glob1)
    summed = across_groups_sum(core_pair_sum(partial1))
    result = (grad1.astype(jnp.float32) + summed).astype(jnp.bfloat16)
    return (result, digest_running.astype(jnp.bfloat16))


def solution(mesh):
    in_specs = (
        P("segment", None),
        P(),
        P("segment", "head"),
        P("segment", "head"),
        P("segment", "head"),
        P("segment", "head"),
        P("segment", None),
        P(),
        P("segment", None),
        P(),
        P("segment", "head"),
    )
    out_specs = (P("segment", "head"), P("segment", "head"))
    return jax.shard_map(local, mesh=mesh, in_specs=in_specs, out_specs=out_specs, check_vma=False)
```

```python
import jax
import jax.numpy as jnp
from jax import lax
from jax.sharding import PartitionSpec as P
from jax.experimental import pallas as pl
from jax.experimental.pallas import tpu as pltpu
import functools

CHANNEL_WIDTH = 128
BAND = 4
GLOB = 2
SUMMARY = 2
SEQ_BLOCKS = 1024
TICKS = 2


EPS = 1e-06


def shifted(value, axis, steps):
    count = lax.axis_size(axis)
    first, last = (max(0, -steps), min(count, count - steps))
    return lax.ppermute(value, axis, [(source, source + steps) for source in range(first, last)])


def core_pair_sum(partial):
    head_group = lax.axis_index("head")
    heads = lax.axis_size("head")
    core = head_group % 2
    keep = lax.dynamic_index_in_dim(partial, core, 1, keepdims=False)
    send = lax.dynamic_index_in_dim(partial, 1 - core, 1, keepdims=False)
    got = lax.ppermute(send, "head", [(h, h ^ 1) for h in range(heads)])
    return keep.astype(jnp.float32) + got.astype(jnp.float32)


def across_groups_sum(halves):
    head_group = lax.axis_index("head")
    heads = lax.axis_size("head")
    groups = heads // 2
    outer = head_group // 2
    total = lax.dynamic_index_in_dim(halves, outer, 0, keepdims=False)
    for step in range(1, groups):
        target = (outer + step) % groups
        piece = lax.dynamic_index_in_dim(halves, target, 0, keepdims=False).astype(jnp.bfloat16)
        pairs = [(h, (((h // 2) + step) % groups) * 2 + h % 2) for h in range(heads)]
        total = total + lax.ppermute(piece, "head", pairs).astype(jnp.float32)
    return total


def shift_down_sum(halves, entering):
    head_group = lax.axis_index("head")
    heads = lax.axis_size("head")
    segments = lax.axis_size("segment")
    groups = heads // 2
    outer = head_group // 2
    total = []
    for step in range(groups):
        target = (outer + step) % groups
        piece = lax.dynamic_index_in_dim(halves, target, 0, keepdims=False)
        if step == 0:
            piece = piece + entering
        pairs = []
        for s in range(1, segments):
            for h in range(heads):
                dest = (((h // 2) + step) % groups) * 2 + h % 2
                pairs.append((s * heads + h, (s - 1) * heads + dest))
        total.append(lax.ppermute(piece.astype(jnp.bfloat16), ("segment", "head"), pairs))
    return total


def row_norm(values):
    return values * lax.rsqrt(jnp.mean(values * values, axis=-1, keepdims=True) + EPS)


def _live_of(init_ref, tick):
    position = init_ref[...] - lax.axis_index("segment") - tick
    shift = SEQ_BLOCKS.bit_length() - 1
    return jnp.minimum(GLOB, 1 + lax.shift_right_arithmetic(GLOB * position, jnp.int32(shift)))


def _pick_columns(full_ref, width):
    head = jnp.zeros((1, 1), jnp.int32) + lax.axis_index("head")
    picked = full_ref[:, 0:width]
    for j in range(1, full_ref.shape[1] // width):
        picked = jnp.where(head == j, full_ref[:, j * width : (j + 1) * width], picked)
    return picked


def _attention_weights(init_ref, ptr_ref, soft_ref, win_ref, summ_ref, ask_ref, look_ref, *, tick, heads_local, block):
    band_rows = BAND * block
    live = _live_of(init_ref, tick)
    own = win_ref[tick * block : (tick + 1) * block, :]
    band = win_ref[tick * block : tick * block + band_rows, :]
    queries = jnp.dot(own, ask_ref[...], preferred_element_type=jnp.float32)
    band_keys = jnp.dot(band, look_ref[...], preferred_element_type=jnp.float32)
    summary_keys = [
        jnp.dot(summ_ref[m], look_ref[...], preferred_element_type=jnp.float32) for m in range(summ_ref.shape[0])
    ]
    glob_keys = []
    for g in range(GLOB):
        slot = ptr_ref[tick : tick + 1, g : g + 1]
        picked = summary_keys[0]
        for m in range(1, len(summary_keys)):
            picked = jnp.where(slot == m, summary_keys[m], picked)
        glob_keys.append(picked)
    key_ids = lax.broadcasted_iota(jnp.int32, (band_rows, block), 0)
    query_ids = lax.broadcasted_iota(jnp.int32, (band_rows, block), 1)
    band_open = (key_ids >= block) | (key_ids <= query_ids)
    contract = (((1,), (1,)), ((), ()))
    for h in range(heads_local):
        cols = slice(h * CHANNEL_WIDTH, (h + 1) * CHANNEL_WIDTH)
        scale = soft_ref[0:1, h : h + 1] * (1.0 / CHANNEL_WIDTH)
        qh = row_norm(queries[:, cols])
        kb = row_norm(band_keys[:, cols])
        sb = lax.dot_general(kb, qh, contract, precision=lax.Precision.HIGHEST, preferred_element_type=jnp.float32) * scale
        eb = jnp.where(band_open, jnp.exp(sb), 0.0)
        denom = jnp.sum(eb, axis=0, keepdims=True)
        eg = []
        for g in range(GLOB):
            kg = row_norm(glob_keys[g][:, cols])
            sg = lax.dot_general(kg, qh, contract, precision=lax.Precision.HIGHEST, preferred_element_type=jnp.float32) * scale
            e = jnp.where(live > g, jnp.exp(sg), 0.0)
            denom = denom + jnp.sum(e, axis=0, keepdims=True)
            eg.append(e)
        yield h, (eb / denom).astype(jnp.bfloat16), [(e / denom).astype(jnp.bfloat16) for e in eg]


def _weights_kernel(init_ref, ptr_ref, soft_ref, win_ref, summ_ref, ask_ref, look_ref, out_ref, *, tick, heads_local, block):
    band_rows = BAND * block
    for h, ab, ags in _attention_weights(
        init_ref, ptr_ref, soft_ref, win_ref, summ_ref, ask_ref, look_ref, tick=tick, heads_local=heads_local, block=block
    ):
        out_ref[h, 0:band_rows, :] = ab
        for g, ag in enumerate(ags):
            lo = band_rows + g * block
            out_ref[h, lo : lo + block, :] = ag


def _partial_into(value_grad, w_ref, partial_ref):
    contract = (((1,), (1,)), ((), ()))
    for g in range(w_ref.shape[0]):
        for p in range(2):
            partial_ref[g, p] = lax.dot_general(
                value_grad, w_ref[g, p], contract, preferred_element_type=jnp.float32
            ).astype(partial_ref.dtype)


def _first_tick_kernel(
    init_ref, ptr_ref, soft_ref, win_ref, summ_ref, ask_ref, look_ref, ent_ref, prior_ref, w_ref,
    partial_ref, carried_ref, glob_ref, grad_out_ref, *, heads_local, block
):
    weights = list(_attention_weights(
        init_ref, ptr_ref, soft_ref, win_ref, summ_ref, ask_ref, look_ref, tick=0, heads_local=heads_local, block=block
    ))
    grad = _pick_columns(ent_ref, grad_out_ref.shape[1])
    grad_out_ref[...] = grad
    value_cols = []
    for h, ab, ags in weights:
        cols = slice(h * CHANNEL_WIDTH, (h + 1) * CHANNEL_WIDTH)
        gh = grad[:, cols]
        band = jnp.dot(ab, gh, preferred_element_type=jnp.float32)
        own = prior_ref[0:block, cols].astype(jnp.float32) + band[0:block]
        value_cols.append(own.astype(jnp.bfloat16))
        carried_ref[:, cols] = prior_ref[block : 2 * block, cols].astype(jnp.float32) + band[block : 2 * block]
        for g, ag in enumerate(ags):
            glob_ref[g * block : (g + 1) * block, cols] = jnp.dot(ag, gh, preferred_element_type=jnp.float32)
    value_grad = value_cols[0] if len(value_cols) == 1 else jnp.concatenate(value_cols, axis=1)
    _partial_into(value_grad, w_ref, partial_ref)


def _last_tick_kernel(obj_ref, att_ref, carried_ref, w_ref, *rest, heads_local, block, groups, phases):
    pieces = rest[:groups]
    partial_ref, glob_ref, grad_out_ref = rest[groups:]
    band_rows = BAND * block
    arrived = pieces[0][...].astype(jnp.float32)
    for piece in pieces[1:]:
        arrived = arrived + piece[...].astype(jnp.float32)
    last = jnp.zeros((1, 1), jnp.int32) + (lax.axis_index("segment") == phases - 1).astype(jnp.int32)
    fresh = _pick_columns(obj_ref, grad_out_ref.shape[1])
    grad = jnp.where(last > 0, fresh, arrived.astype(jnp.bfloat16))
    grad_out_ref[...] = grad
    value_cols = []
    for h in range(heads_local):
        cols = slice(h * CHANNEL_WIDTH, (h + 1) * CHANNEL_WIDTH)
        gh = grad[:, cols]
        own = carried_ref[:, cols] + jnp.dot(att_ref[h, 0:block, :], gh, preferred_element_type=jnp.float32)
        value_cols.append(own.astype(jnp.bfloat16))
        for g in range(GLOB):
            lo = band_rows + g * block
            glob_ref[g * block : (g + 1) * block, cols] = jnp.dot(
                att_ref[h, lo : lo + block, :], gh, preferred_element_type=jnp.float32
            )
    value_grad = value_cols[0] if len(value_cols) == 1 else jnp.concatenate(value_cols, axis=1)
    _partial_into(value_grad, w_ref, partial_ref)


VMEM = pl.BlockSpec(memory_space=pltpu.VMEM)
KERNEL_PARAMS = pltpu.CompilerParams(vmem_limit_bytes=48 * 1024 * 1024)


def first_tick(initial_segment, digest_pointer, softness, window_inputs, summary_blocks, asker, lookup, prior, weights, entering):
    block = summary_blocks.shape[1]
    local_width = asker.shape[1]
    heads_local = local_width // CHANNEL_WIDTH
    groups = weights.shape[0]
    keys_total = (BAND + GLOB) * block
    feat = window_inputs.shape[1]
    flops = 2 * feat * local_width * (block + keys_total) + 14 * keys_total * block * local_width + 4 * block * local_width * groups * local_width
    ins = [initial_segment, digest_pointer, softness, window_inputs, summary_blocks, asker, lookup, entering, prior, weights]
    return pl.pallas_call(
        functools.partial(_first_tick_kernel, heads_local=heads_local, block=block),
        out_shape=(
            jax.ShapeDtypeStruct((groups, 2, block, local_width), jnp.bfloat16),
            jax.ShapeDtypeStruct((block, local_width), jnp.float32),
            jax.ShapeDtypeStruct((GLOB * block, local_width), jnp.float32),
            jax.ShapeDtypeStruct((block, local_width), entering.dtype),
        ),
        in_specs=[VMEM] * len(ins),
        out_specs=(VMEM, VMEM, VMEM, VMEM),
        compiler_params=KERNEL_PARAMS,
        cost_estimate=pl.CostEstimate(flops=flops, transcendentals=keys_total * block * heads_local, bytes_accessed=weights.size * 2 + 8 * block * local_width * 4),
    )(*ins)


def last_tick(att, carried, weights, objective, pieces, phases):
    heads_local, keys_total, block = att.shape
    local_width = carried.shape[1]
    groups = weights.shape[0]
    flops = 2 * keys_total * block * local_width + 4 * block * local_width * groups * local_width
    ins = [objective, att, carried, weights] + list(pieces)
    return pl.pallas_call(
        functools.partial(_last_tick_kernel, heads_local=heads_local, block=block, groups=len(pieces), phases=phases),
        out_shape=(
            jax.ShapeDtypeStruct((groups, 2, block, local_width), jnp.bfloat16),
            jax.ShapeDtypeStruct((GLOB * block, local_width), jnp.float32),
            jax.ShapeDtypeStruct((block, local_width), objective.dtype),
        ),
        in_specs=[VMEM] * len(ins),
        out_specs=(VMEM, VMEM, VMEM),
        compiler_params=KERNEL_PARAMS,
        cost_estimate=pl.CostEstimate(flops=flops, transcendentals=0, bytes_accessed=weights.size * 2 + att.size * 2 + 8 * block * local_width * 4),
    )(*ins)


def attention_weights(tick, initial_segment, digest_pointer, softness, window_inputs, summary_blocks, asker, lookup):
    block = summary_blocks.shape[1]
    local_width = asker.shape[1]
    heads_local = local_width // CHANNEL_WIDTH
    keys_total = (BAND + GLOB) * block
    feat = window_inputs.shape[1]
    flops = 2 * feat * local_width * (block + keys_total) + 12 * keys_total * block * local_width
    ins = [initial_segment, digest_pointer, softness, window_inputs, summary_blocks, asker, lookup]
    return pl.pallas_call(
        functools.partial(_weights_kernel, tick=tick, heads_local=heads_local, block=block),
        out_shape=jax.ShapeDtypeStruct((heads_local, keys_total, block), jnp.bfloat16),
        in_specs=[VMEM] * len(ins),
        out_specs=VMEM,
        compiler_params=KERNEL_PARAMS,
        cost_estimate=pl.CostEstimate(flops=flops, transcendentals=keys_total * block * heads_local, bytes_accessed=keys_total * local_width * 2 + 4 * feat * local_width * 2),
    )(*ins)


def local(
    entering_deriv,
    objective_derivs,
    content_projection,
    asker_projection,
    lookup_projection,
    softness,
    window_inputs,
    digest_inputs,
    digest_pointer,
    initial_segment,
    prior_content_derivs,
):
    period_label = lax.axis_index("segment")
    phases = lax.axis_size("segment")
    head_group = lax.axis_index("head")
    heads = lax.axis_size("head")
    groups = heads // 2
    block_rows = entering_deriv.shape[0]
    local_width = content_projection.shape[1]
    summary_blocks = digest_inputs.reshape(SUMMARY, block_rows, digest_inputs.shape[1])
    weights = content_projection.reshape(groups, 2, local_width, local_width)
    summary_ids = jnp.arange(SUMMARY, dtype=jnp.int32)

    def live_of(tick_index):
        position = initial_segment[0] - period_label - tick_index
        return jnp.minimum(GLOB, 1 + GLOB * position // SEQ_BLOCKS)

    def digest_of(tick_index, glob):
        selector = (digest_pointer[tick_index][:, None] == summary_ids[None, :]).astype(jnp.float32)
        return jnp.sum(
            selector[:, :, None, None] * glob.reshape(GLOB, block_rows, local_width)[:, None], axis=0
        ).reshape(SUMMARY * block_rows, local_width)

    init = initial_segment.reshape(1, 1)
    partial0, carried, glob0, grad0 = first_tick(
        init, digest_pointer, softness, window_inputs, summary_blocks,
        asker_projection, lookup_projection, prior_content_derivs, weights, entering_deriv,
    )
    partial0, feats = lax.optimization_barrier((partial0, (window_inputs, asker_projection, lookup_projection)))
    later_att = attention_weights(
        1, init, digest_pointer, softness, feats[0], summary_blocks, feats[1], feats[2]
    )
    halves = core_pair_sum(partial0)
    pieces = shift_down_sum(halves, grad0.astype(jnp.float32))
    digest_running = digest_of(0, glob0)
    partial1, glob1, grad1 = last_tick(
        later_att, carried, weights, objective_derivs[0:block_rows], pieces, phases
    )
    digest_running = digest_running + digest_of(1, glob1)
    summed = across_groups_sum(core_pair_sum(partial1))
    result = (grad1.astype(jnp.float32) + summed).astype(jnp.bfloat16)
    return (result, digest_running.astype(jnp.bfloat16))


def solution(mesh):
    in_specs = (
        P("segment", None),
        P(),
        P("segment", "head"),
        P("segment", "head"),
        P("segment", "head"),
        P("segment", "head"),
        P("segment", None),
        P(),
        P("segment", None),
        P(),
        P("segment", "head"),
    )
    out_specs = (P("segment", "head"), P("segment", "head"))
    return jax.shard_map(local, mesh=mesh, in_specs=in_specs, out_specs=out_specs, check_vma=False)
```

```python
import jax
import jax.numpy as jnp
from jax import lax
from jax.sharding import PartitionSpec as P
from jax.experimental import pallas as pl
from jax.experimental.pallas import tpu as pltpu
import functools

CHANNEL_WIDTH = 128
BAND = 4
GLOB = 2
SUMMARY = 2
SEQ_BLOCKS = 1024
TICKS = 2


EPS = 1e-06


def shifted(value, axis, steps):
    count = lax.axis_size(axis)
    first, last = (max(0, -steps), min(count, count - steps))
    return lax.ppermute(value, axis, [(source, source + steps) for source in range(first, last)])


def core_pair_sum(partial):
    head_group = lax.axis_index("head")
    heads = lax.axis_size("head")
    core = head_group % 2
    keep = lax.dynamic_index_in_dim(partial, core, 1, keepdims=False)
    send = lax.dynamic_index_in_dim(partial, 1 - core, 1, keepdims=False)
    got = lax.ppermute(send, "head", [(h, h ^ 1) for h in range(heads)])
    return keep.astype(jnp.float32) + got.astype(jnp.float32)


def across_groups_sum(halves):
    head_group = lax.axis_index("head")
    heads = lax.axis_size("head")
    groups = heads // 2
    outer = head_group // 2
    total = lax.dynamic_index_in_dim(halves, outer, 0, keepdims=False)
    for step in range(1, groups):
        target = (outer + step) % groups
        piece = lax.dynamic_index_in_dim(halves, target, 0, keepdims=False).astype(jnp.bfloat16)
        pairs = [(h, (((h // 2) + step) % groups) * 2 + h % 2) for h in range(heads)]
        total = total + lax.ppermute(piece, "head", pairs).astype(jnp.float32)
    return total


def shift_down_sum(halves, entering):
    head_group = lax.axis_index("head")
    heads = lax.axis_size("head")
    segments = lax.axis_size("segment")
    groups = heads // 2
    outer = head_group // 2
    total = []
    for step in range(groups):
        target = (outer + step) % groups
        piece = lax.dynamic_index_in_dim(halves, target, 0, keepdims=False)
        if step == 0:
            piece = piece + entering
        pairs = []
        for s in range(1, segments):
            for h in range(heads):
                dest = (((h // 2) + step) % groups) * 2 + h % 2
                pairs.append((s * heads + h, (s - 1) * heads + dest))
        total.append(lax.ppermute(piece.astype(jnp.bfloat16), ("segment", "head"), pairs))
    return total


def row_norm(values):
    return values * lax.rsqrt(jnp.mean(values * values, axis=-1, keepdims=True) + EPS)


def _live_of(init_ref, tick):
    position = init_ref[...] - lax.axis_index("segment") - tick
    shift = SEQ_BLOCKS.bit_length() - 1
    return jnp.minimum(GLOB, 1 + lax.shift_right_arithmetic(GLOB * position, jnp.int32(shift)))


def _pick_columns(full_ref, width):
    head = jnp.zeros((1, 1), jnp.int32) + lax.axis_index("head")
    picked = full_ref[:, 0:width]
    for j in range(1, full_ref.shape[1] // width):
        picked = jnp.where(head == j, full_ref[:, j * width : (j + 1) * width], picked)
    return picked


def _attention_weights(init_ref, ptr_ref, soft_ref, win_ref, summ_ref, ask_ref, look_ref, *, tick, heads_local, block):
    band_rows = BAND * block
    live = _live_of(init_ref, tick)
    own = win_ref[tick * block : (tick + 1) * block, :]
    band = win_ref[tick * block : tick * block + band_rows, :]
    queries = jnp.dot(own, ask_ref[...], preferred_element_type=jnp.float32)
    band_keys = jnp.dot(band, look_ref[...], preferred_element_type=jnp.float32)
    summary_keys = [
        jnp.dot(summ_ref[m], look_ref[...], preferred_element_type=jnp.float32) for m in range(summ_ref.shape[0])
    ]
    glob_keys = []
    for g in range(GLOB):
        slot = ptr_ref[tick : tick + 1, g : g + 1]
        picked = summary_keys[0]
        for m in range(1, len(summary_keys)):
            picked = jnp.where(slot == m, summary_keys[m], picked)
        glob_keys.append(picked)
    key_ids = lax.broadcasted_iota(jnp.int32, (band_rows, block), 0)
    query_ids = lax.broadcasted_iota(jnp.int32, (band_rows, block), 1)
    band_open = (key_ids >= block) | (key_ids <= query_ids)
    contract = (((1,), (1,)), ((), ()))
    for h in range(heads_local):
        cols = slice(h * CHANNEL_WIDTH, (h + 1) * CHANNEL_WIDTH)
        scale = soft_ref[0:1, h : h + 1] * (1.0 / CHANNEL_WIDTH)
        qh = row_norm(queries[:, cols])
        kb = row_norm(band_keys[:, cols])
        sb = lax.dot_general(kb, qh, contract, precision=lax.Precision.HIGHEST, preferred_element_type=jnp.float32) * scale
        eb = jnp.where(band_open, jnp.exp(sb), 0.0)
        denom = jnp.sum(eb, axis=0, keepdims=True)
        eg = []
        for g in range(GLOB):
            kg = row_norm(glob_keys[g][:, cols])
            sg = lax.dot_general(kg, qh, contract, precision=lax.Precision.HIGHEST, preferred_element_type=jnp.float32) * scale
            e = jnp.where(live > g, jnp.exp(sg), 0.0)
            denom = denom + jnp.sum(e, axis=0, keepdims=True)
            eg.append(e)
        yield h, (eb / denom).astype(jnp.bfloat16), [(e / denom).astype(jnp.bfloat16) for e in eg]


def _weights_kernel(init_ref, ptr_ref, soft_ref, win_ref, summ_ref, ask_ref, look_ref, out_ref, *, tick, heads_local, block):
    band_rows = BAND * block
    for h, ab, ags in _attention_weights(
        init_ref, ptr_ref, soft_ref, win_ref, summ_ref, ask_ref, look_ref, tick=tick, heads_local=heads_local, block=block
    ):
        out_ref[h, 0:band_rows, :] = ab
        for g, ag in enumerate(ags):
            lo = band_rows + g * block
            out_ref[h, lo : lo + block, :] = ag


def _partial_into(value_grad, w_ref, partial_ref):
    contract = (((1,), (1,)), ((), ()))
    for g in range(w_ref.shape[0]):
        for p in range(2):
            partial_ref[g, p] = lax.dot_general(
                value_grad, w_ref[g, p], contract, preferred_element_type=jnp.float32
            ).astype(partial_ref.dtype)


def _first_tick_kernel(
    init_ref, ptr_ref, soft_ref, win_ref, summ_ref, ask_ref, look_ref, ent_ref, prior_ref, w_ref,
    partial_ref, carried_ref, glob_ref, grad_out_ref, *, heads_local, block
):
    weights = list(_attention_weights(
        init_ref, ptr_ref, soft_ref, win_ref, summ_ref, ask_ref, look_ref, tick=0, heads_local=heads_local, block=block
    ))
    grad = _pick_columns(ent_ref, grad_out_ref.shape[1])
    grad_out_ref[...] = grad
    value_cols = []
    for h, ab, ags in weights:
        cols = slice(h * CHANNEL_WIDTH, (h + 1) * CHANNEL_WIDTH)
        gh = grad[:, cols]
        band = jnp.dot(ab, gh, preferred_element_type=jnp.float32)
        own = prior_ref[0:block, cols].astype(jnp.float32) + band[0:block]
        value_cols.append(own.astype(jnp.bfloat16))
        carried_ref[:, cols] = prior_ref[block : 2 * block, cols].astype(jnp.float32) + band[block : 2 * block]
        for g, ag in enumerate(ags):
            glob_ref[g * block : (g + 1) * block, cols] = jnp.dot(ag, gh, preferred_element_type=jnp.float32)
    value_grad = value_cols[0] if len(value_cols) == 1 else jnp.concatenate(value_cols, axis=1)
    _partial_into(value_grad, w_ref, partial_ref)


def _last_tick_kernel(obj_ref, att_ref, carried_ref, w_ref, *rest, heads_local, block, groups, phases):
    pieces = rest[:groups]
    partial_ref, glob_ref, grad_out_ref = rest[groups:]
    band_rows = BAND * block
    arrived = pieces[0][...].astype(jnp.float32)
    for piece in pieces[1:]:
        arrived = arrived + piece[...].astype(jnp.float32)
    last = jnp.zeros((1, 1), jnp.int32) + (lax.axis_index("segment") == phases - 1).astype(jnp.int32)
    fresh = _pick_columns(obj_ref, grad_out_ref.shape[1])
    grad = jnp.where(last > 0, fresh, arrived.astype(jnp.bfloat16))
    grad_out_ref[...] = grad
    value_cols = []
    for h in range(heads_local):
        cols = slice(h * CHANNEL_WIDTH, (h + 1) * CHANNEL_WIDTH)
        gh = grad[:, cols]
        own = carried_ref[:, cols] + jnp.dot(att_ref[h, 0:block, :], gh, preferred_element_type=jnp.float32)
        value_cols.append(own.astype(jnp.bfloat16))
        for g in range(GLOB):
            lo = band_rows + g * block
            glob_ref[g * block : (g + 1) * block, cols] = jnp.dot(
                att_ref[h, lo : lo + block, :], gh, preferred_element_type=jnp.float32
            )
    value_grad = value_cols[0] if len(value_cols) == 1 else jnp.concatenate(value_cols, axis=1)
    _partial_into(value_grad, w_ref, partial_ref)


VMEM = pl.BlockSpec(memory_space=pltpu.VMEM)
KERNEL_PARAMS = pltpu.CompilerParams()


def first_tick(initial_segment, digest_pointer, softness, window_inputs, summary_blocks, asker, lookup, prior, weights, entering):
    block = summary_blocks.shape[1]
    local_width = asker.shape[1]
    heads_local = local_width // CHANNEL_WIDTH
    groups = weights.shape[0]
    keys_total = (BAND + GLOB) * block
    feat = window_inputs.shape[1]
    flops = 2 * feat * local_width * (block + keys_total) + 14 * keys_total * block * local_width + 4 * block * local_width * groups * local_width
    ins = [initial_segment, digest_pointer, softness, window_inputs, summary_blocks, asker, lookup, entering, prior, weights]
    return pl.pallas_call(
        functools.partial(_first_tick_kernel, heads_local=heads_local, block=block),
        out_shape=(
            jax.ShapeDtypeStruct((groups, 2, block, local_width), jnp.bfloat16),
            jax.ShapeDtypeStruct((block, local_width), jnp.float32),
            jax.ShapeDtypeStruct((GLOB * block, local_width), jnp.float32),
            jax.ShapeDtypeStruct((block, local_width), entering.dtype),
        ),
        in_specs=[VMEM] * len(ins),
        out_specs=(VMEM, VMEM, VMEM, VMEM),
        compiler_params=KERNEL_PARAMS,
        cost_estimate=pl.CostEstimate(flops=flops, transcendentals=keys_total * block * heads_local, bytes_accessed=weights.size * 2 + 8 * block * local_width * 4),
    )(*ins)


def last_tick(att, carried, weights, objective, pieces, phases):
    heads_local, keys_total, block = att.shape
    local_width = carried.shape[1]
    groups = weights.shape[0]
    flops = 2 * keys_total * block * local_width + 4 * block * local_width * groups * local_width
    ins = [objective, att, carried, weights] + list(pieces)
    return pl.pallas_call(
        functools.partial(_last_tick_kernel, heads_local=heads_local, block=block, groups=len(pieces), phases=phases),
        out_shape=(
            jax.ShapeDtypeStruct((groups, 2, block, local_width), jnp.bfloat16),
            jax.ShapeDtypeStruct((GLOB * block, local_width), jnp.float32),
            jax.ShapeDtypeStruct((block, local_width), objective.dtype),
        ),
        in_specs=[VMEM] * len(ins),
        out_specs=(VMEM, VMEM, VMEM),
        compiler_params=KERNEL_PARAMS,
        cost_estimate=pl.CostEstimate(flops=flops, transcendentals=0, bytes_accessed=weights.size * 2 + att.size * 2 + 8 * block * local_width * 4),
    )(*ins)


def attention_weights(tick, initial_segment, digest_pointer, softness, window_inputs, summary_blocks, asker, lookup):
    block = summary_blocks.shape[1]
    local_width = asker.shape[1]
    heads_local = local_width // CHANNEL_WIDTH
    keys_total = (BAND + GLOB) * block
    feat = window_inputs.shape[1]
    flops = 2 * feat * local_width * (block + keys_total) + 12 * keys_total * block * local_width
    ins = [initial_segment, digest_pointer, softness, window_inputs, summary_blocks, asker, lookup]
    return pl.pallas_call(
        functools.partial(_weights_kernel, tick=tick, heads_local=heads_local, block=block),
        out_shape=jax.ShapeDtypeStruct((heads_local, keys_total, block), jnp.bfloat16),
        in_specs=[VMEM] * len(ins),
        out_specs=VMEM,
        compiler_params=KERNEL_PARAMS,
        cost_estimate=pl.CostEstimate(flops=flops, transcendentals=keys_total * block * heads_local, bytes_accessed=keys_total * local_width * 2 + 4 * feat * local_width * 2),
    )(*ins)


def local(
    entering_deriv,
    objective_derivs,
    content_projection,
    asker_projection,
    lookup_projection,
    softness,
    window_inputs,
    digest_inputs,
    digest_pointer,
    initial_segment,
    prior_content_derivs,
):
    period_label = lax.axis_index("segment")
    phases = lax.axis_size("segment")
    head_group = lax.axis_index("head")
    heads = lax.axis_size("head")
    groups = heads // 2
    block_rows = entering_deriv.shape[0]
    local_width = content_projection.shape[1]
    summary_blocks = digest_inputs.reshape(SUMMARY, block_rows, digest_inputs.shape[1])
    weights = content_projection.reshape(groups, 2, local_width, local_width)
    summary_ids = jnp.arange(SUMMARY, dtype=jnp.int32)

    def live_of(tick_index):
        position = initial_segment[0] - period_label - tick_index
        return jnp.minimum(GLOB, 1 + GLOB * position // SEQ_BLOCKS)

    def digest_of(tick_index, glob):
        selector = (digest_pointer[tick_index][:, None] == summary_ids[None, :]).astype(jnp.float32)
        return jnp.sum(
            selector[:, :, None, None] * glob.reshape(GLOB, block_rows, local_width)[:, None], axis=0
        ).reshape(SUMMARY * block_rows, local_width)

    init = initial_segment.reshape(1, 1)
    partial0, carried, glob0, grad0 = first_tick(
        init, digest_pointer, softness, window_inputs, summary_blocks,
        asker_projection, lookup_projection, prior_content_derivs, weights, entering_deriv,
    )
    partial0, feats = lax.optimization_barrier((partial0, (window_inputs, asker_projection, lookup_projection)))
    later_att = attention_weights(
        1, init, digest_pointer, softness, feats[0], summary_blocks, feats[1], feats[2]
    )
    halves = core_pair_sum(partial0)
    pieces = shift_down_sum(halves, grad0.astype(jnp.float32))
    digest_running = digest_of(0, glob0)
    partial1, glob1, grad1 = last_tick(
        later_att, carried, weights, objective_derivs[0:block_rows], pieces, phases
    )
    digest_running = digest_running + digest_of(1, glob1)
    summed = across_groups_sum(core_pair_sum(partial1))
    result = (grad1.astype(jnp.float32) + summed).astype(jnp.bfloat16)
    return (result, digest_running.astype(jnp.bfloat16))


def solution(mesh):
    in_specs = (
        P("segment", None),
        P(),
        P("segment", "head"),
        P("segment", "head"),
        P("segment", "head"),
        P("segment", "head"),
        P("segment", None),
        P(),
        P("segment", None),
        P(),
        P("segment", "head"),
    )
    out_specs = (P("segment", "head"), P("segment", "head"))
    return jax.shard_map(local, mesh=mesh, in_specs=in_specs, out_specs=out_specs, check_vma=False)
```

```python
import jax
import jax.numpy as jnp
from jax import lax
from jax.sharding import PartitionSpec as P
from jax.experimental import pallas as pl
from jax.experimental.pallas import tpu as pltpu
import functools

CHANNEL_WIDTH = 128
BAND = 4
GLOB = 2
SUMMARY = 2
SEQ_BLOCKS = 1024
TICKS = 2


EPS = 1e-06


def shifted(value, axis, steps):
    count = lax.axis_size(axis)
    first, last = (max(0, -steps), min(count, count - steps))
    return lax.ppermute(value, axis, [(source, source + steps) for source in range(first, last)])


def core_pair_sum(partial):
    heads = lax.axis_size("head")
    keep, send = partial[0], partial[1]
    got = lax.ppermute(send, "head", [(h, h ^ 1) for h in range(heads)])
    return keep.astype(jnp.float32) + got.astype(jnp.float32)


def across_groups_sum(halves):
    head_group = lax.axis_index("head")
    heads = lax.axis_size("head")
    groups = heads // 2
    outer = head_group // 2
    total = lax.dynamic_index_in_dim(halves, outer, 0, keepdims=False)
    for step in range(1, groups):
        target = (outer + step) % groups
        piece = lax.dynamic_index_in_dim(halves, target, 0, keepdims=False).astype(jnp.bfloat16)
        pairs = [(h, (((h // 2) + step) % groups) * 2 + h % 2) for h in range(heads)]
        total = total + lax.ppermute(piece, "head", pairs).astype(jnp.float32)
    return total


def shift_down_sum(halves, entering):
    head_group = lax.axis_index("head")
    heads = lax.axis_size("head")
    segments = lax.axis_size("segment")
    groups = heads // 2
    outer = head_group // 2
    total = []
    for step in range(groups):
        target = (outer + step) % groups
        piece = lax.dynamic_index_in_dim(halves, target, 0, keepdims=False)
        if step == 0:
            piece = piece + entering
        pairs = []
        for s in range(1, segments):
            for h in range(heads):
                dest = (((h // 2) + step) % groups) * 2 + h % 2
                pairs.append((s * heads + h, (s - 1) * heads + dest))
        total.append(lax.ppermute(piece.astype(jnp.bfloat16), ("segment", "head"), pairs))
    return total


def row_norm(values):
    return values * lax.rsqrt(jnp.mean(values * values, axis=-1, keepdims=True) + EPS)


def _live_of(init_ref, tick):
    position = init_ref[...] - lax.axis_index("segment") - tick
    shift = SEQ_BLOCKS.bit_length() - 1
    return jnp.minimum(GLOB, 1 + lax.shift_right_arithmetic(GLOB * position, jnp.int32(shift)))


def _pick_columns(full_ref, width):
    head = jnp.zeros((1, 1), jnp.int32) + lax.axis_index("head")
    picked = full_ref[:, 0:width]
    for j in range(1, full_ref.shape[1] // width):
        picked = jnp.where(head == j, full_ref[:, j * width : (j + 1) * width], picked)
    return picked


def _attention_weights(init_ref, ptr_ref, soft_ref, win_ref, summ_ref, ask_ref, look_ref, *, tick, heads_local, block):
    band_rows = BAND * block
    live = _live_of(init_ref, tick)
    own = win_ref[tick * block : (tick + 1) * block, :]
    band = win_ref[tick * block : tick * block + band_rows, :]
    queries = jnp.dot(own, ask_ref[...], preferred_element_type=jnp.float32)
    band_keys = jnp.dot(band, look_ref[...], preferred_element_type=jnp.float32)
    summary_keys = [
        jnp.dot(summ_ref[m], look_ref[...], preferred_element_type=jnp.float32) for m in range(summ_ref.shape[0])
    ]
    glob_keys = []
    for g in range(GLOB):
        slot = ptr_ref[tick : tick + 1, g : g + 1]
        picked = summary_keys[0]
        for m in range(1, len(summary_keys)):
            picked = jnp.where(slot == m, summary_keys[m], picked)
        glob_keys.append(picked)
    key_ids = lax.broadcasted_iota(jnp.int32, (band_rows, block), 0)
    query_ids = lax.broadcasted_iota(jnp.int32, (band_rows, block), 1)
    band_open = (key_ids >= block) | (key_ids <= query_ids)
    contract = (((1,), (1,)), ((), ()))
    for h in range(heads_local):
        cols = slice(h * CHANNEL_WIDTH, (h + 1) * CHANNEL_WIDTH)
        scale = soft_ref[0:1, h : h + 1] * (1.0 / CHANNEL_WIDTH)
        qh = row_norm(queries[:, cols])
        kb = row_norm(band_keys[:, cols])
        sb = lax.dot_general(kb, qh, contract, precision=lax.Precision.HIGHEST, preferred_element_type=jnp.float32) * scale
        eb = jnp.where(band_open, jnp.exp(sb), 0.0)
        denom = jnp.sum(eb, axis=0, keepdims=True)
        eg = []
        for g in range(GLOB):
            kg = row_norm(glob_keys[g][:, cols])
            sg = lax.dot_general(kg, qh, contract, precision=lax.Precision.HIGHEST, preferred_element_type=jnp.float32) * scale
            e = jnp.where(live > g, jnp.exp(sg), 0.0)
            denom = denom + jnp.sum(e, axis=0, keepdims=True)
            eg.append(e)
        yield h, (eb / denom).astype(jnp.bfloat16), [(e / denom).astype(jnp.bfloat16) for e in eg]


def _weights_kernel(init_ref, ptr_ref, soft_ref, win_ref, summ_ref, ask_ref, look_ref, out_ref, *, tick, heads_local, block):
    band_rows = BAND * block
    for h, ab, ags in _attention_weights(
        init_ref, ptr_ref, soft_ref, win_ref, summ_ref, ask_ref, look_ref, tick=tick, heads_local=heads_local, block=block
    ):
        out_ref[h, 0:band_rows, :] = ab
        for g, ag in enumerate(ags):
            lo = band_rows + g * block
            out_ref[h, lo : lo + block, :] = ag


def _partial_into(value_grad, w_ref, partial_ref):
    contract = (((1,), (1,)), ((), ()))
    core = lax.axis_index("head") % 2
    for g in range(w_ref.shape[0]):
        for p in range(2):
            partial_ref[(p + core) % 2, g] = lax.dot_general(
                value_grad, w_ref[g, p], contract, preferred_element_type=jnp.float32
            ).astype(partial_ref.dtype)


def _first_tick_kernel(
    init_ref, ptr_ref, soft_ref, win_ref, summ_ref, ask_ref, look_ref, ent_ref, prior_ref, w_ref,
    partial_ref, carried_ref, glob_ref, grad_out_ref, *, heads_local, block
):
    weights = list(_attention_weights(
        init_ref, ptr_ref, soft_ref, win_ref, summ_ref, ask_ref, look_ref, tick=0, heads_local=heads_local, block=block
    ))
    grad = _pick_columns(ent_ref, grad_out_ref.shape[1])
    grad_out_ref[...] = grad
    value_cols = []
    for h, ab, ags in weights:
        cols = slice(h * CHANNEL_WIDTH, (h + 1) * CHANNEL_WIDTH)
        gh = grad[:, cols]
        band = jnp.dot(ab, gh, preferred_element_type=jnp.float32)
        own = prior_ref[0:block, cols].astype(jnp.float32) + band[0:block]
        value_cols.append(own.astype(jnp.bfloat16))
        carried_ref[:, cols] = prior_ref[block : 2 * block, cols].astype(jnp.float32) + band[block : 2 * block]
        for g, ag in enumerate(ags):
            glob_ref[g * block : (g + 1) * block, cols] = jnp.dot(ag, gh, preferred_element_type=jnp.float32)
    value_grad = value_cols[0] if len(value_cols) == 1 else jnp.concatenate(value_cols, axis=1)
    _partial_into(value_grad, w_ref, partial_ref)


def _last_tick_kernel(obj_ref, att_ref, carried_ref, w_ref, *rest, heads_local, block, groups, phases):
    pieces = rest[:groups]
    partial_ref, glob_ref, grad_out_ref = rest[groups:]
    band_rows = BAND * block
    arrived = pieces[0][...].astype(jnp.float32)
    for piece in pieces[1:]:
        arrived = arrived + piece[...].astype(jnp.float32)
    last = jnp.zeros((1, 1), jnp.int32) + (lax.axis_index("segment") == phases - 1).astype(jnp.int32)
    fresh = _pick_columns(obj_ref, grad_out_ref.shape[1])
    grad = jnp.where(last > 0, fresh, arrived.astype(jnp.bfloat16))
    grad_out_ref[...] = grad
    value_cols = []
    for h in range(heads_local):
        cols = slice(h * CHANNEL_WIDTH, (h + 1) * CHANNEL_WIDTH)
        gh = grad[:, cols]
        own = carried_ref[:, cols] + jnp.dot(att_ref[h, 0:block, :], gh, preferred_element_type=jnp.float32)
        value_cols.append(own.astype(jnp.bfloat16))
        for g in range(GLOB):
            lo = band_rows + g * block
            glob_ref[g * block : (g + 1) * block, cols] = jnp.dot(
                att_ref[h, lo : lo + block, :], gh, preferred_element_type=jnp.float32
            )
    value_grad = value_cols[0] if len(value_cols) == 1 else jnp.concatenate(value_cols, axis=1)
    _partial_into(value_grad, w_ref, partial_ref)


VMEM = pl.BlockSpec(memory_space=pltpu.VMEM)
KERNEL_PARAMS = pltpu.CompilerParams()


def first_tick(initial_segment, digest_pointer, softness, window_inputs, summary_blocks, asker, lookup, prior, weights, entering):
    block = summary_blocks.shape[1]
    local_width = asker.shape[1]
    heads_local = local_width // CHANNEL_WIDTH
    groups = weights.shape[0]
    keys_total = (BAND + GLOB) * block
    feat = window_inputs.shape[1]
    flops = 2 * feat * local_width * (block + keys_total) + 14 * keys_total * block * local_width + 4 * block * local_width * groups * local_width
    ins = [initial_segment, digest_pointer, softness, window_inputs, summary_blocks, asker, lookup, entering, prior, weights]
    return pl.pallas_call(
        functools.partial(_first_tick_kernel, heads_local=heads_local, block=block),
        out_shape=(
            jax.ShapeDtypeStruct((2, groups, block, local_width), jnp.bfloat16),
            jax.ShapeDtypeStruct((block, local_width), jnp.float32),
            jax.ShapeDtypeStruct((GLOB * block, local_width), jnp.float32),
            jax.ShapeDtypeStruct((block, local_width), entering.dtype),
        ),
        in_specs=[VMEM] * len(ins),
        out_specs=(VMEM, VMEM, VMEM, VMEM),
        compiler_params=KERNEL_PARAMS,
        cost_estimate=pl.CostEstimate(flops=flops, transcendentals=keys_total * block * heads_local, bytes_accessed=weights.size * 2 + 8 * block * local_width * 4),
    )(*ins)


def last_tick(att, carried, weights, objective, pieces, phases):
    heads_local, keys_total, block = att.shape
    local_width = carried.shape[1]
    groups = weights.shape[0]
    flops = 2 * keys_total * block * local_width + 4 * block * local_width * groups * local_width
    ins = [objective, att, carried, weights] + list(pieces)
    return pl.pallas_call(
        functools.partial(_last_tick_kernel, heads_local=heads_local, block=block, groups=len(pieces), phases=phases),
        out_shape=(
            jax.ShapeDtypeStruct((2, groups, block, local_width), jnp.bfloat16),
            jax.ShapeDtypeStruct((GLOB * block, local_width), jnp.float32),
            jax.ShapeDtypeStruct((block, local_width), objective.dtype),
        ),
        in_specs=[VMEM] * len(ins),
        out_specs=(VMEM, VMEM, VMEM),
        compiler_params=KERNEL_PARAMS,
        cost_estimate=pl.CostEstimate(flops=flops, transcendentals=0, bytes_accessed=weights.size * 2 + att.size * 2 + 8 * block * local_width * 4),
    )(*ins)


def attention_weights(tick, initial_segment, digest_pointer, softness, window_inputs, summary_blocks, asker, lookup):
    block = summary_blocks.shape[1]
    local_width = asker.shape[1]
    heads_local = local_width // CHANNEL_WIDTH
    keys_total = (BAND + GLOB) * block
    feat = window_inputs.shape[1]
    flops = 2 * feat * local_width * (block + keys_total) + 12 * keys_total * block * local_width
    ins = [initial_segment, digest_pointer, softness, window_inputs, summary_blocks, asker, lookup]
    return pl.pallas_call(
        functools.partial(_weights_kernel, tick=tick, heads_local=heads_local, block=block),
        out_shape=jax.ShapeDtypeStruct((heads_local, keys_total, block), jnp.bfloat16),
        in_specs=[VMEM] * len(ins),
        out_specs=VMEM,
        compiler_params=KERNEL_PARAMS,
        cost_estimate=pl.CostEstimate(flops=flops, transcendentals=keys_total * block * heads_local, bytes_accessed=keys_total * local_width * 2 + 4 * feat * local_width * 2),
    )(*ins)


def local(
    entering_deriv,
    objective_derivs,
    content_projection,
    asker_projection,
    lookup_projection,
    softness,
    window_inputs,
    digest_inputs,
    digest_pointer,
    initial_segment,
    prior_content_derivs,
):
    period_label = lax.axis_index("segment")
    phases = lax.axis_size("segment")
    head_group = lax.axis_index("head")
    heads = lax.axis_size("head")
    groups = heads // 2
    block_rows = entering_deriv.shape[0]
    local_width = content_projection.shape[1]
    summary_blocks = digest_inputs.reshape(SUMMARY, block_rows, digest_inputs.shape[1])
    weights = content_projection.reshape(groups, 2, local_width, local_width)
    summary_ids = jnp.arange(SUMMARY, dtype=jnp.int32)

    def live_of(tick_index):
        position = initial_segment[0] - period_label - tick_index
        return jnp.minimum(GLOB, 1 + GLOB * position // SEQ_BLOCKS)

    def digest_of(tick_index, glob):
        selector = (digest_pointer[tick_index][:, None] == summary_ids[None, :]).astype(jnp.float32)
        return jnp.sum(
            selector[:, :, None, None] * glob.reshape(GLOB, block_rows, local_width)[:, None], axis=0
        ).reshape(SUMMARY * block_rows, local_width)

    init = initial_segment.reshape(1, 1)
    partial0, carried, glob0, grad0 = first_tick(
        init, digest_pointer, softness, window_inputs, summary_blocks,
        asker_projection, lookup_projection, prior_content_derivs, weights, entering_deriv,
    )
    feats = (window_inputs, asker_projection, lookup_projection)
    halves = core_pair_sum(partial0)
    halves, feats = lax.optimization_barrier((halves, feats))
    later_att = attention_weights(
        1, init, digest_pointer, softness, feats[0], summary_blocks, feats[1], feats[2]
    )
    pieces = shift_down_sum(halves, grad0.astype(jnp.float32))
    digest_running = digest_of(0, glob0)
    partial1, glob1, grad1 = last_tick(
        later_att, carried, weights, objective_derivs[0:block_rows], pieces, phases
    )
    digest_running = digest_running + digest_of(1, glob1)
    summed = across_groups_sum(core_pair_sum(partial1))
    result = (grad1.astype(jnp.float32) + summed).astype(jnp.bfloat16)
    return (result, digest_running.astype(jnp.bfloat16))


def solution(mesh):
    in_specs = (
        P("segment", None),
        P(),
        P("segment", "head"),
        P("segment", "head"),
        P("segment", "head"),
        P("segment", "head"),
        P("segment", None),
        P(),
        P("segment", None),
        P(),
        P("segment", "head"),
    )
    out_specs = (P("segment", "head"), P("segment", "head"))
    return jax.shard_map(local, mesh=mesh, in_specs=in_specs, out_specs=out_specs, check_vma=False)
```

```python
import jax
import jax.numpy as jnp
from jax import lax
from jax.sharding import PartitionSpec as P
from jax.experimental import pallas as pl
from jax.experimental.pallas import tpu as pltpu
import functools

CHANNEL_WIDTH = 128
BAND = 4
GLOB = 2
SUMMARY = 2
SEQ_BLOCKS = 1024
TICKS = 2


EPS = 1e-06


def shifted(value, axis, steps):
    count = lax.axis_size(axis)
    first, last = (max(0, -steps), min(count, count - steps))
    return lax.ppermute(value, axis, [(source, source + steps) for source in range(first, last)])


def core_pair_sum(keep, send):
    heads = lax.axis_size("head")
    got = lax.ppermute(send, "head", [(h, h ^ 1) for h in range(heads)])
    return keep.astype(jnp.float32) + got.astype(jnp.float32)


def across_groups_sum(halves):
    head_group = lax.axis_index("head")
    heads = lax.axis_size("head")
    groups = heads // 2
    outer = head_group // 2
    total = lax.dynamic_index_in_dim(halves, outer, 0, keepdims=False)
    for step in range(1, groups):
        target = (outer + step) % groups
        piece = lax.dynamic_index_in_dim(halves, target, 0, keepdims=False).astype(jnp.bfloat16)
        pairs = [(h, (((h // 2) + step) % groups) * 2 + h % 2) for h in range(heads)]
        total = total + lax.ppermute(piece, "head", pairs).astype(jnp.float32)
    return total


def shift_down_sum(halves, entering):
    head_group = lax.axis_index("head")
    heads = lax.axis_size("head")
    segments = lax.axis_size("segment")
    groups = heads // 2
    outer = head_group // 2
    total = []
    for step in range(groups):
        target = (outer + step) % groups
        piece = lax.dynamic_index_in_dim(halves, target, 0, keepdims=False)
        if step == 0:
            piece = piece + entering
        pairs = []
        for s in range(1, segments):
            for h in range(heads):
                dest = (((h // 2) + step) % groups) * 2 + h % 2
                pairs.append((s * heads + h, (s - 1) * heads + dest))
        total.append(lax.ppermute(piece.astype(jnp.bfloat16), ("segment", "head"), pairs))
    return total


def row_norm(values):
    return values * lax.rsqrt(jnp.mean(values * values, axis=-1, keepdims=True) + EPS)


def _live_of(init_ref, tick):
    position = init_ref[...] - lax.axis_index("segment") - tick
    shift = SEQ_BLOCKS.bit_length() - 1
    return jnp.minimum(GLOB, 1 + lax.shift_right_arithmetic(GLOB * position, jnp.int32(shift)))


def _pick_columns(full_ref, width):
    head = jnp.zeros((1, 1), jnp.int32) + lax.axis_index("head")
    picked = full_ref[:, 0:width]
    for j in range(1, full_ref.shape[1] // width):
        picked = jnp.where(head == j, full_ref[:, j * width : (j + 1) * width], picked)
    return picked


def _attention_weights(init_ref, ptr_ref, soft_ref, win_ref, summ_ref, ask_ref, look_ref, *, tick, heads_local, block):
    band_rows = BAND * block
    live = _live_of(init_ref, tick)
    own = win_ref[tick * block : (tick + 1) * block, :]
    band = win_ref[tick * block : tick * block + band_rows, :]
    queries = jnp.dot(own, ask_ref[...], preferred_element_type=jnp.float32)
    band_keys = jnp.dot(band, look_ref[...], preferred_element_type=jnp.float32)
    summary_keys = [
        jnp.dot(summ_ref[m], look_ref[...], preferred_element_type=jnp.float32) for m in range(summ_ref.shape[0])
    ]
    glob_keys = []
    for g in range(GLOB):
        slot = ptr_ref[tick : tick + 1, g : g + 1]
        picked = summary_keys[0]
        for m in range(1, len(summary_keys)):
            picked = jnp.where(slot == m, summary_keys[m], picked)
        glob_keys.append(picked)
    key_ids = lax.broadcasted_iota(jnp.int32, (band_rows, block), 0)
    query_ids = lax.broadcasted_iota(jnp.int32, (band_rows, block), 1)
    band_open = (key_ids >= block) | (key_ids <= query_ids)
    contract = (((1,), (1,)), ((), ()))
    for h in range(heads_local):
        cols = slice(h * CHANNEL_WIDTH, (h + 1) * CHANNEL_WIDTH)
        scale = soft_ref[0:1, h : h + 1] * (1.0 / CHANNEL_WIDTH)
        qh = row_norm(queries[:, cols])
        kb = row_norm(band_keys[:, cols])
        sb = lax.dot_general(kb, qh, contract, precision=lax.Precision.HIGHEST, preferred_element_type=jnp.float32) * scale
        eb = jnp.where(band_open, jnp.exp(sb), 0.0)
        denom = jnp.sum(eb, axis=0, keepdims=True)
        eg = []
        for g in range(GLOB):
            kg = row_norm(glob_keys[g][:, cols])
            sg = lax.dot_general(kg, qh, contract, precision=lax.Precision.HIGHEST, preferred_element_type=jnp.float32) * scale
            e = jnp.where(live > g, jnp.exp(sg), 0.0)
            denom = denom + jnp.sum(e, axis=0, keepdims=True)
            eg.append(e)
        yield h, (eb / denom).astype(jnp.bfloat16), [(e / denom).astype(jnp.bfloat16) for e in eg]


def _weights_kernel(init_ref, ptr_ref, soft_ref, win_ref, summ_ref, ask_ref, look_ref, out_ref, *, tick, heads_local, block):
    band_rows = BAND * block
    for h, ab, ags in _attention_weights(
        init_ref, ptr_ref, soft_ref, win_ref, summ_ref, ask_ref, look_ref, tick=tick, heads_local=heads_local, block=block
    ):
        out_ref[h, 0:band_rows, :] = ab
        for g, ag in enumerate(ags):
            lo = band_rows + g * block
            out_ref[h, lo : lo + block, :] = ag


def _partial_into(value_grad, w_ref, keep_ref, send_ref):
    contract = (((1,), (1,)), ((), ()))
    core = jnp.zeros((1, 1), jnp.int32) + lax.axis_index("head") % 2
    for g in range(w_ref.shape[0]):
        even, odd = [
            lax.dot_general(value_grad, w_ref[g, p], contract, preferred_element_type=jnp.float32).astype(keep_ref.dtype)
            for p in range(2)
        ]
        keep_ref[g] = jnp.where(core == 0, even, odd)
        send_ref[g] = jnp.where(core == 0, odd, even)


def _first_tick_kernel(
    init_ref, ptr_ref, soft_ref, win_ref, summ_ref, ask_ref, look_ref, ent_ref, prior_ref, w_hbm,
    keep_ref, send_ref, carried_ref, glob_ref, grad_out_ref, w_ref, w_sem, *, heads_local, block
):
    w_copy = pltpu.make_async_copy(w_hbm, w_ref, w_sem)
    w_copy.start()
    weights = list(_attention_weights(
        init_ref, ptr_ref, soft_ref, win_ref, summ_ref, ask_ref, look_ref, tick=0, heads_local=heads_local, block=block
    ))
    grad = _pick_columns(ent_ref, grad_out_ref.shape[1])
    grad_out_ref[...] = grad
    value_cols = []
    for h, ab, ags in weights:
        cols = slice(h * CHANNEL_WIDTH, (h + 1) * CHANNEL_WIDTH)
        gh = grad[:, cols]
        band = jnp.dot(ab, gh, preferred_element_type=jnp.float32)
        own = prior_ref[0:block, cols].astype(jnp.float32) + band[0:block]
        value_cols.append(own.astype(jnp.bfloat16))
        carried_ref[:, cols] = prior_ref[block : 2 * block, cols].astype(jnp.float32) + band[block : 2 * block]
        for g, ag in enumerate(ags):
            glob_ref[g * block : (g + 1) * block, cols] = jnp.dot(ag, gh, preferred_element_type=jnp.float32)
    value_grad = value_cols[0] if len(value_cols) == 1 else jnp.concatenate(value_cols, axis=1)
    w_copy.wait()
    _partial_into(value_grad, w_ref, keep_ref, send_ref)


def _last_tick_kernel(obj_ref, att_ref, carried_ref, w_hbm, *rest, heads_local, block, groups, phases):
    pieces = rest[:groups]
    keep_ref, send_ref, glob_ref, grad_out_ref, w_ref, w_sem = rest[groups:]
    w_copy = pltpu.make_async_copy(w_hbm, w_ref, w_sem)
    w_copy.start()
    band_rows = BAND * block
    arrived = pieces[0][...].astype(jnp.float32)
    for piece in pieces[1:]:
        arrived = arrived + piece[...].astype(jnp.float32)
    last = jnp.zeros((1, 1), jnp.int32) + (lax.axis_index("segment") == phases - 1).astype(jnp.int32)
    fresh = _pick_columns(obj_ref, grad_out_ref.shape[1])
    grad = jnp.where(last > 0, fresh, arrived.astype(jnp.bfloat16))
    grad_out_ref[...] = grad
    value_cols = []
    for h in range(heads_local):
        cols = slice(h * CHANNEL_WIDTH, (h + 1) * CHANNEL_WIDTH)
        gh = grad[:, cols]
        own = carried_ref[:, cols] + jnp.dot(att_ref[h, 0:block, :], gh, preferred_element_type=jnp.float32)
        value_cols.append(own.astype(jnp.bfloat16))
        for g in range(GLOB):
            lo = band_rows + g * block
            glob_ref[g * block : (g + 1) * block, cols] = jnp.dot(
                att_ref[h, lo : lo + block, :], gh, preferred_element_type=jnp.float32
            )
    value_grad = value_cols[0] if len(value_cols) == 1 else jnp.concatenate(value_cols, axis=1)
    w_copy.wait()
    _partial_into(value_grad, w_ref, keep_ref, send_ref)


ANY = pl.BlockSpec(memory_space=pl.ANY)
VMEM = pl.BlockSpec(memory_space=pltpu.VMEM)
KERNEL_PARAMS = pltpu.CompilerParams()


def first_tick(initial_segment, digest_pointer, softness, window_inputs, summary_blocks, asker, lookup, prior, weights, entering):
    block = summary_blocks.shape[1]
    local_width = asker.shape[1]
    heads_local = local_width // CHANNEL_WIDTH
    groups = weights.shape[0]
    keys_total = (BAND + GLOB) * block
    feat = window_inputs.shape[1]
    flops = 2 * feat * local_width * (block + keys_total) + 14 * keys_total * block * local_width + 4 * block * local_width * groups * local_width
    ins = [initial_segment, digest_pointer, softness, window_inputs, summary_blocks, asker, lookup, entering, prior, weights]
    return pl.pallas_call(
        functools.partial(_first_tick_kernel, heads_local=heads_local, block=block),
        out_shape=(
            jax.ShapeDtypeStruct((groups, block, local_width), jnp.bfloat16),
            jax.ShapeDtypeStruct((groups, block, local_width), jnp.bfloat16),
            jax.ShapeDtypeStruct((block, local_width), jnp.float32),
            jax.ShapeDtypeStruct((GLOB * block, local_width), jnp.float32),
            jax.ShapeDtypeStruct((block, local_width), entering.dtype),
        ),
        in_specs=[VMEM] * (len(ins) - 1) + [ANY],
        out_specs=(VMEM, VMEM, VMEM, VMEM, VMEM),
        scratch_shapes=[pltpu.VMEM(weights.shape, weights.dtype), pltpu.SemaphoreType.DMA(())],
        compiler_params=KERNEL_PARAMS,
        cost_estimate=pl.CostEstimate(flops=flops, transcendentals=keys_total * block * heads_local, bytes_accessed=weights.size * 2 + 8 * block * local_width * 4),
    )(*ins)


def last_tick(att, carried, weights, objective, pieces, phases):
    heads_local, keys_total, block = att.shape
    local_width = carried.shape[1]
    groups = weights.shape[0]
    flops = 2 * keys_total * block * local_width + 4 * block * local_width * groups * local_width
    ins = [objective, att, carried, weights] + list(pieces)
    return pl.pallas_call(
        functools.partial(_last_tick_kernel, heads_local=heads_local, block=block, groups=len(pieces), phases=phases),
        out_shape=(
            jax.ShapeDtypeStruct((groups, block, local_width), jnp.bfloat16),
            jax.ShapeDtypeStruct((groups, block, local_width), jnp.bfloat16),
            jax.ShapeDtypeStruct((GLOB * block, local_width), jnp.float32),
            jax.ShapeDtypeStruct((block, local_width), objective.dtype),
        ),
        in_specs=[VMEM, VMEM, VMEM, ANY] + [VMEM] * len(pieces),
        out_specs=(VMEM, VMEM, VMEM, VMEM),
        scratch_shapes=[pltpu.VMEM(weights.shape, weights.dtype), pltpu.SemaphoreType.DMA(())],
        compiler_params=KERNEL_PARAMS,
        cost_estimate=pl.CostEstimate(flops=flops, transcendentals=0, bytes_accessed=weights.size * 2 + att.size * 2 + 8 * block * local_width * 4),
    )(*ins)


def attention_weights(tick, initial_segment, digest_pointer, softness, window_inputs, summary_blocks, asker, lookup):
    block = summary_blocks.shape[1]
    local_width = asker.shape[1]
    heads_local = local_width // CHANNEL_WIDTH
    keys_total = (BAND + GLOB) * block
    feat = window_inputs.shape[1]
    flops = 2 * feat * local_width * (block + keys_total) + 12 * keys_total * block * local_width
    ins = [initial_segment, digest_pointer, softness, window_inputs, summary_blocks, asker, lookup]
    return pl.pallas_call(
        functools.partial(_weights_kernel, tick=tick, heads_local=heads_local, block=block),
        out_shape=jax.ShapeDtypeStruct((heads_local, keys_total, block), jnp.bfloat16),
        in_specs=[VMEM] * len(ins),
        out_specs=VMEM,
        compiler_params=KERNEL_PARAMS,
        cost_estimate=pl.CostEstimate(flops=flops, transcendentals=keys_total * block * heads_local, bytes_accessed=keys_total * local_width * 2 + 4 * feat * local_width * 2),
    )(*ins)


def local(
    entering_deriv,
    objective_derivs,
    content_projection,
    asker_projection,
    lookup_projection,
    softness,
    window_inputs,
    digest_inputs,
    digest_pointer,
    initial_segment,
    prior_content_derivs,
):
    period_label = lax.axis_index("segment")
    phases = lax.axis_size("segment")
    head_group = lax.axis_index("head")
    heads = lax.axis_size("head")
    groups = heads // 2
    block_rows = entering_deriv.shape[0]
    local_width = content_projection.shape[1]
    summary_blocks = digest_inputs.reshape(SUMMARY, block_rows, digest_inputs.shape[1])
    weights = content_projection.reshape(groups, 2, local_width, local_width)
    summary_ids = jnp.arange(SUMMARY, dtype=jnp.int32)

    def live_of(tick_index):
        position = initial_segment[0] - period_label - tick_index
        return jnp.minimum(GLOB, 1 + GLOB * position // SEQ_BLOCKS)

    def digest_of(tick_index, glob):
        selector = (digest_pointer[tick_index][:, None] == summary_ids[None, :]).astype(jnp.float32)
        return jnp.sum(
            selector[:, :, None, None] * glob.reshape(GLOB, block_rows, local_width)[:, None], axis=0
        ).reshape(SUMMARY * block_rows, local_width)

    init = initial_segment.reshape(1, 1)
    keep0, send0, carried, glob0, grad0 = first_tick(
        init, digest_pointer, softness, window_inputs, summary_blocks,
        asker_projection, lookup_projection, prior_content_derivs, weights, entering_deriv,
    )
    feats = (window_inputs, asker_projection, lookup_projection)
    halves = core_pair_sum(keep0, send0)
    halves, feats = lax.optimization_barrier((halves, feats))
    later_att = attention_weights(
        1, init, digest_pointer, softness, feats[0], summary_blocks, feats[1], feats[2]
    )
    pieces = shift_down_sum(halves, grad0.astype(jnp.float32))
    digest_running = digest_of(0, glob0)
    keep1, send1, glob1, grad1 = last_tick(
        later_att, carried, weights, objective_derivs[0:block_rows], pieces, phases
    )
    digest_running = digest_running + digest_of(1, glob1)
    summed = across_groups_sum(core_pair_sum(keep1, send1))
    result = (grad1.astype(jnp.float32) + summed).astype(jnp.bfloat16)
    return (result, digest_running.astype(jnp.bfloat16))


def solution(mesh):
    in_specs = (
        P("segment", None),
        P(),
        P("segment", "head"),
        P("segment", "head"),
        P("segment", "head"),
        P("segment", "head"),
        P("segment", None),
        P(),
        P("segment", None),
        P(),
        P("segment", "head"),
    )
    out_specs = (P("segment", "head"), P("segment", "head"))
    return jax.shard_map(local, mesh=mesh, in_specs=in_specs, out_specs=out_specs, check_vma=False)
```

```python
import jax
import jax.numpy as jnp
from jax import lax
from jax.sharding import PartitionSpec as P
from jax.experimental import pallas as pl
from jax.experimental.pallas import tpu as pltpu
import functools

CHANNEL_WIDTH = 128
BAND = 4
GLOB = 2
SUMMARY = 2
SEQ_BLOCKS = 1024
TICKS = 2
SEND_PARTS = 2


EPS = 1e-06


def shifted(value, axis, steps):
    count = lax.axis_size(axis)
    first, last = (max(0, -steps), min(count, count - steps))
    return lax.ppermute(value, axis, [(source, source + steps) for source in range(first, last)])


def core_pair_sum(keep, send):
    heads = lax.axis_size("head")
    got = lax.ppermute(send, "head", [(h, h ^ 1) for h in range(heads)])
    return keep.astype(jnp.float32) + got.astype(jnp.float32)


def across_groups_sum(halves):
    head_group = lax.axis_index("head")
    heads = lax.axis_size("head")
    groups = heads // 2
    outer = head_group // 2
    total = lax.dynamic_index_in_dim(halves, outer, 0, keepdims=False)
    for step in range(1, groups):
        target = (outer + step) % groups
        piece = lax.dynamic_index_in_dim(halves, target, 0, keepdims=False).astype(jnp.bfloat16)
        pairs = [(h, (((h // 2) + step) % groups) * 2 + h % 2) for h in range(heads)]
        total = total + lax.ppermute(piece, "head", pairs).astype(jnp.float32)
    return total


def shift_down_sum(halves, entering):
    head_group = lax.axis_index("head")
    heads = lax.axis_size("head")
    segments = lax.axis_size("segment")
    groups = heads // 2
    outer = head_group // 2
    total = []
    for step in range(groups):
        target = (outer + step) % groups
        piece = lax.dynamic_index_in_dim(halves, target, 0, keepdims=False)
        if step == 0:
            piece = piece + entering
        pairs = []
        for s in range(1, segments):
            for h in range(heads):
                dest = (((h // 2) + step) % groups) * 2 + h % 2
                pairs.append((s * heads + h, (s - 1) * heads + dest))
        piece = piece.astype(jnp.bfloat16)
        rows = piece.shape[0] // SEND_PARTS
        for r in range(SEND_PARTS):
            total.append(lax.ppermute(piece[r * rows : (r + 1) * rows], ("segment", "head"), pairs))
    return total


def row_norm(values):
    return values * lax.rsqrt(jnp.mean(values * values, axis=-1, keepdims=True) + EPS)


def _live_of(init_ref, tick):
    position = init_ref[...] - lax.axis_index("segment") - tick
    shift = SEQ_BLOCKS.bit_length() - 1
    return jnp.minimum(GLOB, 1 + lax.shift_right_arithmetic(GLOB * position, jnp.int32(shift)))


def _pick_columns(full_ref, width):
    head = jnp.zeros((1, 1), jnp.int32) + lax.axis_index("head")
    picked = full_ref[:, 0:width]
    for j in range(1, full_ref.shape[1] // width):
        picked = jnp.where(head == j, full_ref[:, j * width : (j + 1) * width], picked)
    return picked


def _attention_weights(init_ref, ptr_ref, soft_ref, win_ref, summ_ref, ask_ref, look_ref, *, tick, heads_local, block):
    band_rows = BAND * block
    live = _live_of(init_ref, tick)
    own = win_ref[tick * block : (tick + 1) * block, :]
    band = win_ref[tick * block : tick * block + band_rows, :]
    queries = jnp.dot(own, ask_ref[...], preferred_element_type=jnp.float32)
    band_keys = jnp.dot(band, look_ref[...], preferred_element_type=jnp.float32)
    summary_keys = [
        jnp.dot(summ_ref[m], look_ref[...], preferred_element_type=jnp.float32) for m in range(summ_ref.shape[0])
    ]
    glob_keys = []
    for g in range(GLOB):
        slot = ptr_ref[tick : tick + 1, g : g + 1]
        picked = summary_keys[0]
        for m in range(1, len(summary_keys)):
            picked = jnp.where(slot == m, summary_keys[m], picked)
        glob_keys.append(picked)
    key_ids = lax.broadcasted_iota(jnp.int32, (band_rows, block), 0)
    query_ids = lax.broadcasted_iota(jnp.int32, (band_rows, block), 1)
    band_open = (key_ids >= block) | (key_ids <= query_ids)
    contract = (((1,), (1,)), ((), ()))
    for h in range(heads_local):
        cols = slice(h * CHANNEL_WIDTH, (h + 1) * CHANNEL_WIDTH)
        scale = soft_ref[0:1, h : h + 1] * (1.0 / CHANNEL_WIDTH)
        qh = row_norm(queries[:, cols])
        kb = row_norm(band_keys[:, cols])
        sb = lax.dot_general(kb, qh, contract, precision=lax.Precision.HIGHEST, preferred_element_type=jnp.float32) * scale
        eb = jnp.where(band_open, jnp.exp(sb), 0.0)
        denom = jnp.sum(eb, axis=0, keepdims=True)
        eg = []
        for g in range(GLOB):
            kg = row_norm(glob_keys[g][:, cols])
            sg = lax.dot_general(kg, qh, contract, precision=lax.Precision.HIGHEST, preferred_element_type=jnp.float32) * scale
            e = jnp.where(live > g, jnp.exp(sg), 0.0)
            denom = denom + jnp.sum(e, axis=0, keepdims=True)
            eg.append(e)
        yield h, (eb / denom).astype(jnp.bfloat16), [(e / denom).astype(jnp.bfloat16) for e in eg]


def _weights_kernel(init_ref, ptr_ref, soft_ref, win_ref, summ_ref, ask_ref, look_ref, out_ref, *, tick, heads_local, block):
    band_rows = BAND * block
    for h, ab, ags in _attention_weights(
        init_ref, ptr_ref, soft_ref, win_ref, summ_ref, ask_ref, look_ref, tick=tick, heads_local=heads_local, block=block
    ):
        out_ref[h, 0:band_rows, :] = ab
        for g, ag in enumerate(ags):
            lo = band_rows + g * block
            out_ref[h, lo : lo + block, :] = ag


def _partial_into(value_grad, w_ref, keep_ref, send_ref):
    contract = (((1,), (1,)), ((), ()))
    core = jnp.zeros((1, 1), jnp.int32) + lax.axis_index("head") % 2
    for g in range(w_ref.shape[0]):
        even, odd = [
            lax.dot_general(value_grad, w_ref[g, p], contract, preferred_element_type=jnp.float32).astype(keep_ref.dtype)
            for p in range(2)
        ]
        keep_ref[g] = jnp.where(core == 0, even, odd)
        send_ref[g] = jnp.where(core == 0, odd, even)


def _first_tick_kernel(
    init_ref, ptr_ref, soft_ref, win_ref, summ_ref, ask_ref, look_ref, ent_ref, prior_ref, w_hbm,
    keep_ref, send_ref, carried_ref, glob_ref, grad_out_ref, w_ref, w_sem, *, heads_local, block
):
    w_copy = pltpu.make_async_copy(w_hbm, w_ref, w_sem)
    w_copy.start()
    weights = list(_attention_weights(
        init_ref, ptr_ref, soft_ref, win_ref, summ_ref, ask_ref, look_ref, tick=0, heads_local=heads_local, block=block
    ))
    grad = _pick_columns(ent_ref, grad_out_ref.shape[1])
    grad_out_ref[...] = grad
    value_cols = []
    for h, ab, ags in weights:
        cols = slice(h * CHANNEL_WIDTH, (h + 1) * CHANNEL_WIDTH)
        gh = grad[:, cols]
        band = jnp.dot(ab, gh, preferred_element_type=jnp.float32)
        own = prior_ref[0:block, cols].astype(jnp.float32) + band[0:block]
        value_cols.append(own.astype(jnp.bfloat16))
        carried_ref[:, cols] = prior_ref[block : 2 * block, cols].astype(jnp.float32) + band[block : 2 * block]
        for g, ag in enumerate(ags):
            glob_ref[g * block : (g + 1) * block, cols] = jnp.dot(ag, gh, preferred_element_type=jnp.float32)
    value_grad = value_cols[0] if len(value_cols) == 1 else jnp.concatenate(value_cols, axis=1)
    w_copy.wait()
    _partial_into(value_grad, w_ref, keep_ref, send_ref)


def _last_tick_kernel(obj_ref, att_ref, carried_ref, w_hbm, *rest, heads_local, block, groups, phases):
    pieces = rest[:groups]
    keep_ref, send_ref, glob_ref, grad_out_ref, w_ref, w_sem = rest[groups:]
    w_copy = pltpu.make_async_copy(w_hbm, w_ref, w_sem)
    w_copy.start()
    band_rows = BAND * block
    parts = []
    for r in range(SEND_PARTS):
        part = pieces[r][...].astype(jnp.float32)
        for step in range(1, groups // SEND_PARTS):
            part = part + pieces[step * SEND_PARTS + r][...].astype(jnp.float32)
        parts.append(part)
    arrived = parts[0] if SEND_PARTS == 1 else jnp.concatenate(parts, axis=0)
    last = jnp.zeros((1, 1), jnp.int32) + (lax.axis_index("segment") == phases - 1).astype(jnp.int32)
    fresh = _pick_columns(obj_ref, grad_out_ref.shape[1])
    grad = jnp.where(last > 0, fresh, arrived.astype(jnp.bfloat16))
    grad_out_ref[...] = grad
    value_cols = []
    for h in range(heads_local):
        cols = slice(h * CHANNEL_WIDTH, (h + 1) * CHANNEL_WIDTH)
        gh = grad[:, cols]
        own = carried_ref[:, cols] + jnp.dot(att_ref[h, 0:block, :], gh, preferred_element_type=jnp.float32)
        value_cols.append(own.astype(jnp.bfloat16))
        for g in range(GLOB):
            lo = band_rows + g * block
            glob_ref[g * block : (g + 1) * block, cols] = jnp.dot(
                att_ref[h, lo : lo + block, :], gh, preferred_element_type=jnp.float32
            )
    value_grad = value_cols[0] if len(value_cols) == 1 else jnp.concatenate(value_cols, axis=1)
    w_copy.wait()
    _partial_into(value_grad, w_ref, keep_ref, send_ref)


ANY = pl.BlockSpec(memory_space=pl.ANY)
VMEM = pl.BlockSpec(memory_space=pltpu.VMEM)
KERNEL_PARAMS = pltpu.CompilerParams()


def first_tick(initial_segment, digest_pointer, softness, window_inputs, summary_blocks, asker, lookup, prior, weights, entering):
    block = summary_blocks.shape[1]
    local_width = asker.shape[1]
    heads_local = local_width // CHANNEL_WIDTH
    groups = weights.shape[0]
    keys_total = (BAND + GLOB) * block
    feat = window_inputs.shape[1]
    flops = 2 * feat * local_width * (block + keys_total) + 14 * keys_total * block * local_width + 4 * block * local_width * groups * local_width
    ins = [initial_segment, digest_pointer, softness, window_inputs, summary_blocks, asker, lookup, entering, prior, weights]
    return pl.pallas_call(
        functools.partial(_first_tick_kernel, heads_local=heads_local, block=block),
        out_shape=(
            jax.ShapeDtypeStruct((groups, block, local_width), jnp.bfloat16),
            jax.ShapeDtypeStruct((groups, block, local_width), jnp.bfloat16),
            jax.ShapeDtypeStruct((block, local_width), jnp.float32),
            jax.ShapeDtypeStruct((GLOB * block, local_width), jnp.float32),
            jax.ShapeDtypeStruct((block, local_width), entering.dtype),
        ),
        in_specs=[VMEM] * (len(ins) - 1) + [ANY],
        out_specs=(VMEM, VMEM, VMEM, VMEM, VMEM),
        scratch_shapes=[pltpu.VMEM(weights.shape, weights.dtype), pltpu.SemaphoreType.DMA(())],
        compiler_params=KERNEL_PARAMS,
        cost_estimate=pl.CostEstimate(flops=flops, transcendentals=keys_total * block * heads_local, bytes_accessed=weights.size * 2 + 8 * block * local_width * 4),
    )(*ins)


def last_tick(att, carried, weights, objective, pieces, phases):
    heads_local, keys_total, block = att.shape
    local_width = carried.shape[1]
    groups = weights.shape[0]
    flops = 2 * keys_total * block * local_width + 4 * block * local_width * groups * local_width
    ins = [objective, att, carried, weights] + list(pieces)
    return pl.pallas_call(
        functools.partial(_last_tick_kernel, heads_local=heads_local, block=block, groups=len(pieces), phases=phases),
        out_shape=(
            jax.ShapeDtypeStruct((groups, block, local_width), jnp.bfloat16),
            jax.ShapeDtypeStruct((groups, block, local_width), jnp.bfloat16),
            jax.ShapeDtypeStruct((GLOB * block, local_width), jnp.float32),
            jax.ShapeDtypeStruct((block, local_width), objective.dtype),
        ),
        in_specs=[VMEM, VMEM, VMEM, ANY] + [VMEM] * len(pieces),
        out_specs=(VMEM, VMEM, VMEM, VMEM),
        scratch_shapes=[pltpu.VMEM(weights.shape, weights.dtype), pltpu.SemaphoreType.DMA(())],
        compiler_params=KERNEL_PARAMS,
        cost_estimate=pl.CostEstimate(flops=flops, transcendentals=0, bytes_accessed=weights.size * 2 + att.size * 2 + 8 * block * local_width * 4),
    )(*ins)


def attention_weights(tick, initial_segment, digest_pointer, softness, window_inputs, summary_blocks, asker, lookup):
    block = summary_blocks.shape[1]
    local_width = asker.shape[1]
    heads_local = local_width // CHANNEL_WIDTH
    keys_total = (BAND + GLOB) * block
    feat = window_inputs.shape[1]
    flops = 2 * feat * local_width * (block + keys_total) + 12 * keys_total * block * local_width
    ins = [initial_segment, digest_pointer, softness, window_inputs, summary_blocks, asker, lookup]
    return pl.pallas_call(
        functools.partial(_weights_kernel, tick=tick, heads_local=heads_local, block=block),
        out_shape=jax.ShapeDtypeStruct((heads_local, keys_total, block), jnp.bfloat16),
        in_specs=[VMEM] * len(ins),
        out_specs=VMEM,
        compiler_params=KERNEL_PARAMS,
        cost_estimate=pl.CostEstimate(flops=flops, transcendentals=keys_total * block * heads_local, bytes_accessed=keys_total * local_width * 2 + 4 * feat * local_width * 2),
    )(*ins)


def local(
    entering_deriv,
    objective_derivs,
    content_projection,
    asker_projection,
    lookup_projection,
    softness,
    window_inputs,
    digest_inputs,
    digest_pointer,
    initial_segment,
    prior_content_derivs,
):
    period_label = lax.axis_index("segment")
    phases = lax.axis_size("segment")
    head_group = lax.axis_index("head")
    heads = lax.axis_size("head")
    groups = heads // 2
    block_rows = entering_deriv.shape[0]
    local_width = content_projection.shape[1]
    summary_blocks = digest_inputs.reshape(SUMMARY, block_rows, digest_inputs.shape[1])
    weights = content_projection.reshape(groups, 2, local_width, local_width)
    summary_ids = jnp.arange(SUMMARY, dtype=jnp.int32)

    def live_of(tick_index):
        position = initial_segment[0] - period_label - tick_index
        return jnp.minimum(GLOB, 1 + GLOB * position // SEQ_BLOCKS)

    def digest_of(tick_index, glob):
        selector = (digest_pointer[tick_index][:, None] == summary_ids[None, :]).astype(jnp.float32)
        return jnp.sum(
            selector[:, :, None, None] * glob.reshape(GLOB, block_rows, local_width)[:, None], axis=0
        ).reshape(SUMMARY * block_rows, local_width)

    init = initial_segment.reshape(1, 1)
    keep0, send0, carried, glob0, grad0 = first_tick(
        init, digest_pointer, softness, window_inputs, summary_blocks,
        asker_projection, lookup_projection, prior_content_derivs, weights, entering_deriv,
    )
    feats = (window_inputs, asker_projection, lookup_projection)
    halves = core_pair_sum(keep0, send0)
    halves, feats = lax.optimization_barrier((halves, feats))
    later_att = attention_weights(
        1, init, digest_pointer, softness, feats[0], summary_blocks, feats[1], feats[2]
    )
    pieces = shift_down_sum(halves, grad0.astype(jnp.float32))
    digest_running = digest_of(0, glob0)
    keep1, send1, glob1, grad1 = last_tick(
        later_att, carried, weights, objective_derivs[0:block_rows], pieces, phases
    )
    digest_running = digest_running + digest_of(1, glob1)
    summed = across_groups_sum(core_pair_sum(keep1, send1))
    result = (grad1.astype(jnp.float32) + summed).astype(jnp.bfloat16)
    return (result, digest_running.astype(jnp.bfloat16))


def solution(mesh):
    in_specs = (
        P("segment", None),
        P(),
        P("segment", "head"),
        P("segment", "head"),
        P("segment", "head"),
        P("segment", "head"),
        P("segment", None),
        P(),
        P("segment", None),
        P(),
        P("segment", "head"),
    )
    out_specs = (P("segment", "head"), P("segment", "head"))
    return jax.shard_map(local, mesh=mesh, in_specs=in_specs, out_specs=out_specs, check_vma=False)
```

```python
import jax
import jax.numpy as jnp
from jax import lax
from jax.sharding import PartitionSpec as P
from jax.experimental import pallas as pl
from jax.experimental.pallas import tpu as pltpu
import functools

CHANNEL_WIDTH = 128
BAND = 4
GLOB = 2
SUMMARY = 2
SEQ_BLOCKS = 1024
TICKS = 2
SEND_PARTS = 2


EPS = 1e-06


def shifted(value, axis, steps):
    count = lax.axis_size(axis)
    first, last = (max(0, -steps), min(count, count - steps))
    return lax.ppermute(value, axis, [(source, source + steps) for source in range(first, last)])


def core_pair_sum(keep, send):
    heads = lax.axis_size("head")
    got = lax.ppermute(send, "head", [(h, h ^ 1) for h in range(heads)])
    return keep.astype(jnp.float32) + got.astype(jnp.float32)


def across_groups_sum(halves):
    head_group = lax.axis_index("head")
    heads = lax.axis_size("head")
    groups = heads // 2
    outer = head_group // 2
    total = lax.dynamic_index_in_dim(halves, outer, 0, keepdims=False)
    for step in range(1, groups):
        target = (outer + step) % groups
        piece = lax.dynamic_index_in_dim(halves, target, 0, keepdims=False).astype(jnp.bfloat16)
        pairs = [(h, (((h // 2) + step) % groups) * 2 + h % 2) for h in range(heads)]
        total = total + lax.ppermute(piece, "head", pairs).astype(jnp.float32)
    return total


def shift_down_sum(halves, entering, side_work):
    heads = lax.axis_size("head")
    segments = lax.axis_size("segment")
    rows = halves.shape[1] // SEND_PARTS
    pairs = [(s * heads + h, (s - 1) * heads + h) for s in range(1, segments) for h in range(heads)]
    sent = []
    fillers = []
    previous = halves
    for r in range(SEND_PARTS):
        chunk = halves[:, r * rows : (r + 1) * rows]
        if r > 0:
            chunk, _ = lax.optimization_barrier((chunk, previous))
        if r < len(side_work):
            _, held = lax.optimization_barrier((previous, side_work[r][1]))
            fillers.append(side_work[r][0](held))
        reduced = across_groups_sum(chunk) + entering[r * rows : (r + 1) * rows]
        previous = reduced
        sent.append(lax.ppermute(reduced.astype(jnp.bfloat16), ("segment", "head"), pairs))
    for work, operands in side_work[SEND_PARTS:]:
        fillers.append(work(operands))
    return sent, fillers
def row_norm(values):
    return values * lax.rsqrt(jnp.mean(values * values, axis=-1, keepdims=True) + EPS)


def _live_of(init_ref, tick):
    position = init_ref[...] - lax.axis_index("segment") - tick
    shift = SEQ_BLOCKS.bit_length() - 1
    return jnp.minimum(GLOB, 1 + lax.shift_right_arithmetic(GLOB * position, jnp.int32(shift)))


def _pick_columns(full_ref, width):
    head = jnp.zeros((1, 1), jnp.int32) + lax.axis_index("head")
    picked = full_ref[:, 0:width]
    for j in range(1, full_ref.shape[1] // width):
        picked = jnp.where(head == j, full_ref[:, j * width : (j + 1) * width], picked)
    return picked


def _attention_weights(init_ref, ptr_ref, soft_ref, win_ref, summ_ref, ask_ref, look_ref, *, tick, heads, block):
    band_rows = BAND * block
    live = _live_of(init_ref, tick)
    own = win_ref[tick * block : (tick + 1) * block, :]
    band = win_ref[tick * block : tick * block + band_rows, :]
    queries = jnp.dot(own, ask_ref[...], preferred_element_type=jnp.float32)
    band_keys = jnp.dot(band, look_ref[...], preferred_element_type=jnp.float32)
    summary_keys = [
        jnp.dot(summ_ref[m], look_ref[...], preferred_element_type=jnp.float32) for m in range(summ_ref.shape[0])
    ]
    glob_keys = []
    for g in range(GLOB):
        slot = ptr_ref[tick : tick + 1, g : g + 1]
        picked = summary_keys[0]
        for m in range(1, len(summary_keys)):
            picked = jnp.where(slot == m, summary_keys[m], picked)
        glob_keys.append(picked)
    key_ids = lax.broadcasted_iota(jnp.int32, (band_rows, block), 0)
    query_ids = lax.broadcasted_iota(jnp.int32, (band_rows, block), 1)
    band_open = (key_ids >= block) | (key_ids <= query_ids)
    contract = (((1,), (1,)), ((), ()))
    for h in heads:
        cols = slice(h * CHANNEL_WIDTH, (h + 1) * CHANNEL_WIDTH)
        scale = soft_ref[0:1, h : h + 1] * (1.0 / CHANNEL_WIDTH)
        qh = row_norm(queries[:, cols])
        kb = row_norm(band_keys[:, cols])
        sb = lax.dot_general(kb, qh, contract, precision=lax.Precision.HIGHEST, preferred_element_type=jnp.float32) * scale
        eb = jnp.where(band_open, jnp.exp(sb), 0.0)
        denom = jnp.sum(eb, axis=0, keepdims=True)
        eg = []
        for g in range(GLOB):
            kg = row_norm(glob_keys[g][:, cols])
            sg = lax.dot_general(kg, qh, contract, precision=lax.Precision.HIGHEST, preferred_element_type=jnp.float32) * scale
            e = jnp.where(live > g, jnp.exp(sg), 0.0)
            denom = denom + jnp.sum(e, axis=0, keepdims=True)
            eg.append(e)
        yield h, (eb / denom).astype(jnp.bfloat16), [(e / denom).astype(jnp.bfloat16) for e in eg]


def _weights_kernel(init_ref, ptr_ref, soft_ref, win_ref, summ_ref, ask_ref, look_ref, out_ref, *, tick, heads, block):
    band_rows = BAND * block
    for h, ab, ags in _attention_weights(
        init_ref, ptr_ref, soft_ref, win_ref, summ_ref, ask_ref, look_ref, tick=tick, heads=heads, block=block
    ):
        i = h - heads[0]
        out_ref[i, 0:band_rows, :] = ab
        for g, ag in enumerate(ags):
            lo = band_rows + g * block
            out_ref[i, lo : lo + block, :] = ag


def _partial_into(value_grad, w_ref, keep_ref, send_ref):
    contract = (((1,), (1,)), ((), ()))
    core = jnp.zeros((1, 1), jnp.int32) + lax.axis_index("head") % 2
    for g in range(w_ref.shape[0]):
        even, odd = [
            lax.dot_general(value_grad, w_ref[g, p], contract, preferred_element_type=jnp.float32).astype(keep_ref.dtype)
            for p in range(2)
        ]
        keep_ref[g] = jnp.where(core == 0, even, odd)
        send_ref[g] = jnp.where(core == 0, odd, even)


def _first_tick_kernel(
    init_ref, ptr_ref, soft_ref, win_ref, summ_ref, ask_ref, look_ref, ent_ref, prior_ref, w_hbm,
    keep_ref, send_ref, carried_ref, glob_ref, grad_out_ref, w_ref, w_sem, *, heads_local, block
):
    w_copy = pltpu.make_async_copy(w_hbm, w_ref, w_sem)
    w_copy.start()
    weights = list(_attention_weights(
        init_ref, ptr_ref, soft_ref, win_ref, summ_ref, ask_ref, look_ref, tick=0, heads=range(heads_local), block=block
    ))
    grad = _pick_columns(ent_ref, grad_out_ref.shape[1])
    grad_out_ref[...] = grad
    value_cols = []
    for h, ab, ags in weights:
        cols = slice(h * CHANNEL_WIDTH, (h + 1) * CHANNEL_WIDTH)
        gh = grad[:, cols]
        band = jnp.dot(ab, gh, preferred_element_type=jnp.float32)
        own = prior_ref[0:block, cols].astype(jnp.float32) + band[0:block]
        value_cols.append(own.astype(jnp.bfloat16))
        carried_ref[:, cols] = prior_ref[block : 2 * block, cols].astype(jnp.float32) + band[block : 2 * block]
        for g, ag in enumerate(ags):
            glob_ref[g * block : (g + 1) * block, cols] = jnp.dot(ag, gh, preferred_element_type=jnp.float32)
    value_grad = value_cols[0] if len(value_cols) == 1 else jnp.concatenate(value_cols, axis=1)
    w_copy.wait()
    _partial_into(value_grad, w_ref, keep_ref, send_ref)


def _last_tick_kernel(obj_ref, carried_ref, w_hbm, *rest, heads_local, block, groups, phases, att_parts):
    att_refs = rest[:att_parts]
    pieces = rest[att_parts : att_parts + groups]
    keep_ref, send_ref, glob_ref, grad_out_ref, w_ref, w_sem = rest[att_parts + groups :]
    per_part = heads_local // att_parts
    w_copy = pltpu.make_async_copy(w_hbm, w_ref, w_sem)
    w_copy.start()
    band_rows = BAND * block
    parts = []
    for r in range(SEND_PARTS):
        part = pieces[r][...].astype(jnp.float32)
        for step in range(1, groups // SEND_PARTS):
            part = part + pieces[step * SEND_PARTS + r][...].astype(jnp.float32)
        parts.append(part)
    arrived = parts[0] if SEND_PARTS == 1 else jnp.concatenate(parts, axis=0)
    last = jnp.zeros((1, 1), jnp.int32) + (lax.axis_index("segment") == phases - 1).astype(jnp.int32)
    fresh = _pick_columns(obj_ref, grad_out_ref.shape[1])
    grad = jnp.where(last > 0, fresh, arrived.astype(jnp.bfloat16))
    grad_out_ref[...] = grad
    value_cols = []
    for h in range(heads_local):
        cols = slice(h * CHANNEL_WIDTH, (h + 1) * CHANNEL_WIDTH)
        gh = grad[:, cols]
        att_ref = att_refs[h // per_part].at[h % per_part]
        own = carried_ref[:, cols] + jnp.dot(att_ref[0:block, :], gh, preferred_element_type=jnp.float32)
        value_cols.append(own.astype(jnp.bfloat16))
        for g in range(GLOB):
            lo = band_rows + g * block
            glob_ref[g * block : (g + 1) * block, cols] = jnp.dot(
                att_ref[lo : lo + block, :], gh, preferred_element_type=jnp.float32
            )
    value_grad = value_cols[0] if len(value_cols) == 1 else jnp.concatenate(value_cols, axis=1)
    w_copy.wait()
    _partial_into(value_grad, w_ref, keep_ref, send_ref)


ANY = pl.BlockSpec(memory_space=pl.ANY)
VMEM = pl.BlockSpec(memory_space=pltpu.VMEM)
KERNEL_PARAMS = pltpu.CompilerParams()


def first_tick(initial_segment, digest_pointer, softness, window_inputs, summary_blocks, asker, lookup, prior, weights, entering):
    block = summary_blocks.shape[1]
    local_width = asker.shape[1]
    heads_local = local_width // CHANNEL_WIDTH
    groups = weights.shape[0]
    keys_total = (BAND + GLOB) * block
    feat = window_inputs.shape[1]
    flops = 2 * feat * local_width * (block + keys_total) + 14 * keys_total * block * local_width + 4 * block * local_width * groups * local_width
    ins = [initial_segment, digest_pointer, softness, window_inputs, summary_blocks, asker, lookup, entering, prior, weights]
    return pl.pallas_call(
        functools.partial(_first_tick_kernel, heads_local=heads_local, block=block),
        out_shape=(
            jax.ShapeDtypeStruct((groups, block, local_width), jnp.bfloat16),
            jax.ShapeDtypeStruct((groups, block, local_width), jnp.bfloat16),
            jax.ShapeDtypeStruct((block, local_width), jnp.float32),
            jax.ShapeDtypeStruct((GLOB * block, local_width), jnp.float32),
            jax.ShapeDtypeStruct((block, local_width), entering.dtype),
        ),
        in_specs=[VMEM] * (len(ins) - 1) + [ANY],
        out_specs=(VMEM, VMEM, VMEM, VMEM, VMEM),
        scratch_shapes=[pltpu.VMEM(weights.shape, weights.dtype), pltpu.SemaphoreType.DMA(())],
        compiler_params=KERNEL_PARAMS,
        cost_estimate=pl.CostEstimate(flops=flops, transcendentals=keys_total * block * heads_local, bytes_accessed=weights.size * 2 + 8 * block * local_width * 4),
    )(*ins)


def last_tick(atts, carried, weights, objective, pieces, phases):
    heads_local = sum(a.shape[0] for a in atts)
    keys_total, block = atts[0].shape[1:]
    local_width = carried.shape[1]
    groups = weights.shape[0]
    flops = 2 * keys_total * block * local_width + 4 * block * local_width * groups * local_width
    ins = [objective, carried, weights] + list(atts) + list(pieces)
    return pl.pallas_call(
        functools.partial(_last_tick_kernel, heads_local=heads_local, block=block, groups=len(pieces), phases=phases, att_parts=len(atts)),
        out_shape=(
            jax.ShapeDtypeStruct((groups, block, local_width), jnp.bfloat16),
            jax.ShapeDtypeStruct((groups, block, local_width), jnp.bfloat16),
            jax.ShapeDtypeStruct((GLOB * block, local_width), jnp.float32),
            jax.ShapeDtypeStruct((block, local_width), objective.dtype),
        ),
        in_specs=[VMEM, VMEM, ANY] + [VMEM] * (len(atts) + len(pieces)),
        out_specs=(VMEM, VMEM, VMEM, VMEM),
        scratch_shapes=[pltpu.VMEM(weights.shape, weights.dtype), pltpu.SemaphoreType.DMA(())],
        compiler_params=KERNEL_PARAMS,
        cost_estimate=pl.CostEstimate(flops=flops, transcendentals=0, bytes_accessed=weights.size * 2 + heads_local * keys_total * block * 2 + 8 * block * local_width * 4),
    )(*ins)


def attention_weights(tick, heads, initial_segment, digest_pointer, softness, window_inputs, summary_blocks, asker, lookup):
    block = summary_blocks.shape[1]
    local_width = asker.shape[1]
    heads_local = len(heads)
    keys_total = (BAND + GLOB) * block
    feat = window_inputs.shape[1]
    flops = 2 * feat * local_width * (block + keys_total) + 12 * keys_total * block * local_width
    ins = [initial_segment, digest_pointer, softness, window_inputs, summary_blocks, asker, lookup]
    return pl.pallas_call(
        functools.partial(_weights_kernel, tick=tick, heads=heads, block=block),
        out_shape=jax.ShapeDtypeStruct((heads_local, keys_total, block), jnp.bfloat16),
        in_specs=[VMEM] * len(ins),
        out_specs=VMEM,
        compiler_params=KERNEL_PARAMS,
        cost_estimate=pl.CostEstimate(flops=flops, transcendentals=keys_total * block * heads_local, bytes_accessed=keys_total * local_width * 2 + 4 * feat * local_width * 2),
    )(*ins)


def local(
    entering_deriv,
    objective_derivs,
    content_projection,
    asker_projection,
    lookup_projection,
    softness,
    window_inputs,
    digest_inputs,
    digest_pointer,
    initial_segment,
    prior_content_derivs,
):
    period_label = lax.axis_index("segment")
    phases = lax.axis_size("segment")
    head_group = lax.axis_index("head")
    heads = lax.axis_size("head")
    groups = heads // 2
    block_rows = entering_deriv.shape[0]
    local_width = content_projection.shape[1]
    summary_blocks = digest_inputs.reshape(SUMMARY, block_rows, digest_inputs.shape[1])
    weights = content_projection.reshape(groups, 2, local_width, local_width)
    summary_ids = jnp.arange(SUMMARY, dtype=jnp.int32)

    def live_of(tick_index):
        position = initial_segment[0] - period_label - tick_index
        return jnp.minimum(GLOB, 1 + GLOB * position // SEQ_BLOCKS)

    def digest_of(tick_index, glob):
        selector = (digest_pointer[tick_index][:, None] == summary_ids[None, :]).astype(jnp.float32)
        return jnp.sum(
            selector[:, :, None, None] * glob.reshape(GLOB, block_rows, local_width)[:, None], axis=0
        ).reshape(SUMMARY * block_rows, local_width)

    init = initial_segment.reshape(1, 1)
    keep0, send0, carried, glob0, grad0 = first_tick(
        init, digest_pointer, softness, window_inputs, summary_blocks,
        asker_projection, lookup_projection, prior_content_derivs, weights, entering_deriv,
    )
    feats = (window_inputs, asker_projection, lookup_projection)
    halves = core_pair_sum(keep0, send0)
    heads_local = local_width // CHANNEL_WIDTH
    split = 2 if heads_local % 2 == 0 else 1
    per_split = heads_local // split

    def weights_for(heads):
        return lambda ops: attention_weights(1, heads, ops[0], ops[1], ops[2], ops[3], ops[4], ops[5], ops[6])

    operands = (init, digest_pointer, softness, feats[0], summary_blocks, feats[1], feats[2])
    side_work = [
        (weights_for(tuple(range(i * per_split, (i + 1) * per_split))), operands) for i in range(split)
    ]
    pieces, later_att = shift_down_sum(halves, grad0.astype(jnp.float32), side_work)
    digest_running = digest_of(0, glob0)
    keep1, send1, glob1, grad1 = last_tick(
        later_att, carried, weights, objective_derivs[0:block_rows], pieces, phases
    )
    digest_running = digest_running + digest_of(1, glob1)
    summed = across_groups_sum(core_pair_sum(keep1, send1))
    result = (grad1.astype(jnp.float32) + summed).astype(jnp.bfloat16)
    return (result, digest_running.astype(jnp.bfloat16))


def solution(mesh):
    in_specs = (
        P("segment", None),
        P(),
        P("segment", "head"),
        P("segment", "head"),
        P("segment", "head"),
        P("segment", "head"),
        P("segment", None),
        P(),
        P("segment", None),
        P(),
        P("segment", "head"),
    )
    out_specs = (P("segment", "head"), P("segment", "head"))
    return jax.shard_map(local, mesh=mesh, in_specs=in_specs, out_specs=out_specs, check_vma=False)
```

```python
import jax
import jax.numpy as jnp
from jax import lax
from jax.sharding import PartitionSpec as P
from jax.experimental import pallas as pl
from jax.experimental.pallas import tpu as pltpu
import functools

CHANNEL_WIDTH = 128
BAND = 4
GLOB = 2
SUMMARY = 2
SEQ_BLOCKS = 1024
TICKS = 2


EPS = 1e-06


def shifted(value, axis, steps):
    count = lax.axis_size(axis)
    first, last = (max(0, -steps), min(count, count - steps))
    return lax.ppermute(value, axis, [(source, source + steps) for source in range(first, last)])


def core_pair_sum(keep, send):
    heads = lax.axis_size("head")
    got = lax.ppermute(send, "head", [(h, h ^ 1) for h in range(heads)])
    return keep.astype(jnp.float32) + got.astype(jnp.float32)


def across_groups_sum(halves):
    head_group = lax.axis_index("head")
    heads = lax.axis_size("head")
    groups = heads // 2
    outer = head_group // 2
    total = lax.dynamic_index_in_dim(halves, outer, 0, keepdims=False)
    for step in range(1, groups):
        target = (outer + step) % groups
        piece = lax.dynamic_index_in_dim(halves, target, 0, keepdims=False).astype(jnp.bfloat16)
        pairs = [(h, (((h // 2) + step) % groups) * 2 + h % 2) for h in range(heads)]
        total = total + lax.ppermute(piece, "head", pairs).astype(jnp.float32)
    return total


def shift_down_sum(halves, entering):
    head_group = lax.axis_index("head")
    heads = lax.axis_size("head")
    segments = lax.axis_size("segment")
    groups = heads // 2
    outer = head_group // 2
    total = []
    for step in range(groups):
        target = (outer + step) % groups
        piece = lax.dynamic_index_in_dim(halves, target, 0, keepdims=False)
        if step == 0:
            piece = piece + entering
        pairs = []
        for s in range(1, segments):
            for h in range(heads):
                dest = (((h // 2) + step) % groups) * 2 + h % 2
                pairs.append((s * heads + h, (s - 1) * heads + dest))
        total.append(lax.ppermute(piece.astype(jnp.bfloat16), ("segment", "head"), pairs))
    return total


def row_norm(values):
    return values * lax.rsqrt(jnp.mean(values * values, axis=-1, keepdims=True) + EPS)


def _live_of(init_ref, tick):
    position = init_ref[...] - lax.axis_index("segment") - tick
    shift = SEQ_BLOCKS.bit_length() - 1
    return jnp.minimum(GLOB, 1 + lax.shift_right_arithmetic(GLOB * position, jnp.int32(shift)))


def _pick_columns(full_ref, width):
    head = jnp.zeros((1, 1), jnp.int32) + lax.axis_index("head")
    picked = full_ref[:, 0:width]
    for j in range(1, full_ref.shape[1] // width):
        picked = jnp.where(head == j, full_ref[:, j * width : (j + 1) * width], picked)
    return picked


def _attention_weights(init_ref, ptr_ref, soft_ref, win_ref, summ_ref, ask_ref, look_ref, *, tick, heads_local, block):
    band_rows = BAND * block
    live = _live_of(init_ref, tick)
    own = win_ref[tick * block : (tick + 1) * block, :]
    band = win_ref[tick * block : tick * block + band_rows, :]
    queries = jnp.dot(own, ask_ref[...], preferred_element_type=jnp.float32)
    band_keys = jnp.dot(band, look_ref[...], preferred_element_type=jnp.float32)
    summary_keys = [
        jnp.dot(summ_ref[m], look_ref[...], preferred_element_type=jnp.float32) for m in range(summ_ref.shape[0])
    ]
    glob_keys = []
    for g in range(GLOB):
        slot = ptr_ref[tick : tick + 1, g : g + 1]
        picked = summary_keys[0]
        for m in range(1, len(summary_keys)):
            picked = jnp.where(slot == m, summary_keys[m], picked)
        glob_keys.append(picked)
    keys_total = band_rows + GLOB * block
    key_ids = lax.broadcasted_iota(jnp.int32, (keys_total, block), 0)
    query_ids = lax.broadcasted_iota(jnp.int32, (keys_total, block), 1)
    slot_of = (key_ids - band_rows) // block
    admitted = ((key_ids < band_rows) & ((key_ids >= block) | (key_ids <= query_ids))) | (
        (key_ids >= band_rows) & (slot_of < live)
    )
    all_keys = jnp.concatenate([band_keys] + glob_keys, axis=0)
    contract = (((1,), (1,)), ((), ()))
    for h in range(heads_local):
        cols = slice(h * CHANNEL_WIDTH, (h + 1) * CHANNEL_WIDTH)
        scale = soft_ref[0:1, h : h + 1] * (1.0 / CHANNEL_WIDTH)
        qh = row_norm(queries[:, cols])
        kh = row_norm(all_keys[:, cols])
        sc = lax.dot_general(kh, qh, contract, precision=lax.Precision.HIGHEST, preferred_element_type=jnp.float32) * scale
        ex = jnp.where(admitted, jnp.exp(sc), 0.0)
        att = (ex / jnp.sum(ex, axis=0, keepdims=True)).astype(jnp.bfloat16)
        yield h, att[0:band_rows], [att[band_rows + g * block : band_rows + (g + 1) * block] for g in range(GLOB)]


def _weights_kernel(init_ref, ptr_ref, soft_ref, win_ref, summ_ref, ask_ref, look_ref, out_ref, *, tick, heads_local, block):
    band_rows = BAND * block
    for h, ab, ags in _attention_weights(
        init_ref, ptr_ref, soft_ref, win_ref, summ_ref, ask_ref, look_ref, tick=tick, heads_local=heads_local, block=block
    ):
        out_ref[h, 0:band_rows, :] = ab
        for g, ag in enumerate(ags):
            lo = band_rows + g * block
            out_ref[h, lo : lo + block, :] = ag


def _partial_into(value_grad, w_ref, keep_ref, send_ref):
    contract = (((1,), (1,)), ((), ()))
    core = jnp.zeros((1, 1), jnp.int32) + lax.axis_index("head") % 2
    for g in range(w_ref.shape[0]):
        even, odd = [
            lax.dot_general(value_grad, w_ref[g, p], contract, preferred_element_type=jnp.float32).astype(keep_ref.dtype)
            for p in range(2)
        ]
        keep_ref[g] = jnp.where(core == 0, even, odd)
        send_ref[g] = jnp.where(core == 0, odd, even)


def _first_tick_kernel(
    init_ref, ptr_ref, soft_ref, win_ref, summ_ref, ask_ref, look_ref, ent_ref, prior_ref, w_hbm,
    keep_ref, send_ref, carried_ref, glob_ref, grad_out_ref, w_ref, w_sem, *, heads_local, block
):
    w_copy = pltpu.make_async_copy(w_hbm, w_ref, w_sem)
    w_copy.start()
    weights = list(_attention_weights(
        init_ref, ptr_ref, soft_ref, win_ref, summ_ref, ask_ref, look_ref, tick=0, heads_local=heads_local, block=block
    ))
    grad = _pick_columns(ent_ref, grad_out_ref.shape[1])
    grad_out_ref[...] = grad
    value_cols = []
    for h, ab, ags in weights:
        cols = slice(h * CHANNEL_WIDTH, (h + 1) * CHANNEL_WIDTH)
        gh = grad[:, cols]
        band = jnp.dot(ab, gh, preferred_element_type=jnp.float32)
        own = prior_ref[0:block, cols].astype(jnp.float32) + band[0:block]
        value_cols.append(own.astype(jnp.bfloat16))
        carried_ref[:, cols] = prior_ref[block : 2 * block, cols].astype(jnp.float32) + band[block : 2 * block]
        for g, ag in enumerate(ags):
            glob_ref[g * block : (g + 1) * block, cols] = jnp.dot(ag, gh, preferred_element_type=jnp.float32)
    value_grad = value_cols[0] if len(value_cols) == 1 else jnp.concatenate(value_cols, axis=1)
    w_copy.wait()
    _partial_into(value_grad, w_ref, keep_ref, send_ref)


def _last_tick_kernel(obj_ref, att_ref, carried_ref, w_hbm, *rest, heads_local, block, groups, phases):
    pieces = rest[:groups]
    keep_ref, send_ref, glob_ref, grad_out_ref, w_ref, w_sem = rest[groups:]
    w_copy = pltpu.make_async_copy(w_hbm, w_ref, w_sem)
    w_copy.start()
    band_rows = BAND * block
    arrived = pieces[0][...].astype(jnp.float32)
    for piece in pieces[1:]:
        arrived = arrived + piece[...].astype(jnp.float32)
    last = jnp.zeros((1, 1), jnp.int32) + (lax.axis_index("segment") == phases - 1).astype(jnp.int32)
    fresh = _pick_columns(obj_ref, grad_out_ref.shape[1])
    grad = jnp.where(last > 0, fresh, arrived.astype(jnp.bfloat16))
    grad_out_ref[...] = grad
    value_cols = []
    for h in range(heads_local):
        cols = slice(h * CHANNEL_WIDTH, (h + 1) * CHANNEL_WIDTH)
        gh = grad[:, cols]
        own = carried_ref[:, cols] + jnp.dot(att_ref[h, 0:block, :], gh, preferred_element_type=jnp.float32)
        value_cols.append(own.astype(jnp.bfloat16))
        for g in range(GLOB):
            lo = band_rows + g * block
            glob_ref[g * block : (g + 1) * block, cols] = jnp.dot(
                att_ref[h, lo : lo + block, :], gh, preferred_element_type=jnp.float32
            )
    value_grad = value_cols[0] if len(value_cols) == 1 else jnp.concatenate(value_cols, axis=1)
    w_copy.wait()
    _partial_into(value_grad, w_ref, keep_ref, send_ref)


ANY = pl.BlockSpec(memory_space=pl.ANY)
VMEM = pl.BlockSpec(memory_space=pltpu.VMEM)
KERNEL_PARAMS = pltpu.CompilerParams()


def first_tick(initial_segment, digest_pointer, softness, window_inputs, summary_blocks, asker, lookup, prior, weights, entering):
    block = summary_blocks.shape[1]
    local_width = asker.shape[1]
    heads_local = local_width // CHANNEL_WIDTH
    groups = weights.shape[0]
    keys_total = (BAND + GLOB) * block
    feat = window_inputs.shape[1]
    flops = 2 * feat * local_width * (block + keys_total) + 14 * keys_total * block * local_width + 4 * block * local_width * groups * local_width
    ins = [initial_segment, digest_pointer, softness, window_inputs, summary_blocks, asker, lookup, entering, prior, weights]
    return pl.pallas_call(
        functools.partial(_first_tick_kernel, heads_local=heads_local, block=block),
        out_shape=(
            jax.ShapeDtypeStruct((groups, block, local_width), jnp.bfloat16),
            jax.ShapeDtypeStruct((groups, block, local_width), jnp.bfloat16),
            jax.ShapeDtypeStruct((block, local_width), jnp.float32),
            jax.ShapeDtypeStruct((GLOB * block, local_width), jnp.float32),
            jax.ShapeDtypeStruct((block, local_width), entering.dtype),
        ),
        in_specs=[VMEM] * (len(ins) - 1) + [ANY],
        out_specs=(VMEM, VMEM, VMEM, VMEM, VMEM),
        scratch_shapes=[pltpu.VMEM(weights.shape, weights.dtype), pltpu.SemaphoreType.DMA(())],
        compiler_params=KERNEL_PARAMS,
        cost_estimate=pl.CostEstimate(flops=flops, transcendentals=keys_total * block * heads_local, bytes_accessed=weights.size * 2 + 8 * block * local_width * 4),
    )(*ins)


def last_tick(att, carried, weights, objective, pieces, phases):
    heads_local, keys_total, block = att.shape
    local_width = carried.shape[1]
    groups = weights.shape[0]
    flops = 2 * keys_total * block * local_width + 4 * block * local_width * groups * local_width
    ins = [objective, att, carried, weights] + list(pieces)
    return pl.pallas_call(
        functools.partial(_last_tick_kernel, heads_local=heads_local, block=block, groups=len(pieces), phases=phases),
        out_shape=(
            jax.ShapeDtypeStruct((groups, block, local_width), jnp.bfloat16),
            jax.ShapeDtypeStruct((groups, block, local_width), jnp.bfloat16),
            jax.ShapeDtypeStruct((GLOB * block, local_width), jnp.float32),
            jax.ShapeDtypeStruct((block, local_width), objective.dtype),
        ),
        in_specs=[VMEM, VMEM, VMEM, ANY] + [VMEM] * len(pieces),
        out_specs=(VMEM, VMEM, VMEM, VMEM),
        scratch_shapes=[pltpu.VMEM(weights.shape, weights.dtype), pltpu.SemaphoreType.DMA(())],
        compiler_params=KERNEL_PARAMS,
        cost_estimate=pl.CostEstimate(flops=flops, transcendentals=0, bytes_accessed=weights.size * 2 + att.size * 2 + 8 * block * local_width * 4),
    )(*ins)


def attention_weights(tick, initial_segment, digest_pointer, softness, window_inputs, summary_blocks, asker, lookup):
    block = summary_blocks.shape[1]
    local_width = asker.shape[1]
    heads_local = local_width // CHANNEL_WIDTH
    keys_total = (BAND + GLOB) * block
    feat = window_inputs.shape[1]
    flops = 2 * feat * local_width * (block + keys_total) + 12 * keys_total * block * local_width
    ins = [initial_segment, digest_pointer, softness, window_inputs, summary_blocks, asker, lookup]
    return pl.pallas_call(
        functools.partial(_weights_kernel, tick=tick, heads_local=heads_local, block=block),
        out_shape=jax.ShapeDtypeStruct((heads_local, keys_total, block), jnp.bfloat16),
        in_specs=[VMEM] * len(ins),
        out_specs=VMEM,
        compiler_params=KERNEL_PARAMS,
        cost_estimate=pl.CostEstimate(flops=flops, transcendentals=keys_total * block * heads_local, bytes_accessed=keys_total * local_width * 2 + 4 * feat * local_width * 2),
    )(*ins)


def local(
    entering_deriv,
    objective_derivs,
    content_projection,
    asker_projection,
    lookup_projection,
    softness,
    window_inputs,
    digest_inputs,
    digest_pointer,
    initial_segment,
    prior_content_derivs,
):
    period_label = lax.axis_index("segment")
    phases = lax.axis_size("segment")
    head_group = lax.axis_index("head")
    heads = lax.axis_size("head")
    groups = heads // 2
    block_rows = entering_deriv.shape[0]
    local_width = content_projection.shape[1]
    summary_blocks = digest_inputs.reshape(SUMMARY, block_rows, digest_inputs.shape[1])
    weights = content_projection.reshape(groups, 2, local_width, local_width)
    summary_ids = jnp.arange(SUMMARY, dtype=jnp.int32)

    def live_of(tick_index):
        position = initial_segment[0] - period_label - tick_index
        return jnp.minimum(GLOB, 1 + GLOB * position // SEQ_BLOCKS)

    def digest_of(tick_index, glob):
        selector = (digest_pointer[tick_index][:, None] == summary_ids[None, :]).astype(jnp.float32)
        return jnp.sum(
            selector[:, :, None, None] * glob.reshape(GLOB, block_rows, local_width)[:, None], axis=0
        ).reshape(SUMMARY * block_rows, local_width)

    init = initial_segment.reshape(1, 1)
    keep0, send0, carried, glob0, grad0 = first_tick(
        init, digest_pointer, softness, window_inputs, summary_blocks,
        asker_projection, lookup_projection, prior_content_derivs, weights, entering_deriv,
    )
    feats = (window_inputs, asker_projection, lookup_projection)
    halves = core_pair_sum(keep0, send0)
    halves, feats = lax.optimization_barrier((halves, feats))
    later_att = attention_weights(
        1, init, digest_pointer, softness, feats[0], summary_blocks, feats[1], feats[2]
    )
    pieces = shift_down_sum(halves, grad0.astype(jnp.float32))
    digest_running = digest_of(0, glob0)
    keep1, send1, glob1, grad1 = last_tick(
        later_att, carried, weights, objective_derivs[0:block_rows], pieces, phases
    )
    digest_running = digest_running + digest_of(1, glob1)
    summed = across_groups_sum(core_pair_sum(keep1, send1))
    result = (grad1.astype(jnp.float32) + summed).astype(jnp.bfloat16)
    return (result, digest_running.astype(jnp.bfloat16))


def solution(mesh):
    in_specs = (
        P("segment", None),
        P(),
        P("segment", "head"),
        P("segment", "head"),
        P("segment", "head"),
        P("segment", "head"),
        P("segment", None),
        P(),
        P("segment", None),
        P(),
        P("segment", "head"),
    )
    out_specs = (P("segment", "head"), P("segment", "head"))
    return jax.shard_map(local, mesh=mesh, in_specs=in_specs, out_specs=out_specs, check_vma=False)
```

```python
import jax
import jax.numpy as jnp
from jax import lax
from jax.sharding import PartitionSpec as P
from jax.experimental import pallas as pl
from jax.experimental.pallas import tpu as pltpu
import functools

CHANNEL_WIDTH = 128
BAND = 4
GLOB = 2
SUMMARY = 2
SEQ_BLOCKS = 1024
TICKS = 2


EPS = 1e-06


def shifted(value, axis, steps):
    count = lax.axis_size(axis)
    first, last = (max(0, -steps), min(count, count - steps))
    return lax.ppermute(value, axis, [(source, source + steps) for source in range(first, last)])


def core_pair_sum(keep, send):
    heads = lax.axis_size("head")
    got = lax.ppermute(send, "head", [(h, h ^ 1) for h in range(heads)])
    return keep.astype(jnp.float32) + got.astype(jnp.float32)


def across_groups_sum(halves):
    head_group = lax.axis_index("head")
    heads = lax.axis_size("head")
    groups = heads // 2
    outer = head_group // 2
    total = lax.dynamic_index_in_dim(halves, outer, 0, keepdims=False)
    for step in range(1, groups):
        target = (outer + step) % groups
        piece = lax.dynamic_index_in_dim(halves, target, 0, keepdims=False).astype(jnp.bfloat16)
        pairs = [(h, (((h // 2) + step) % groups) * 2 + h % 2) for h in range(heads)]
        total = total + lax.ppermute(piece, "head", pairs).astype(jnp.float32)
    return total


def shift_down_sum(halves, entering):
    head_group = lax.axis_index("head")
    heads = lax.axis_size("head")
    segments = lax.axis_size("segment")
    groups = heads // 2
    outer = head_group // 2
    total = []
    for step in range(groups):
        target = (outer + step) % groups
        piece = lax.dynamic_index_in_dim(halves, target, 0, keepdims=False)
        if step == 0:
            piece = piece + entering
        pairs = []
        for s in range(1, segments):
            for h in range(heads):
                dest = (((h // 2) + step) % groups) * 2 + h % 2
                pairs.append((s * heads + h, (s - 1) * heads + dest))
        total.append(lax.ppermute(piece.astype(jnp.bfloat16), ("segment", "head"), pairs))
    return total


def row_norm(values):
    return values * lax.rsqrt(jnp.mean(values * values, axis=-1, keepdims=True) + EPS)


def _live_of(init_ref, tick):
    position = init_ref[...] - lax.axis_index("segment") - tick
    shift = SEQ_BLOCKS.bit_length() - 1
    return jnp.minimum(GLOB, 1 + lax.shift_right_arithmetic(GLOB * position, jnp.int32(shift)))


def _pick_columns(full_ref, width):
    head = jnp.zeros((1, 1), jnp.int32) + lax.axis_index("head")
    picked = full_ref[:, 0:width]
    for j in range(1, full_ref.shape[1] // width):
        picked = jnp.where(head == j, full_ref[:, j * width : (j + 1) * width], picked)
    return picked


def _attention_weights(init_ref, ptr_ref, soft_ref, win_ref, summ_ref, ask_ref, look_ref, *, tick, heads_local, block, precision=lax.Precision.HIGHEST):
    band_rows = BAND * block
    live = _live_of(init_ref, tick)
    own = win_ref[tick * block : (tick + 1) * block, :]
    band = win_ref[tick * block : tick * block + band_rows, :]
    queries = jnp.dot(own, ask_ref[...], preferred_element_type=jnp.float32)
    band_keys = jnp.dot(band, look_ref[...], preferred_element_type=jnp.float32)
    summary_keys = [
        jnp.dot(summ_ref[m], look_ref[...], preferred_element_type=jnp.float32) for m in range(summ_ref.shape[0])
    ]
    glob_keys = []
    for g in range(GLOB):
        slot = ptr_ref[tick : tick + 1, g : g + 1]
        picked = summary_keys[0]
        for m in range(1, len(summary_keys)):
            picked = jnp.where(slot == m, summary_keys[m], picked)
        glob_keys.append(picked)
    keys_total = band_rows + GLOB * block
    key_ids = lax.broadcasted_iota(jnp.int32, (keys_total, block), 0)
    query_ids = lax.broadcasted_iota(jnp.int32, (keys_total, block), 1)
    slot_of = (key_ids - band_rows) // block
    admitted = ((key_ids < band_rows) & ((key_ids >= block) | (key_ids <= query_ids))) | (
        (key_ids >= band_rows) & (slot_of < live)
    )
    all_keys = jnp.concatenate([band_keys] + glob_keys, axis=0)
    contract = (((1,), (1,)), ((), ()))
    for h in range(heads_local):
        cols = slice(h * CHANNEL_WIDTH, (h + 1) * CHANNEL_WIDTH)
        scale = soft_ref[0:1, h : h + 1] * (1.0 / CHANNEL_WIDTH)
        qh = row_norm(queries[:, cols])
        kh = row_norm(all_keys[:, cols])
        sc = lax.dot_general(kh, qh, contract, precision=precision, preferred_element_type=jnp.float32) * scale
        ex = jnp.where(admitted, jnp.exp(sc), 0.0)
        att = (ex / jnp.sum(ex, axis=0, keepdims=True)).astype(jnp.bfloat16)
        yield h, att[0:band_rows], [att[band_rows + g * block : band_rows + (g + 1) * block] for g in range(GLOB)]


def _weights_kernel(init_ref, ptr_ref, soft_ref, win_ref, summ_ref, ask_ref, look_ref, out_ref, *, tick, heads_local, block):
    band_rows = BAND * block
    for h, ab, ags in _attention_weights(
        init_ref, ptr_ref, soft_ref, win_ref, summ_ref, ask_ref, look_ref, tick=tick, heads_local=heads_local, block=block
    ):
        out_ref[h, 0:band_rows, :] = ab
        for g, ag in enumerate(ags):
            lo = band_rows + g * block
            out_ref[h, lo : lo + block, :] = ag


def _partial_into(value_grad, w_ref, keep_ref, send_ref):
    contract = (((1,), (1,)), ((), ()))
    core = jnp.zeros((1, 1), jnp.int32) + lax.axis_index("head") % 2
    for g in range(w_ref.shape[0]):
        even, odd = [
            lax.dot_general(value_grad, w_ref[g, p], contract, preferred_element_type=jnp.float32).astype(keep_ref.dtype)
            for p in range(2)
        ]
        keep_ref[g] = jnp.where(core == 0, even, odd)
        send_ref[g] = jnp.where(core == 0, odd, even)


def _first_tick_kernel(
    init_ref, ptr_ref, soft_ref, win_ref, summ_ref, ask_ref, look_ref, ent_ref, prior_ref, w_hbm,
    keep_ref, send_ref, carried_ref, glob_ref, grad_out_ref, w_ref, w_sem, *, heads_local, block
):
    w_copy = pltpu.make_async_copy(w_hbm, w_ref, w_sem)
    w_copy.start()
    weights = list(_attention_weights(
        init_ref, ptr_ref, soft_ref, win_ref, summ_ref, ask_ref, look_ref, tick=0, heads_local=heads_local, block=block,
        precision=lax.Precision.HIGH,
    ))
    grad = _pick_columns(ent_ref, grad_out_ref.shape[1])
    grad_out_ref[...] = grad
    value_cols = []
    for h, ab, ags in weights:
        cols = slice(h * CHANNEL_WIDTH, (h + 1) * CHANNEL_WIDTH)
        gh = grad[:, cols]
        band = jnp.dot(ab, gh, preferred_element_type=jnp.float32)
        own = prior_ref[0:block, cols].astype(jnp.float32) + band[0:block]
        value_cols.append(own.astype(jnp.bfloat16))
        carried_ref[:, cols] = prior_ref[block : 2 * block, cols].astype(jnp.float32) + band[block : 2 * block]
        for g, ag in enumerate(ags):
            glob_ref[g * block : (g + 1) * block, cols] = jnp.dot(ag, gh, preferred_element_type=jnp.float32)
    value_grad = value_cols[0] if len(value_cols) == 1 else jnp.concatenate(value_cols, axis=1)
    w_copy.wait()
    _partial_into(value_grad, w_ref, keep_ref, send_ref)


def _last_tick_kernel(obj_ref, att_ref, carried_ref, w_hbm, *rest, heads_local, block, groups, phases):
    pieces = rest[:groups]
    keep_ref, send_ref, glob_ref, grad_out_ref, w_ref, w_sem = rest[groups:]
    w_copy = pltpu.make_async_copy(w_hbm, w_ref, w_sem)
    w_copy.start()
    band_rows = BAND * block
    arrived = pieces[0][...].astype(jnp.float32)
    for piece in pieces[1:]:
        arrived = arrived + piece[...].astype(jnp.float32)
    last = jnp.zeros((1, 1), jnp.int32) + (lax.axis_index("segment") == phases - 1).astype(jnp.int32)
    fresh = _pick_columns(obj_ref, grad_out_ref.shape[1])
    grad = jnp.where(last > 0, fresh, arrived.astype(jnp.bfloat16))
    grad_out_ref[...] = grad
    value_cols = []
    for h in range(heads_local):
        cols = slice(h * CHANNEL_WIDTH, (h + 1) * CHANNEL_WIDTH)
        gh = grad[:, cols]
        own = carried_ref[:, cols] + jnp.dot(att_ref[h, 0:block, :], gh, preferred_element_type=jnp.float32)
        value_cols.append(own.astype(jnp.bfloat16))
        for g in range(GLOB):
            lo = band_rows + g * block
            glob_ref[g * block : (g + 1) * block, cols] = jnp.dot(
                att_ref[h, lo : lo + block, :], gh, preferred_element_type=jnp.float32
            )
    value_grad = value_cols[0] if len(value_cols) == 1 else jnp.concatenate(value_cols, axis=1)
    w_copy.wait()
    _partial_into(value_grad, w_ref, keep_ref, send_ref)


ANY = pl.BlockSpec(memory_space=pl.ANY)
VMEM = pl.BlockSpec(memory_space=pltpu.VMEM)
KERNEL_PARAMS = pltpu.CompilerParams()


def first_tick(initial_segment, digest_pointer, softness, window_inputs, summary_blocks, asker, lookup, prior, weights, entering):
    block = summary_blocks.shape[1]
    local_width = asker.shape[1]
    heads_local = local_width // CHANNEL_WIDTH
    groups = weights.shape[0]
    keys_total = (BAND + GLOB) * block
    feat = window_inputs.shape[1]
    flops = 2 * feat * local_width * (block + keys_total) + 14 * keys_total * block * local_width + 4 * block * local_width * groups * local_width
    ins = [initial_segment, digest_pointer, softness, window_inputs, summary_blocks, asker, lookup, entering, prior, weights]
    return pl.pallas_call(
        functools.partial(_first_tick_kernel, heads_local=heads_local, block=block),
        out_shape=(
            jax.ShapeDtypeStruct((groups, block, local_width), jnp.bfloat16),
            jax.ShapeDtypeStruct((groups, block, local_width), jnp.bfloat16),
            jax.ShapeDtypeStruct((block, local_width), jnp.float32),
            jax.ShapeDtypeStruct((GLOB * block, local_width), jnp.float32),
            jax.ShapeDtypeStruct((block, local_width), entering.dtype),
        ),
        in_specs=[VMEM] * (len(ins) - 1) + [ANY],
        out_specs=(VMEM, VMEM, VMEM, VMEM, VMEM),
        scratch_shapes=[pltpu.VMEM(weights.shape, weights.dtype), pltpu.SemaphoreType.DMA(())],
        compiler_params=KERNEL_PARAMS,
        cost_estimate=pl.CostEstimate(flops=flops, transcendentals=keys_total * block * heads_local, bytes_accessed=weights.size * 2 + 8 * block * local_width * 4),
    )(*ins)


def last_tick(att, carried, weights, objective, pieces, phases):
    heads_local, keys_total, block = att.shape
    local_width = carried.shape[1]
    groups = weights.shape[0]
    flops = 2 * keys_total * block * local_width + 4 * block * local_width * groups * local_width
    ins = [objective, att, carried, weights] + list(pieces)
    return pl.pallas_call(
        functools.partial(_last_tick_kernel, heads_local=heads_local, block=block, groups=len(pieces), phases=phases),
        out_shape=(
            jax.ShapeDtypeStruct((groups, block, local_width), jnp.bfloat16),
            jax.ShapeDtypeStruct((groups, block, local_width), jnp.bfloat16),
            jax.ShapeDtypeStruct((GLOB * block, local_width), jnp.float32),
            jax.ShapeDtypeStruct((block, local_width), objective.dtype),
        ),
        in_specs=[VMEM, VMEM, VMEM, ANY] + [VMEM] * len(pieces),
        out_specs=(VMEM, VMEM, VMEM, VMEM),
        scratch_shapes=[pltpu.VMEM(weights.shape, weights.dtype), pltpu.SemaphoreType.DMA(())],
        compiler_params=KERNEL_PARAMS,
        cost_estimate=pl.CostEstimate(flops=flops, transcendentals=0, bytes_accessed=weights.size * 2 + att.size * 2 + 8 * block * local_width * 4),
    )(*ins)


def attention_weights(tick, initial_segment, digest_pointer, softness, window_inputs, summary_blocks, asker, lookup):
    block = summary_blocks.shape[1]
    local_width = asker.shape[1]
    heads_local = local_width // CHANNEL_WIDTH
    keys_total = (BAND + GLOB) * block
    feat = window_inputs.shape[1]
    flops = 2 * feat * local_width * (block + keys_total) + 12 * keys_total * block * local_width
    ins = [initial_segment, digest_pointer, softness, window_inputs, summary_blocks, asker, lookup]
    return pl.pallas_call(
        functools.partial(_weights_kernel, tick=tick, heads_local=heads_local, block=block),
        out_shape=jax.ShapeDtypeStruct((heads_local, keys_total, block), jnp.bfloat16),
        in_specs=[VMEM] * len(ins),
        out_specs=VMEM,
        compiler_params=KERNEL_PARAMS,
        cost_estimate=pl.CostEstimate(flops=flops, transcendentals=keys_total * block * heads_local, bytes_accessed=keys_total * local_width * 2 + 4 * feat * local_width * 2),
    )(*ins)


def local(
    entering_deriv,
    objective_derivs,
    content_projection,
    asker_projection,
    lookup_projection,
    softness,
    window_inputs,
    digest_inputs,
    digest_pointer,
    initial_segment,
    prior_content_derivs,
):
    period_label = lax.axis_index("segment")
    phases = lax.axis_size("segment")
    head_group = lax.axis_index("head")
    heads = lax.axis_size("head")
    groups = heads // 2
    block_rows = entering_deriv.shape[0]
    local_width = content_projection.shape[1]
    summary_blocks = digest_inputs.reshape(SUMMARY, block_rows, digest_inputs.shape[1])
    weights = content_projection.reshape(groups, 2, local_width, local_width)
    summary_ids = jnp.arange(SUMMARY, dtype=jnp.int32)

    def live_of(tick_index):
        position = initial_segment[0] - period_label - tick_index
        return jnp.minimum(GLOB, 1 + GLOB * position // SEQ_BLOCKS)

    def digest_of(tick_index, glob):
        selector = (digest_pointer[tick_index][:, None] == summary_ids[None, :]).astype(jnp.float32)
        return jnp.sum(
            selector[:, :, None, None] * glob.reshape(GLOB, block_rows, local_width)[:, None], axis=0
        ).reshape(SUMMARY * block_rows, local_width)

    init = initial_segment.reshape(1, 1)
    keep0, send0, carried, glob0, grad0 = first_tick(
        init, digest_pointer, softness, window_inputs, summary_blocks,
        asker_projection, lookup_projection, prior_content_derivs, weights, entering_deriv,
    )
    feats = (window_inputs, asker_projection, lookup_projection)
    halves = core_pair_sum(keep0, send0)
    halves, feats = lax.optimization_barrier((halves, feats))
    later_att = attention_weights(
        1, init, digest_pointer, softness, feats[0], summary_blocks, feats[1], feats[2]
    )
    pieces = shift_down_sum(halves, grad0.astype(jnp.float32))
    digest_running = digest_of(0, glob0)
    keep1, send1, glob1, grad1 = last_tick(
        later_att, carried, weights, objective_derivs[0:block_rows], pieces, phases
    )
    digest_running = digest_running + digest_of(1, glob1)
    summed = across_groups_sum(core_pair_sum(keep1, send1))
    result = (grad1.astype(jnp.float32) + summed).astype(jnp.bfloat16)
    return (result, digest_running.astype(jnp.bfloat16))


def solution(mesh):
    in_specs = (
        P("segment", None),
        P(),
        P("segment", "head"),
        P("segment", "head"),
        P("segment", "head"),
        P("segment", "head"),
        P("segment", None),
        P(),
        P("segment", None),
        P(),
        P("segment", "head"),
    )
    out_specs = (P("segment", "head"), P("segment", "head"))
    return jax.shard_map(local, mesh=mesh, in_specs=in_specs, out_specs=out_specs, check_vma=False)
```

```python
import jax
import jax.numpy as jnp
from jax import lax
from jax.sharding import PartitionSpec as P
from jax.experimental import pallas as pl
from jax.experimental.pallas import tpu as pltpu
import functools

CHANNEL_WIDTH = 128
BAND = 4
GLOB = 2
SUMMARY = 2
SEQ_BLOCKS = 1024
TICKS = 2


EPS = 1e-06


def shifted(value, axis, steps):
    count = lax.axis_size(axis)
    first, last = (max(0, -steps), min(count, count - steps))
    return lax.ppermute(value, axis, [(source, source + steps) for source in range(first, last)])


def core_pair_sum(keep, send):
    heads = lax.axis_size("head")
    got = lax.ppermute(send, "head", [(h, h ^ 1) for h in range(heads)])
    return keep.astype(jnp.float32) + got.astype(jnp.float32)


def across_groups_sum(halves):
    head_group = lax.axis_index("head")
    heads = lax.axis_size("head")
    groups = heads // 2
    outer = head_group // 2
    total = lax.dynamic_index_in_dim(halves, outer, 0, keepdims=False)
    for step in range(1, groups):
        target = (outer + step) % groups
        piece = lax.dynamic_index_in_dim(halves, target, 0, keepdims=False).astype(jnp.bfloat16)
        pairs = [(h, (((h // 2) + step) % groups) * 2 + h % 2) for h in range(heads)]
        total = total + lax.ppermute(piece, "head", pairs).astype(jnp.float32)
    return total


def shift_down_sum(halves, entering):
    head_group = lax.axis_index("head")
    heads = lax.axis_size("head")
    segments = lax.axis_size("segment")
    groups = heads // 2
    outer = head_group // 2
    total = []
    for step in range(groups):
        target = (outer + step) % groups
        piece = lax.dynamic_index_in_dim(halves, target, 0, keepdims=False)
        if step == 0:
            piece = piece + entering
        pairs = []
        for s in range(1, segments):
            for h in range(heads):
                dest = (((h // 2) + step) % groups) * 2 + h % 2
                pairs.append((s * heads + h, (s - 1) * heads + dest))
        total.append(lax.ppermute(piece.astype(jnp.bfloat16), ("segment", "head"), pairs))
    return total


def row_norm(values):
    return values * lax.rsqrt(jnp.mean(values * values, axis=-1, keepdims=True) + EPS)


def _live_of(init_ref, tick):
    position = init_ref[...] - lax.axis_index("segment") - tick
    shift = SEQ_BLOCKS.bit_length() - 1
    return jnp.minimum(GLOB, 1 + lax.shift_right_arithmetic(GLOB * position, jnp.int32(shift)))


def _pick_columns(full_ref, width):
    head = jnp.zeros((1, 1), jnp.int32) + lax.axis_index("head")
    picked = full_ref[:, 0:width]
    for j in range(1, full_ref.shape[1] // width):
        picked = jnp.where(head == j, full_ref[:, j * width : (j + 1) * width], picked)
    return picked


def _attention_weights(init_ref, ptr_ref, soft_ref, win_ref, summ_ref, ask_ref, look_ref, *, tick, heads_local, block):
    band_rows = BAND * block
    live = _live_of(init_ref, tick)
    own = win_ref[tick * block : (tick + 1) * block, :]
    band = win_ref[tick * block : tick * block + band_rows, :]
    queries = jnp.dot(own, ask_ref[...], preferred_element_type=jnp.float32)
    band_keys = jnp.dot(band, look_ref[...], preferred_element_type=jnp.float32)
    summary_keys = [
        jnp.dot(summ_ref[m], look_ref[...], preferred_element_type=jnp.float32) for m in range(summ_ref.shape[0])
    ]
    glob_keys = []
    for g in range(GLOB):
        slot = ptr_ref[tick : tick + 1, g : g + 1]
        picked = summary_keys[0]
        for m in range(1, len(summary_keys)):
            picked = jnp.where(slot == m, summary_keys[m], picked)
        glob_keys.append(picked)
    keys_total = band_rows + GLOB * block
    key_ids = lax.broadcasted_iota(jnp.int32, (keys_total, block), 0)
    query_ids = lax.broadcasted_iota(jnp.int32, (keys_total, block), 1)
    slot_of = (key_ids - band_rows) // block
    admitted = ((key_ids < band_rows) & ((key_ids >= block) | (key_ids <= query_ids))) | (
        (key_ids >= band_rows) & (slot_of < live)
    )
    all_keys = jnp.concatenate([band_keys] + glob_keys, axis=0)
    contract = (((1,), (1,)), ((), ()))
    for h in range(heads_local):
        cols = slice(h * CHANNEL_WIDTH, (h + 1) * CHANNEL_WIDTH)
        scale = soft_ref[0:1, h : h + 1] * (1.0 / CHANNEL_WIDTH)
        qh = row_norm(queries[:, cols])
        kh = row_norm(all_keys[:, cols])
        sc = lax.dot_general(kh, qh, contract, precision=lax.Precision.HIGHEST, preferred_element_type=jnp.float32) * scale
        ex = jnp.where(admitted, jnp.exp(sc), 0.0)
        att = (ex / jnp.sum(ex, axis=0, keepdims=True)).astype(jnp.bfloat16)
        yield h, att[0:band_rows], [att[band_rows + g * block : band_rows + (g + 1) * block] for g in range(GLOB)]


def _weights_kernel(init_ref, ptr_ref, soft_ref, win_ref, summ_ref, ask_ref, look_ref, out_ref, *, tick, heads_local, block):
    band_rows = BAND * block
    for h, ab, ags in _attention_weights(
        init_ref, ptr_ref, soft_ref, win_ref, summ_ref, ask_ref, look_ref, tick=tick, heads_local=heads_local, block=block
    ):
        out_ref[h, 0:band_rows, :] = ab
        for g, ag in enumerate(ags):
            lo = band_rows + g * block
            out_ref[h, lo : lo + block, :] = ag


def _fetch_weights(w_hbm, w_ref, w_sem):
    copies = []
    for g in range(w_hbm.shape[0]):
        for p in range(2):
            copy = pltpu.make_async_copy(w_hbm.at[g, p], w_ref.at[g, p], w_sem.at[2 * g + p])
            copy.start()
            copies.append(copy)
    return copies


def _partial_into(value_grad, w_ref, copies, keep_ref, send_ref):
    contract = (((1,), (1,)), ((), ()))
    core = jnp.zeros((1, 1), jnp.int32) + lax.axis_index("head") % 2
    for g in range(w_ref.shape[0]):
        blocks = []
        for p in range(2):
            copies[2 * g + p].wait()
            blocks.append(
                lax.dot_general(value_grad, w_ref[g, p], contract, preferred_element_type=jnp.float32).astype(keep_ref.dtype)
            )
        even, odd = blocks
        keep_ref[g] = jnp.where(core == 0, even, odd)
        send_ref[g] = jnp.where(core == 0, odd, even)


def _first_tick_kernel(
    init_ref, ptr_ref, soft_ref, win_ref, summ_ref, ask_ref, look_ref, ent_ref, prior_ref, w_hbm,
    keep_ref, send_ref, carried_ref, glob_ref, grad_out_ref, w_ref, w_sem, *, heads_local, block
):
    w_copies = _fetch_weights(w_hbm, w_ref, w_sem)
    weights = list(_attention_weights(
        init_ref, ptr_ref, soft_ref, win_ref, summ_ref, ask_ref, look_ref, tick=0, heads_local=heads_local, block=block
    ))
    grad = _pick_columns(ent_ref, grad_out_ref.shape[1])
    grad_out_ref[...] = grad
    value_cols = []
    for h, ab, ags in weights:
        cols = slice(h * CHANNEL_WIDTH, (h + 1) * CHANNEL_WIDTH)
        gh = grad[:, cols]
        band = jnp.dot(ab, gh, preferred_element_type=jnp.float32)
        own = prior_ref[0:block, cols].astype(jnp.float32) + band[0:block]
        value_cols.append(own.astype(jnp.bfloat16))
        carried_ref[:, cols] = prior_ref[block : 2 * block, cols].astype(jnp.float32) + band[block : 2 * block]
        for g, ag in enumerate(ags):
            glob_ref[g * block : (g + 1) * block, cols] = jnp.dot(ag, gh, preferred_element_type=jnp.float32)
    value_grad = value_cols[0] if len(value_cols) == 1 else jnp.concatenate(value_cols, axis=1)
    _partial_into(value_grad, w_ref, w_copies, keep_ref, send_ref)


def _last_tick_kernel(obj_ref, att_ref, carried_ref, w_hbm, *rest, heads_local, block, groups, phases):
    pieces = rest[:groups]
    keep_ref, send_ref, glob_ref, grad_out_ref, w_ref, w_sem = rest[groups:]
    w_copies = _fetch_weights(w_hbm, w_ref, w_sem)
    band_rows = BAND * block
    arrived = pieces[0][...].astype(jnp.float32)
    for piece in pieces[1:]:
        arrived = arrived + piece[...].astype(jnp.float32)
    last = jnp.zeros((1, 1), jnp.int32) + (lax.axis_index("segment") == phases - 1).astype(jnp.int32)
    fresh = _pick_columns(obj_ref, grad_out_ref.shape[1])
    grad = jnp.where(last > 0, fresh, arrived.astype(jnp.bfloat16))
    grad_out_ref[...] = grad
    value_cols = []
    for h in range(heads_local):
        cols = slice(h * CHANNEL_WIDTH, (h + 1) * CHANNEL_WIDTH)
        gh = grad[:, cols]
        own = carried_ref[:, cols] + jnp.dot(att_ref[h, 0:block, :], gh, preferred_element_type=jnp.float32)
        value_cols.append(own.astype(jnp.bfloat16))
        for g in range(GLOB):
            lo = band_rows + g * block
            glob_ref[g * block : (g + 1) * block, cols] = jnp.dot(
                att_ref[h, lo : lo + block, :], gh, preferred_element_type=jnp.float32
            )
    value_grad = value_cols[0] if len(value_cols) == 1 else jnp.concatenate(value_cols, axis=1)
    _partial_into(value_grad, w_ref, w_copies, keep_ref, send_ref)


ANY = pl.BlockSpec(memory_space=pl.ANY)
VMEM = pl.BlockSpec(memory_space=pltpu.VMEM)
KERNEL_PARAMS = pltpu.CompilerParams()


def first_tick(initial_segment, digest_pointer, softness, window_inputs, summary_blocks, asker, lookup, prior, weights, entering):
    block = summary_blocks.shape[1]
    local_width = asker.shape[1]
    heads_local = local_width // CHANNEL_WIDTH
    groups = weights.shape[0]
    keys_total = (BAND + GLOB) * block
    feat = window_inputs.shape[1]
    flops = 2 * feat * local_width * (block + keys_total) + 14 * keys_total * block * local_width + 4 * block * local_width * groups * local_width
    ins = [initial_segment, digest_pointer, softness, window_inputs, summary_blocks, asker, lookup, entering, prior, weights]
    return pl.pallas_call(
        functools.partial(_first_tick_kernel, heads_local=heads_local, block=block),
        out_shape=(
            jax.ShapeDtypeStruct((groups, block, local_width), jnp.bfloat16),
            jax.ShapeDtypeStruct((groups, block, local_width), jnp.bfloat16),
            jax.ShapeDtypeStruct((block, local_width), jnp.float32),
            jax.ShapeDtypeStruct((GLOB * block, local_width), jnp.float32),
            jax.ShapeDtypeStruct((block, local_width), entering.dtype),
        ),
        in_specs=[VMEM] * (len(ins) - 1) + [ANY],
        out_specs=(VMEM, VMEM, VMEM, VMEM, VMEM),
        scratch_shapes=[pltpu.VMEM(weights.shape, weights.dtype), pltpu.SemaphoreType.DMA((2 * groups,))],
        compiler_params=KERNEL_PARAMS,
        cost_estimate=pl.CostEstimate(flops=flops, transcendentals=keys_total * block * heads_local, bytes_accessed=weights.size * 2 + 8 * block * local_width * 4),
    )(*ins)


def last_tick(att, carried, weights, objective, pieces, phases):
    heads_local, keys_total, block = att.shape
    local_width = carried.shape[1]
    groups = weights.shape[0]
    flops = 2 * keys_total * block * local_width + 4 * block * local_width * groups * local_width
    ins = [objective, att, carried, weights] + list(pieces)
    return pl.pallas_call(
        functools.partial(_last_tick_kernel, heads_local=heads_local, block=block, groups=len(pieces), phases=phases),
        out_shape=(
            jax.ShapeDtypeStruct((groups, block, local_width), jnp.bfloat16),
            jax.ShapeDtypeStruct((groups, block, local_width), jnp.bfloat16),
            jax.ShapeDtypeStruct((GLOB * block, local_width), jnp.float32),
            jax.ShapeDtypeStruct((block, local_width), objective.dtype),
        ),
        in_specs=[VMEM, VMEM, VMEM, ANY] + [VMEM] * len(pieces),
        out_specs=(VMEM, VMEM, VMEM, VMEM),
        scratch_shapes=[pltpu.VMEM(weights.shape, weights.dtype), pltpu.SemaphoreType.DMA((2 * groups,))],
        compiler_params=KERNEL_PARAMS,
        cost_estimate=pl.CostEstimate(flops=flops, transcendentals=0, bytes_accessed=weights.size * 2 + att.size * 2 + 8 * block * local_width * 4),
    )(*ins)


def attention_weights(tick, initial_segment, digest_pointer, softness, window_inputs, summary_blocks, asker, lookup):
    block = summary_blocks.shape[1]
    local_width = asker.shape[1]
    heads_local = local_width // CHANNEL_WIDTH
    keys_total = (BAND + GLOB) * block
    feat = window_inputs.shape[1]
    flops = 2 * feat * local_width * (block + keys_total) + 12 * keys_total * block * local_width
    ins = [initial_segment, digest_pointer, softness, window_inputs, summary_blocks, asker, lookup]
    return pl.pallas_call(
        functools.partial(_weights_kernel, tick=tick, heads_local=heads_local, block=block),
        out_shape=jax.ShapeDtypeStruct((heads_local, keys_total, block), jnp.bfloat16),
        in_specs=[VMEM] * len(ins),
        out_specs=VMEM,
        compiler_params=KERNEL_PARAMS,
        cost_estimate=pl.CostEstimate(flops=flops, transcendentals=keys_total * block * heads_local, bytes_accessed=keys_total * local_width * 2 + 4 * feat * local_width * 2),
    )(*ins)


def local(
    entering_deriv,
    objective_derivs,
    content_projection,
    asker_projection,
    lookup_projection,
    softness,
    window_inputs,
    digest_inputs,
    digest_pointer,
    initial_segment,
    prior_content_derivs,
):
    period_label = lax.axis_index("segment")
    phases = lax.axis_size("segment")
    head_group = lax.axis_index("head")
    heads = lax.axis_size("head")
    groups = heads // 2
    block_rows = entering_deriv.shape[0]
    local_width = content_projection.shape[1]
    summary_blocks = digest_inputs.reshape(SUMMARY, block_rows, digest_inputs.shape[1])
    weights = content_projection.reshape(groups, 2, local_width, local_width)
    summary_ids = jnp.arange(SUMMARY, dtype=jnp.int32)

    def live_of(tick_index):
        position = initial_segment[0] - period_label - tick_index
        return jnp.minimum(GLOB, 1 + GLOB * position // SEQ_BLOCKS)

    def digest_of(tick_index, glob):
        selector = (digest_pointer[tick_index][:, None] == summary_ids[None, :]).astype(jnp.float32)
        return jnp.sum(
            selector[:, :, None, None] * glob.reshape(GLOB, block_rows, local_width)[:, None], axis=0
        ).reshape(SUMMARY * block_rows, local_width)

    init = initial_segment.reshape(1, 1)
    keep0, send0, carried, glob0, grad0 = first_tick(
        init, digest_pointer, softness, window_inputs, summary_blocks,
        asker_projection, lookup_projection, prior_content_derivs, weights, entering_deriv,
    )
    feats = (window_inputs, asker_projection, lookup_projection)
    halves = core_pair_sum(keep0, send0)
    halves, feats = lax.optimization_barrier((halves, feats))
    later_att = attention_weights(
        1, init, digest_pointer, softness, feats[0], summary_blocks, feats[1], feats[2]
    )
    pieces = shift_down_sum(halves, grad0.astype(jnp.float32))
    digest_running = digest_of(0, glob0)
    keep1, send1, glob1, grad1 = last_tick(
        later_att, carried, weights, objective_derivs[0:block_rows], pieces, phases
    )
    digest_running = digest_running + digest_of(1, glob1)
    summed = across_groups_sum(core_pair_sum(keep1, send1))
    result = (grad1.astype(jnp.float32) + summed).astype(jnp.bfloat16)
    return (result, digest_running.astype(jnp.bfloat16))


def solution(mesh):
    in_specs = (
        P("segment", None),
        P(),
        P("segment", "head"),
        P("segment", "head"),
        P("segment", "head"),
        P("segment", "head"),
        P("segment", None),
        P(),
        P("segment", None),
        P(),
        P("segment", "head"),
    )
    out_specs = (P("segment", "head"), P("segment", "head"))
    return jax.shard_map(local, mesh=mesh, in_specs=in_specs, out_specs=out_specs, check_vma=False)
```

```python
import jax
import jax.numpy as jnp
from jax import lax
from jax.sharding import PartitionSpec as P
from jax.experimental import pallas as pl
from jax.experimental.pallas import tpu as pltpu
import functools

CHANNEL_WIDTH = 128
BAND = 4
GLOB = 2
SUMMARY = 2
SEQ_BLOCKS = 1024
TICKS = 2


EPS = 1e-06


def shifted(value, axis, steps):
    count = lax.axis_size(axis)
    first, last = (max(0, -steps), min(count, count - steps))
    return lax.ppermute(value, axis, [(source, source + steps) for source in range(first, last)])


def core_pair_sum(keep, send):
    heads = lax.axis_size("head")
    got = lax.ppermute(send, "head", [(h, h ^ 1) for h in range(heads)])
    return keep.astype(jnp.float32) + got.astype(jnp.float32)


def across_groups_sum(halves):
    head_group = lax.axis_index("head")
    heads = lax.axis_size("head")
    groups = heads // 2
    outer = head_group // 2
    total = lax.dynamic_index_in_dim(halves, outer, 0, keepdims=False)
    for step in range(1, groups):
        target = (outer + step) % groups
        piece = lax.dynamic_index_in_dim(halves, target, 0, keepdims=False).astype(jnp.bfloat16)
        pairs = [(h, (((h // 2) + step) % groups) * 2 + h % 2) for h in range(heads)]
        total = total + lax.ppermute(piece, "head", pairs).astype(jnp.float32)
    return total


def shift_down_sum(halves, entering):
    head_group = lax.axis_index("head")
    heads = lax.axis_size("head")
    segments = lax.axis_size("segment")
    groups = heads // 2
    outer = head_group // 2
    total = []
    for step in range(groups):
        target = (outer + step) % groups
        piece = lax.dynamic_index_in_dim(halves, target, 0, keepdims=False)
        if step == 0:
            piece = piece + entering
        pairs = []
        for s in range(1, segments):
            for h in range(heads):
                dest = (((h // 2) + step) % groups) * 2 + h % 2
                pairs.append((s * heads + h, (s - 1) * heads + dest))
        total.append(lax.ppermute(piece.astype(jnp.bfloat16), ("segment", "head"), pairs))
    return total


def row_norm(values):
    return values * lax.rsqrt(jnp.mean(values * values, axis=-1, keepdims=True) + EPS)


def _live_of(init_ref, tick):
    position = init_ref[...] - lax.axis_index("segment") - tick
    shift = SEQ_BLOCKS.bit_length() - 1
    return jnp.minimum(GLOB, 1 + lax.shift_right_arithmetic(GLOB * position, jnp.int32(shift)))


def _pick_columns(full_ref, width):
    head = jnp.zeros((1, 1), jnp.int32) + lax.axis_index("head")
    picked = full_ref[:, 0:width]
    for j in range(1, full_ref.shape[1] // width):
        picked = jnp.where(head == j, full_ref[:, j * width : (j + 1) * width], picked)
    return picked


def _attention_weights(init_ref, ptr_ref, soft_ref, win_ref, summ_ref, ask_ref, look_ref, *, tick, heads_local, block):
    band_rows = BAND * block
    live = _live_of(init_ref, tick)
    own = win_ref[tick * block : (tick + 1) * block, :]
    band = win_ref[tick * block : tick * block + band_rows, :]
    queries = jnp.dot(own, ask_ref[...], preferred_element_type=jnp.float32)
    band_keys = jnp.dot(band, look_ref[...], preferred_element_type=jnp.float32)
    summary_keys = [
        jnp.dot(summ_ref[m], look_ref[...], preferred_element_type=jnp.float32) for m in range(summ_ref.shape[0])
    ]
    glob_keys = []
    for g in range(GLOB):
        slot = ptr_ref[tick : tick + 1, g : g + 1]
        picked = summary_keys[0]
        for m in range(1, len(summary_keys)):
            picked = jnp.where(slot == m, summary_keys[m], picked)
        glob_keys.append(picked)
    keys_total = band_rows + GLOB * block
    key_ids = lax.broadcasted_iota(jnp.int32, (keys_total, block), 0)
    query_ids = lax.broadcasted_iota(jnp.int32, (keys_total, block), 1)
    slot_of = (key_ids - band_rows) // block
    admitted = ((key_ids < band_rows) & ((key_ids >= block) | (key_ids <= query_ids))) | (
        (key_ids >= band_rows) & (slot_of < live)
    )
    all_keys = jnp.concatenate([band_keys] + glob_keys, axis=0)
    contract = (((1,), (1,)), ((), ()))
    for h in range(heads_local):
        cols = slice(h * CHANNEL_WIDTH, (h + 1) * CHANNEL_WIDTH)
        scale = soft_ref[0:1, h : h + 1] * (1.0 / CHANNEL_WIDTH)
        qh = row_norm(queries[:, cols])
        kh = row_norm(all_keys[:, cols])
        sc = lax.dot_general(kh, qh, contract, precision=lax.Precision.HIGHEST, preferred_element_type=jnp.float32) * scale
        ex = jnp.where(admitted, jnp.exp(sc), 0.0)
        att = (ex / jnp.sum(ex, axis=0, keepdims=True)).astype(jnp.bfloat16)
        yield h, att[0:band_rows], [att[band_rows + g * block : band_rows + (g + 1) * block] for g in range(GLOB)]


def _weights_kernel(init_ref, ptr_ref, soft_ref, win_ref, summ_ref, ask_ref, look_ref, out_ref, *, tick, heads_local, block):
    for h, ab, ags in _attention_weights(
        init_ref, ptr_ref, soft_ref, win_ref, summ_ref, ask_ref, look_ref, tick=tick, heads_local=heads_local, block=block
    ):
        out_ref[h, 0:block, :] = ab[0:block]
        for g, ag in enumerate(ags):
            lo = (1 + g) * block
            out_ref[h, lo : lo + block, :] = ag


def _partial_into(value_grad, w_ref, keep_ref, send_ref):
    contract = (((1,), (1,)), ((), ()))
    core = jnp.zeros((1, 1), jnp.int32) + lax.axis_index("head") % 2
    for g in range(w_ref.shape[0]):
        even, odd = [
            lax.dot_general(value_grad, w_ref[g, p], contract, preferred_element_type=jnp.float32).astype(keep_ref.dtype)
            for p in range(2)
        ]
        keep_ref[g] = jnp.where(core == 0, even, odd)
        send_ref[g] = jnp.where(core == 0, odd, even)


def _first_tick_kernel(
    init_ref, ptr_ref, soft_ref, win_ref, summ_ref, ask_ref, look_ref, ent_ref, prior_ref, w_hbm,
    keep_ref, send_ref, carried_ref, glob_ref, grad_out_ref, w_ref, w_sem, *, heads_local, block
):
    w_copy = pltpu.make_async_copy(w_hbm, w_ref, w_sem)
    w_copy.start()
    weights = list(_attention_weights(
        init_ref, ptr_ref, soft_ref, win_ref, summ_ref, ask_ref, look_ref, tick=0, heads_local=heads_local, block=block
    ))
    grad = _pick_columns(ent_ref, grad_out_ref.shape[1])
    grad_out_ref[...] = grad
    value_cols = []
    for h, ab, ags in weights:
        cols = slice(h * CHANNEL_WIDTH, (h + 1) * CHANNEL_WIDTH)
        gh = grad[:, cols]
        band = jnp.dot(ab, gh, preferred_element_type=jnp.float32)
        own = prior_ref[0:block, cols].astype(jnp.float32) + band[0:block]
        value_cols.append(own.astype(jnp.bfloat16))
        carried_ref[:, cols] = prior_ref[block : 2 * block, cols].astype(jnp.float32) + band[block : 2 * block]
        for g, ag in enumerate(ags):
            glob_ref[g * block : (g + 1) * block, cols] = jnp.dot(ag, gh, preferred_element_type=jnp.float32)
    value_grad = value_cols[0] if len(value_cols) == 1 else jnp.concatenate(value_cols, axis=1)
    w_copy.wait()
    _partial_into(value_grad, w_ref, keep_ref, send_ref)


def _last_tick_kernel(obj_ref, att_ref, carried_ref, w_hbm, *rest, heads_local, block, groups, phases):
    pieces = rest[:groups]
    keep_ref, send_ref, glob_ref, grad_out_ref, w_ref, w_sem = rest[groups:]
    w_copy = pltpu.make_async_copy(w_hbm, w_ref, w_sem)
    w_copy.start()
    band_rows = BAND * block
    arrived = pieces[0][...].astype(jnp.float32)
    for piece in pieces[1:]:
        arrived = arrived + piece[...].astype(jnp.float32)
    last = jnp.zeros((1, 1), jnp.int32) + (lax.axis_index("segment") == phases - 1).astype(jnp.int32)
    fresh = obj_ref[...]
    grad = jnp.where(last > 0, fresh, arrived.astype(jnp.bfloat16))
    grad_out_ref[...] = grad
    value_cols = []
    for h in range(heads_local):
        cols = slice(h * CHANNEL_WIDTH, (h + 1) * CHANNEL_WIDTH)
        gh = grad[:, cols]
        own = carried_ref[:, cols] + jnp.dot(att_ref[h, 0:block, :], gh, preferred_element_type=jnp.float32)
        value_cols.append(own.astype(jnp.bfloat16))
        for g in range(GLOB):
            lo = (1 + g) * block
            glob_ref[g * block : (g + 1) * block, cols] = jnp.dot(
                att_ref[h, lo : lo + block, :], gh, preferred_element_type=jnp.float32
            )
    value_grad = value_cols[0] if len(value_cols) == 1 else jnp.concatenate(value_cols, axis=1)
    w_copy.wait()
    _partial_into(value_grad, w_ref, keep_ref, send_ref)


ANY = pl.BlockSpec(memory_space=pl.ANY)
VMEM = pl.BlockSpec(memory_space=pltpu.VMEM)
KERNEL_PARAMS = pltpu.CompilerParams()


def first_tick(initial_segment, digest_pointer, softness, window_inputs, summary_blocks, asker, lookup, prior, weights, entering):
    block = summary_blocks.shape[1]
    local_width = asker.shape[1]
    heads_local = local_width // CHANNEL_WIDTH
    groups = weights.shape[0]
    keys_total = (BAND + GLOB) * block
    feat = window_inputs.shape[1]
    flops = 2 * feat * local_width * (block + keys_total) + 14 * keys_total * block * local_width + 4 * block * local_width * groups * local_width
    ins = [initial_segment, digest_pointer, softness, window_inputs, summary_blocks, asker, lookup, entering, prior, weights]
    return pl.pallas_call(
        functools.partial(_first_tick_kernel, heads_local=heads_local, block=block),
        out_shape=(
            jax.ShapeDtypeStruct((groups, block, local_width), jnp.bfloat16),
            jax.ShapeDtypeStruct((groups, block, local_width), jnp.bfloat16),
            jax.ShapeDtypeStruct((block, local_width), jnp.float32),
            jax.ShapeDtypeStruct((GLOB * block, local_width), jnp.float32),
            jax.ShapeDtypeStruct((block, local_width), entering.dtype),
        ),
        in_specs=[VMEM] * (len(ins) - 1) + [ANY],
        out_specs=(VMEM, VMEM, VMEM, VMEM, VMEM),
        scratch_shapes=[pltpu.VMEM(weights.shape, weights.dtype), pltpu.SemaphoreType.DMA(())],
        compiler_params=KERNEL_PARAMS,
        cost_estimate=pl.CostEstimate(flops=flops, transcendentals=keys_total * block * heads_local, bytes_accessed=weights.size * 2 + 8 * block * local_width * 4),
    )(*ins)


def last_tick(att, carried, weights, objective, pieces, phases):
    heads_local, keys_total, block = att.shape
    local_width = carried.shape[1]
    groups = weights.shape[0]
    flops = 2 * keys_total * block * local_width + 4 * block * local_width * groups * local_width
    ins = [objective, att, carried, weights] + list(pieces)
    return pl.pallas_call(
        functools.partial(_last_tick_kernel, heads_local=heads_local, block=block, groups=len(pieces), phases=phases),
        out_shape=(
            jax.ShapeDtypeStruct((groups, block, local_width), jnp.bfloat16),
            jax.ShapeDtypeStruct((groups, block, local_width), jnp.bfloat16),
            jax.ShapeDtypeStruct((GLOB * block, local_width), jnp.float32),
            jax.ShapeDtypeStruct((block, local_width), objective.dtype),
        ),
        in_specs=[VMEM, VMEM, VMEM, ANY] + [VMEM] * len(pieces),
        out_specs=(VMEM, VMEM, VMEM, VMEM),
        scratch_shapes=[pltpu.VMEM(weights.shape, weights.dtype), pltpu.SemaphoreType.DMA(())],
        compiler_params=KERNEL_PARAMS,
        cost_estimate=pl.CostEstimate(flops=flops, transcendentals=0, bytes_accessed=weights.size * 2 + att.size * 2 + 8 * block * local_width * 4),
    )(*ins)


def attention_weights(tick, initial_segment, digest_pointer, softness, window_inputs, summary_blocks, asker, lookup):
    block = summary_blocks.shape[1]
    local_width = asker.shape[1]
    heads_local = local_width // CHANNEL_WIDTH
    keys_total = (BAND + GLOB) * block
    feat = window_inputs.shape[1]
    flops = 2 * feat * local_width * (block + keys_total) + 12 * keys_total * block * local_width
    ins = [initial_segment, digest_pointer, softness, window_inputs, summary_blocks, asker, lookup]
    return pl.pallas_call(
        functools.partial(_weights_kernel, tick=tick, heads_local=heads_local, block=block),
        out_shape=jax.ShapeDtypeStruct((heads_local, (1 + GLOB) * block, block), jnp.bfloat16),
        in_specs=[VMEM] * len(ins),
        out_specs=VMEM,
        compiler_params=KERNEL_PARAMS,
        cost_estimate=pl.CostEstimate(flops=flops, transcendentals=keys_total * block * heads_local, bytes_accessed=keys_total * local_width * 2 + 4 * feat * local_width * 2),
    )(*ins)


def local(
    entering_deriv,
    objective_derivs,
    content_projection,
    asker_projection,
    lookup_projection,
    softness,
    window_inputs,
    digest_inputs,
    digest_pointer,
    initial_segment,
    prior_content_derivs,
):
    period_label = lax.axis_index("segment")
    phases = lax.axis_size("segment")
    head_group = lax.axis_index("head")
    heads = lax.axis_size("head")
    groups = heads // 2
    block_rows = entering_deriv.shape[0]
    local_width = content_projection.shape[1]
    summary_blocks = digest_inputs.reshape(SUMMARY, block_rows, digest_inputs.shape[1])
    weights = content_projection.reshape(groups, 2, local_width, local_width)
    summary_ids = jnp.arange(SUMMARY, dtype=jnp.int32)

    def live_of(tick_index):
        position = initial_segment[0] - period_label - tick_index
        return jnp.minimum(GLOB, 1 + GLOB * position // SEQ_BLOCKS)

    def digest_of(tick_index, glob):
        selector = (digest_pointer[tick_index][:, None] == summary_ids[None, :]).astype(jnp.float32)
        return jnp.sum(
            selector[:, :, None, None] * glob.reshape(GLOB, block_rows, local_width)[:, None], axis=0
        ).reshape(SUMMARY * block_rows, local_width)

    init = initial_segment.reshape(1, 1)
    keep0, send0, carried, glob0, grad0 = first_tick(
        init, digest_pointer, softness, window_inputs, summary_blocks,
        asker_projection, lookup_projection, prior_content_derivs, weights, entering_deriv,
    )
    feats = (window_inputs, asker_projection, lookup_projection)
    halves = core_pair_sum(keep0, send0)
    halves, feats = lax.optimization_barrier((halves, feats))
    later_att = attention_weights(
        1, init, digest_pointer, softness, feats[0], summary_blocks, feats[1], feats[2]
    )
    pieces = shift_down_sum(halves, grad0.astype(jnp.float32))
    digest_running = digest_of(0, glob0)
    keep1, send1, glob1, grad1 = last_tick(
        later_att, carried, weights,
        lax.dynamic_slice_in_dim(objective_derivs[0:block_rows], head_group * local_width, local_width, 1),
        pieces, phases
    )
    digest_running = digest_running + digest_of(1, glob1)
    summed = across_groups_sum(core_pair_sum(keep1, send1))
    result = (grad1.astype(jnp.float32) + summed).astype(jnp.bfloat16)
    return (result, digest_running.astype(jnp.bfloat16))


def solution(mesh):
    in_specs = (
        P("segment", None),
        P(),
        P("segment", "head"),
        P("segment", "head"),
        P("segment", "head"),
        P("segment", "head"),
        P("segment", None),
        P(),
        P("segment", None),
        P(),
        P("segment", "head"),
    )
    out_specs = (P("segment", "head"), P("segment", "head"))
    return jax.shard_map(local, mesh=mesh, in_specs=in_specs, out_specs=out_specs, check_vma=False)
```

```python
import jax
import jax.numpy as jnp
from jax import lax
from jax.sharding import PartitionSpec as P
from jax.experimental import pallas as pl
from jax.experimental.pallas import tpu as pltpu
import functools

CHANNEL_WIDTH = 128
BAND = 4
GLOB = 2
SUMMARY = 2
SEQ_BLOCKS = 1024
TICKS = 2


EPS = 1e-06


def shifted(value, axis, steps):
    count = lax.axis_size(axis)
    first, last = (max(0, -steps), min(count, count - steps))
    return lax.ppermute(value, axis, [(source, source + steps) for source in range(first, last)])


def core_pair_sum(keep, send):
    heads = lax.axis_size("head")
    got = lax.ppermute(send, "head", [(h, h ^ 1) for h in range(heads)])
    return keep.astype(jnp.float32) + got.astype(jnp.float32)


def across_groups_sum(halves):
    head_group = lax.axis_index("head")
    heads = lax.axis_size("head")
    groups = heads // 2
    outer = head_group // 2
    total = lax.dynamic_index_in_dim(halves, outer, 0, keepdims=False)
    for step in range(1, groups):
        target = (outer + step) % groups
        piece = lax.dynamic_index_in_dim(halves, target, 0, keepdims=False).astype(jnp.bfloat16)
        pairs = [(h, (((h // 2) + step) % groups) * 2 + h % 2) for h in range(heads)]
        total = total + lax.ppermute(piece, "head", pairs).astype(jnp.float32)
    return total


def shift_down_sum(keep, send, entering):
    head_group = lax.axis_index("head")
    heads = lax.axis_size("head")
    segments = lax.axis_size("segment")
    groups = heads // 2
    outer = head_group // 2
    got = lax.ppermute(send, "head", [(h, h ^ 1) for h in range(heads)])
    total = []
    for step in range(groups):
        target = (outer + step) % groups
        piece = lax.dynamic_index_in_dim(keep, target, 0, keepdims=False).astype(jnp.float32) + lax.dynamic_index_in_dim(
            got, target, 0, keepdims=False
        ).astype(jnp.float32)
        if step == 0:
            piece = piece + entering
        pairs = []
        for s in range(1, segments):
            for h in range(heads):
                dest = (((h // 2) + step) % groups) * 2 + h % 2
                pairs.append((s * heads + h, (s - 1) * heads + dest))
        total.append(lax.ppermute(piece.astype(jnp.bfloat16), ("segment", "head"), pairs))
    return total, got
def row_norm(values):
    return values * lax.rsqrt(jnp.mean(values * values, axis=-1, keepdims=True) + EPS)


def _live_of(init_ref, tick):
    position = init_ref[...] - lax.axis_index("segment") - tick
    shift = SEQ_BLOCKS.bit_length() - 1
    return jnp.minimum(GLOB, 1 + lax.shift_right_arithmetic(GLOB * position, jnp.int32(shift)))


def _pick_columns(full_ref, width):
    head = jnp.zeros((1, 1), jnp.int32) + lax.axis_index("head")
    picked = full_ref[:, 0:width]
    for j in range(1, full_ref.shape[1] // width):
        picked = jnp.where(head == j, full_ref[:, j * width : (j + 1) * width], picked)
    return picked


def _attention_weights(init_ref, ptr_ref, soft_ref, win_ref, summ_ref, ask_ref, look_ref, *, tick, heads_local, block):
    band_rows = BAND * block
    live = _live_of(init_ref, tick)
    own = win_ref[tick * block : (tick + 1) * block, :]
    band = win_ref[tick * block : tick * block + band_rows, :]
    queries = jnp.dot(own, ask_ref[...], preferred_element_type=jnp.float32)
    band_keys = jnp.dot(band, look_ref[...], preferred_element_type=jnp.float32)
    summary_keys = [
        jnp.dot(summ_ref[m], look_ref[...], preferred_element_type=jnp.float32) for m in range(summ_ref.shape[0])
    ]
    glob_keys = []
    for g in range(GLOB):
        slot = ptr_ref[tick : tick + 1, g : g + 1]
        picked = summary_keys[0]
        for m in range(1, len(summary_keys)):
            picked = jnp.where(slot == m, summary_keys[m], picked)
        glob_keys.append(picked)
    keys_total = band_rows + GLOB * block
    key_ids = lax.broadcasted_iota(jnp.int32, (keys_total, block), 0)
    query_ids = lax.broadcasted_iota(jnp.int32, (keys_total, block), 1)
    slot_of = (key_ids - band_rows) // block
    admitted = ((key_ids < band_rows) & ((key_ids >= block) | (key_ids <= query_ids))) | (
        (key_ids >= band_rows) & (slot_of < live)
    )
    all_keys = jnp.concatenate([band_keys] + glob_keys, axis=0)
    contract = (((1,), (1,)), ((), ()))
    for h in range(heads_local):
        cols = slice(h * CHANNEL_WIDTH, (h + 1) * CHANNEL_WIDTH)
        scale = soft_ref[0:1, h : h + 1] * (1.0 / CHANNEL_WIDTH)
        qh = row_norm(queries[:, cols])
        kh = row_norm(all_keys[:, cols])
        sc = lax.dot_general(kh, qh, contract, precision=lax.Precision.HIGHEST, preferred_element_type=jnp.float32) * scale
        ex = jnp.where(admitted, jnp.exp(sc), 0.0)
        att = (ex / jnp.sum(ex, axis=0, keepdims=True)).astype(jnp.bfloat16)
        yield h, att[0:band_rows], [att[band_rows + g * block : band_rows + (g + 1) * block] for g in range(GLOB)]


def _weights_kernel(init_ref, ptr_ref, soft_ref, win_ref, summ_ref, ask_ref, look_ref, out_ref, *, tick, heads_local, block):
    for h, ab, ags in _attention_weights(
        init_ref, ptr_ref, soft_ref, win_ref, summ_ref, ask_ref, look_ref, tick=tick, heads_local=heads_local, block=block
    ):
        out_ref[h, 0:block, :] = ab[0:block]
        for g, ag in enumerate(ags):
            lo = (1 + g) * block
            out_ref[h, lo : lo + block, :] = ag


def _partial_into(value_grad, w_ref, keep_ref, send_ref):
    contract = (((1,), (1,)), ((), ()))
    core = jnp.zeros((1, 1), jnp.int32) + lax.axis_index("head") % 2
    for g in range(w_ref.shape[0]):
        even, odd = [
            lax.dot_general(value_grad, w_ref[g, p], contract, preferred_element_type=jnp.float32).astype(keep_ref.dtype)
            for p in range(2)
        ]
        keep_ref[g] = jnp.where(core == 0, even, odd)
        send_ref[g] = jnp.where(core == 0, odd, even)


def _first_tick_kernel(
    init_ref, ptr_ref, soft_ref, win_ref, summ_ref, ask_ref, look_ref, ent_ref, prior_ref, w_hbm,
    keep_ref, send_ref, carried_ref, glob_ref, grad_out_ref, w_ref, w_sem, *, heads_local, block
):
    w_copy = pltpu.make_async_copy(w_hbm, w_ref, w_sem)
    w_copy.start()
    weights = list(_attention_weights(
        init_ref, ptr_ref, soft_ref, win_ref, summ_ref, ask_ref, look_ref, tick=0, heads_local=heads_local, block=block
    ))
    grad = _pick_columns(ent_ref, grad_out_ref.shape[1])
    grad_out_ref[...] = grad
    value_cols = []
    for h, ab, ags in weights:
        cols = slice(h * CHANNEL_WIDTH, (h + 1) * CHANNEL_WIDTH)
        gh = grad[:, cols]
        band = jnp.dot(ab, gh, preferred_element_type=jnp.float32)
        own = prior_ref[0:block, cols].astype(jnp.float32) + band[0:block]
        value_cols.append(own.astype(jnp.bfloat16))
        carried_ref[:, cols] = prior_ref[block : 2 * block, cols].astype(jnp.float32) + band[block : 2 * block]
        for g, ag in enumerate(ags):
            glob_ref[g * block : (g + 1) * block, cols] = jnp.dot(ag, gh, preferred_element_type=jnp.float32)
    value_grad = value_cols[0] if len(value_cols) == 1 else jnp.concatenate(value_cols, axis=1)
    w_copy.wait()
    _partial_into(value_grad, w_ref, keep_ref, send_ref)


def _last_tick_kernel(obj_ref, att_ref, carried_ref, w_hbm, *rest, heads_local, block, groups, phases):
    pieces = rest[:groups]
    keep_ref, send_ref, glob_ref, grad_out_ref, w_ref, w_sem = rest[groups:]
    w_copy = pltpu.make_async_copy(w_hbm, w_ref, w_sem)
    w_copy.start()
    band_rows = BAND * block
    arrived = pieces[0][...].astype(jnp.float32)
    for piece in pieces[1:]:
        arrived = arrived + piece[...].astype(jnp.float32)
    last = jnp.zeros((1, 1), jnp.int32) + (lax.axis_index("segment") == phases - 1).astype(jnp.int32)
    fresh = obj_ref[...]
    grad = jnp.where(last > 0, fresh, arrived.astype(jnp.bfloat16))
    grad_out_ref[...] = grad
    value_cols = []
    for h in range(heads_local):
        cols = slice(h * CHANNEL_WIDTH, (h + 1) * CHANNEL_WIDTH)
        gh = grad[:, cols]
        own = carried_ref[:, cols] + jnp.dot(att_ref[h, 0:block, :], gh, preferred_element_type=jnp.float32)
        value_cols.append(own.astype(jnp.bfloat16))
        for g in range(GLOB):
            lo = (1 + g) * block
            glob_ref[g * block : (g + 1) * block, cols] = jnp.dot(
                att_ref[h, lo : lo + block, :], gh, preferred_element_type=jnp.float32
            )
    value_grad = value_cols[0] if len(value_cols) == 1 else jnp.concatenate(value_cols, axis=1)
    w_copy.wait()
    _partial_into(value_grad, w_ref, keep_ref, send_ref)


ANY = pl.BlockSpec(memory_space=pl.ANY)
VMEM = pl.BlockSpec(memory_space=pltpu.VMEM)
KERNEL_PARAMS = pltpu.CompilerParams()


def first_tick(initial_segment, digest_pointer, softness, window_inputs, summary_blocks, asker, lookup, prior, weights, entering):
    block = summary_blocks.shape[1]
    local_width = asker.shape[1]
    heads_local = local_width // CHANNEL_WIDTH
    groups = weights.shape[0]
    keys_total = (BAND + GLOB) * block
    feat = window_inputs.shape[1]
    flops = 2 * feat * local_width * (block + keys_total) + 14 * keys_total * block * local_width + 4 * block * local_width * groups * local_width
    ins = [initial_segment, digest_pointer, softness, window_inputs, summary_blocks, asker, lookup, entering, prior, weights]
    return pl.pallas_call(
        functools.partial(_first_tick_kernel, heads_local=heads_local, block=block),
        out_shape=(
            jax.ShapeDtypeStruct((groups, block, local_width), jnp.bfloat16),
            jax.ShapeDtypeStruct((groups, block, local_width), jnp.bfloat16),
            jax.ShapeDtypeStruct((block, local_width), jnp.float32),
            jax.ShapeDtypeStruct((GLOB * block, local_width), jnp.float32),
            jax.ShapeDtypeStruct((block, local_width), entering.dtype),
        ),
        in_specs=[VMEM] * (len(ins) - 1) + [ANY],
        out_specs=(VMEM, VMEM, VMEM, VMEM, VMEM),
        scratch_shapes=[pltpu.VMEM(weights.shape, weights.dtype), pltpu.SemaphoreType.DMA(())],
        compiler_params=KERNEL_PARAMS,
        cost_estimate=pl.CostEstimate(flops=flops, transcendentals=keys_total * block * heads_local, bytes_accessed=weights.size * 2 + 8 * block * local_width * 4),
    )(*ins)


def last_tick(att, carried, weights, objective, pieces, phases):
    heads_local, keys_total, block = att.shape
    local_width = carried.shape[1]
    groups = weights.shape[0]
    flops = 2 * keys_total * block * local_width + 4 * block * local_width * groups * local_width
    ins = [objective, att, carried, weights] + list(pieces)
    return pl.pallas_call(
        functools.partial(_last_tick_kernel, heads_local=heads_local, block=block, groups=len(pieces), phases=phases),
        out_shape=(
            jax.ShapeDtypeStruct((groups, block, local_width), jnp.bfloat16),
            jax.ShapeDtypeStruct((groups, block, local_width), jnp.bfloat16),
            jax.ShapeDtypeStruct((GLOB * block, local_width), jnp.float32),
            jax.ShapeDtypeStruct((block, local_width), objective.dtype),
        ),
        in_specs=[VMEM, VMEM, VMEM, ANY] + [VMEM] * len(pieces),
        out_specs=(VMEM, VMEM, VMEM, VMEM),
        scratch_shapes=[pltpu.VMEM(weights.shape, weights.dtype), pltpu.SemaphoreType.DMA(())],
        compiler_params=KERNEL_PARAMS,
        cost_estimate=pl.CostEstimate(flops=flops, transcendentals=0, bytes_accessed=weights.size * 2 + att.size * 2 + 8 * block * local_width * 4),
    )(*ins)


def attention_weights(tick, initial_segment, digest_pointer, softness, window_inputs, summary_blocks, asker, lookup):
    block = summary_blocks.shape[1]
    local_width = asker.shape[1]
    heads_local = local_width // CHANNEL_WIDTH
    keys_total = (BAND + GLOB) * block
    feat = window_inputs.shape[1]
    flops = 2 * feat * local_width * (block + keys_total) + 12 * keys_total * block * local_width
    ins = [initial_segment, digest_pointer, softness, window_inputs, summary_blocks, asker, lookup]
    return pl.pallas_call(
        functools.partial(_weights_kernel, tick=tick, heads_local=heads_local, block=block),
        out_shape=jax.ShapeDtypeStruct((heads_local, (1 + GLOB) * block, block), jnp.bfloat16),
        in_specs=[VMEM] * len(ins),
        out_specs=VMEM,
        compiler_params=KERNEL_PARAMS,
        cost_estimate=pl.CostEstimate(flops=flops, transcendentals=keys_total * block * heads_local, bytes_accessed=keys_total * local_width * 2 + 4 * feat * local_width * 2),
    )(*ins)


def local(
    entering_deriv,
    objective_derivs,
    content_projection,
    asker_projection,
    lookup_projection,
    softness,
    window_inputs,
    digest_inputs,
    digest_pointer,
    initial_segment,
    prior_content_derivs,
):
    period_label = lax.axis_index("segment")
    phases = lax.axis_size("segment")
    head_group = lax.axis_index("head")
    heads = lax.axis_size("head")
    groups = heads // 2
    block_rows = entering_deriv.shape[0]
    local_width = content_projection.shape[1]
    summary_blocks = digest_inputs.reshape(SUMMARY, block_rows, digest_inputs.shape[1])
    weights = content_projection.reshape(groups, 2, local_width, local_width)
    summary_ids = jnp.arange(SUMMARY, dtype=jnp.int32)

    def live_of(tick_index):
        position = initial_segment[0] - period_label - tick_index
        return jnp.minimum(GLOB, 1 + GLOB * position // SEQ_BLOCKS)

    def digest_of(tick_index, glob):
        selector = (digest_pointer[tick_index][:, None] == summary_ids[None, :]).astype(jnp.float32)
        return jnp.sum(
            selector[:, :, None, None] * glob.reshape(GLOB, block_rows, local_width)[:, None], axis=0
        ).reshape(SUMMARY * block_rows, local_width)

    init = initial_segment.reshape(1, 1)
    keep0, send0, carried, glob0, grad0 = first_tick(
        init, digest_pointer, softness, window_inputs, summary_blocks,
        asker_projection, lookup_projection, prior_content_derivs, weights, entering_deriv,
    )
    feats = (window_inputs, asker_projection, lookup_projection)
    pieces, got0 = shift_down_sum(keep0, send0, grad0.astype(jnp.float32))
    _, feats = lax.optimization_barrier((got0, feats))
    later_att = attention_weights(
        1, init, digest_pointer, softness, feats[0], summary_blocks, feats[1], feats[2]
    )
    digest_running = digest_of(0, glob0)
    keep1, send1, glob1, grad1 = last_tick(
        later_att, carried, weights,
        lax.dynamic_slice_in_dim(objective_derivs[0:block_rows], head_group * local_width, local_width, 1),
        pieces, phases
    )
    digest_running = digest_running + digest_of(1, glob1)
    summed = across_groups_sum(core_pair_sum(keep1, send1))
    result = (grad1.astype(jnp.float32) + summed).astype(jnp.bfloat16)
    return (result, digest_running.astype(jnp.bfloat16))


def solution(mesh):
    in_specs = (
        P("segment", None),
        P(),
        P("segment", "head"),
        P("segment", "head"),
        P("segment", "head"),
        P("segment", "head"),
        P("segment", None),
        P(),
        P("segment", None),
        P(),
        P("segment", "head"),
    )
    out_specs = (P("segment", "head"), P("segment", "head"))
    return jax.shard_map(local, mesh=mesh, in_specs=in_specs, out_specs=out_specs, check_vma=False)
```

```python
import jax
import jax.numpy as jnp
from jax import lax
from jax.sharding import PartitionSpec as P
from jax.experimental import pallas as pl
from jax.experimental.pallas import tpu as pltpu
import functools

CHANNEL_WIDTH = 128
BAND = 4
GLOB = 2
SUMMARY = 2
SEQ_BLOCKS = 1024
TICKS = 2


EPS = 1e-06


def shifted(value, axis, steps):
    count = lax.axis_size(axis)
    first, last = (max(0, -steps), min(count, count - steps))
    return lax.ppermute(value, axis, [(source, source + steps) for source in range(first, last)])


def core_pair_sum(keep, send):
    heads = lax.axis_size("head")
    got = lax.ppermute(send, "head", [(h, h ^ 1) for h in range(heads)])
    return keep.astype(jnp.float32) + got.astype(jnp.float32)


def across_groups_sum(halves):
    head_group = lax.axis_index("head")
    heads = lax.axis_size("head")
    groups = heads // 2
    outer = head_group // 2
    total = lax.dynamic_index_in_dim(halves, outer, 0, keepdims=False)
    for step in range(1, groups):
        target = (outer + step) % groups
        piece = lax.dynamic_index_in_dim(halves, target, 0, keepdims=False).astype(jnp.bfloat16)
        pairs = [(h, (((h // 2) + step) % groups) * 2 + h % 2) for h in range(heads)]
        total = total + lax.ppermute(piece, "head", pairs).astype(jnp.float32)
    return total


def shift_down_sum(keep, send, entering):
    head_group = lax.axis_index("head")
    heads = lax.axis_size("head")
    segments = lax.axis_size("segment")
    groups = heads // 2
    outer = head_group // 2
    got = lax.ppermute(send, "head", [(h, h ^ 1) for h in range(heads)])
    total = []
    for step in range(groups):
        target = (outer + step) % groups
        piece = lax.dynamic_index_in_dim(keep, target, 0, keepdims=False).astype(jnp.float32) + lax.dynamic_index_in_dim(
            got, target, 0, keepdims=False
        ).astype(jnp.float32)
        if step == 0:
            piece = piece + entering
        pairs = []
        for s in range(1, segments):
            for h in range(heads):
                dest = (((h // 2) + step) % groups) * 2 + h % 2
                pairs.append((s * heads + h, (s - 1) * heads + dest))
        total.append(lax.ppermute(piece.astype(jnp.bfloat16), ("segment", "head"), pairs))
    return total, got
def row_norm(values):
    return values * lax.rsqrt(jnp.mean(values * values, axis=-1, keepdims=True) + EPS)


def _live_of(init_ref, tick):
    position = init_ref[...] - lax.axis_index("segment") - tick
    shift = SEQ_BLOCKS.bit_length() - 1
    return jnp.minimum(GLOB, 1 + lax.shift_right_arithmetic(GLOB * position, jnp.int32(shift)))


def _pick_columns(full_ref, width):
    head = jnp.zeros((1, 1), jnp.int32) + lax.axis_index("head")
    picked = full_ref[:, 0:width]
    for j in range(1, full_ref.shape[1] // width):
        picked = jnp.where(head == j, full_ref[:, j * width : (j + 1) * width], picked)
    return picked


def _attention_weights(init_ref, ptr_ref, soft_ref, win_ref, summ_ref, ask_ref, look_ref, *, tick, heads_local, block):
    band_rows = BAND * block
    live = _live_of(init_ref, tick)
    own = win_ref[tick * block : (tick + 1) * block, :]
    band = win_ref[tick * block : tick * block + band_rows, :]
    queries = jnp.dot(own, ask_ref[...], preferred_element_type=jnp.float32)
    band_keys = jnp.dot(band, look_ref[...], preferred_element_type=jnp.float32)
    summary_keys = [
        jnp.dot(summ_ref[m], look_ref[...], preferred_element_type=jnp.float32) for m in range(summ_ref.shape[0])
    ]
    glob_keys = []
    for g in range(GLOB):
        slot = ptr_ref[tick : tick + 1, g : g + 1]
        picked = summary_keys[0]
        for m in range(1, len(summary_keys)):
            picked = jnp.where(slot == m, summary_keys[m], picked)
        glob_keys.append(picked)
    keys_total = band_rows + GLOB * block
    key_ids = lax.broadcasted_iota(jnp.int32, (keys_total, block), 0)
    query_ids = lax.broadcasted_iota(jnp.int32, (keys_total, block), 1)
    slot_of = (key_ids - band_rows) // block
    admitted = ((key_ids < band_rows) & ((key_ids >= block) | (key_ids <= query_ids))) | (
        (key_ids >= band_rows) & (slot_of < live)
    )
    all_keys = jnp.concatenate([band_keys] + glob_keys, axis=0)
    contract = (((1,), (1,)), ((), ()))
    for h in range(heads_local):
        cols = slice(h * CHANNEL_WIDTH, (h + 1) * CHANNEL_WIDTH)
        scale = soft_ref[0:1, h : h + 1] * (1.0 / CHANNEL_WIDTH)
        qh = row_norm(queries[:, cols])
        kh = row_norm(all_keys[:, cols])
        sc = lax.dot_general(kh, qh, contract, precision=lax.Precision.HIGHEST, preferred_element_type=jnp.float32) * scale
        ex = jnp.where(admitted, jnp.exp(sc), 0.0)
        att = (ex / jnp.sum(ex, axis=0, keepdims=True)).astype(jnp.bfloat16)
        yield h, att[0:band_rows], [att[band_rows + g * block : band_rows + (g + 1) * block] for g in range(GLOB)]


def _weights_kernel(init_ref, ptr_ref, soft_ref, win_ref, summ_ref, ask_ref, look_ref, out_ref, *, tick, heads_local, block):
    for h, ab, ags in _attention_weights(
        init_ref, ptr_ref, soft_ref, win_ref, summ_ref, ask_ref, look_ref, tick=tick, heads_local=heads_local, block=block
    ):
        out_ref[h, 0:block, :] = ab[0:block]
        for g, ag in enumerate(ags):
            lo = (1 + g) * block
            out_ref[h, lo : lo + block, :] = ag


def _partial_into(value_grad, w_ref, keep_ref, send_ref):
    contract = (((1,), (1,)), ((), ()))
    core = jnp.zeros((1, 1), jnp.int32) + lax.axis_index("head") % 2
    for g in range(w_ref.shape[0]):
        even, odd = [
            lax.dot_general(value_grad, w_ref[g, p], contract, preferred_element_type=jnp.float32).astype(keep_ref.dtype)
            for p in range(2)
        ]
        keep_ref[g] = jnp.where(core == 0, even, odd)
        send_ref[g] = jnp.where(core == 0, odd, even)


def _first_tick_kernel(
    init_ref, ptr_ref, soft_ref, win_ref, summ_ref, ask_ref, look_ref, ent_hbm, prior_ref, w_hbm,
    keep_ref, send_ref, carried_ref, glob_ref, grad_out_ref, w_ref, w_sem, grad_buf, grad_sem, *, heads_local, block
):
    width = grad_buf.shape[1]
    start = pl.multiple_of(lax.axis_index("head") * width, CHANNEL_WIDTH)
    grad_copy = pltpu.make_async_copy(ent_hbm.at[:, pl.ds(start, width)], grad_buf, grad_sem)
    grad_copy.start()
    w_copy = pltpu.make_async_copy(w_hbm, w_ref, w_sem)
    w_copy.start()
    weights = list(_attention_weights(
        init_ref, ptr_ref, soft_ref, win_ref, summ_ref, ask_ref, look_ref, tick=0, heads_local=heads_local, block=block
    ))
    grad_copy.wait()
    grad = grad_buf[...]
    grad_out_ref[...] = grad
    value_cols = []
    for h, ab, ags in weights:
        cols = slice(h * CHANNEL_WIDTH, (h + 1) * CHANNEL_WIDTH)
        gh = grad[:, cols]
        band = jnp.dot(ab, gh, preferred_element_type=jnp.float32)
        own = prior_ref[0:block, cols].astype(jnp.float32) + band[0:block]
        value_cols.append(own.astype(jnp.bfloat16))
        carried_ref[:, cols] = prior_ref[block : 2 * block, cols].astype(jnp.float32) + band[block : 2 * block]
        for g, ag in enumerate(ags):
            glob_ref[g * block : (g + 1) * block, cols] = jnp.dot(ag, gh, preferred_element_type=jnp.float32)
    value_grad = value_cols[0] if len(value_cols) == 1 else jnp.concatenate(value_cols, axis=1)
    w_copy.wait()
    _partial_into(value_grad, w_ref, keep_ref, send_ref)


def _last_tick_kernel(obj_ref, att_ref, carried_ref, w_hbm, *rest, heads_local, block, groups, phases):
    pieces = rest[:groups]
    keep_ref, send_ref, glob_ref, grad_out_ref, w_ref, w_sem = rest[groups:]
    w_copy = pltpu.make_async_copy(w_hbm, w_ref, w_sem)
    w_copy.start()
    band_rows = BAND * block
    arrived = pieces[0][...].astype(jnp.float32)
    for piece in pieces[1:]:
        arrived = arrived + piece[...].astype(jnp.float32)
    last = jnp.zeros((1, 1), jnp.int32) + (lax.axis_index("segment") == phases - 1).astype(jnp.int32)
    fresh = obj_ref[...]
    grad = jnp.where(last > 0, fresh, arrived.astype(jnp.bfloat16))
    grad_out_ref[...] = grad
    value_cols = []
    for h in range(heads_local):
        cols = slice(h * CHANNEL_WIDTH, (h + 1) * CHANNEL_WIDTH)
        gh = grad[:, cols]
        own = carried_ref[:, cols] + jnp.dot(att_ref[h, 0:block, :], gh, preferred_element_type=jnp.float32)
        value_cols.append(own.astype(jnp.bfloat16))
        for g in range(GLOB):
            lo = (1 + g) * block
            glob_ref[g * block : (g + 1) * block, cols] = jnp.dot(
                att_ref[h, lo : lo + block, :], gh, preferred_element_type=jnp.float32
            )
    value_grad = value_cols[0] if len(value_cols) == 1 else jnp.concatenate(value_cols, axis=1)
    w_copy.wait()
    _partial_into(value_grad, w_ref, keep_ref, send_ref)


ANY = pl.BlockSpec(memory_space=pl.ANY)
VMEM = pl.BlockSpec(memory_space=pltpu.VMEM)
KERNEL_PARAMS = pltpu.CompilerParams()


def first_tick(initial_segment, digest_pointer, softness, window_inputs, summary_blocks, asker, lookup, prior, weights, entering):
    block = summary_blocks.shape[1]
    local_width = asker.shape[1]
    heads_local = local_width // CHANNEL_WIDTH
    groups = weights.shape[0]
    keys_total = (BAND + GLOB) * block
    feat = window_inputs.shape[1]
    flops = 2 * feat * local_width * (block + keys_total) + 14 * keys_total * block * local_width + 4 * block * local_width * groups * local_width
    ins = [initial_segment, digest_pointer, softness, window_inputs, summary_blocks, asker, lookup, entering, prior, weights]
    return pl.pallas_call(
        functools.partial(_first_tick_kernel, heads_local=heads_local, block=block),
        out_shape=(
            jax.ShapeDtypeStruct((groups, block, local_width), jnp.bfloat16),
            jax.ShapeDtypeStruct((groups, block, local_width), jnp.bfloat16),
            jax.ShapeDtypeStruct((block, local_width), jnp.float32),
            jax.ShapeDtypeStruct((GLOB * block, local_width), jnp.float32),
            jax.ShapeDtypeStruct((block, local_width), entering.dtype),
        ),
        in_specs=[VMEM] * 7 + [ANY, VMEM, ANY],
        out_specs=(VMEM, VMEM, VMEM, VMEM, VMEM),
        scratch_shapes=[
            pltpu.VMEM(weights.shape, weights.dtype),
            pltpu.SemaphoreType.DMA(()),
            pltpu.VMEM((block, local_width), entering.dtype),
            pltpu.SemaphoreType.DMA(()),
        ],
        compiler_params=KERNEL_PARAMS,
        cost_estimate=pl.CostEstimate(flops=flops, transcendentals=keys_total * block * heads_local, bytes_accessed=weights.size * 2 + 8 * block * local_width * 4),
    )(*ins)


def last_tick(att, carried, weights, objective, pieces, phases):
    heads_local, keys_total, block = att.shape
    local_width = carried.shape[1]
    groups = weights.shape[0]
    flops = 2 * keys_total * block * local_width + 4 * block * local_width * groups * local_width
    ins = [objective, att, carried, weights] + list(pieces)
    return pl.pallas_call(
        functools.partial(_last_tick_kernel, heads_local=heads_local, block=block, groups=len(pieces), phases=phases),
        out_shape=(
            jax.ShapeDtypeStruct((groups, block, local_width), jnp.bfloat16),
            jax.ShapeDtypeStruct((groups, block, local_width), jnp.bfloat16),
            jax.ShapeDtypeStruct((GLOB * block, local_width), jnp.float32),
            jax.ShapeDtypeStruct((block, local_width), objective.dtype),
        ),
        in_specs=[VMEM, VMEM, VMEM, ANY] + [VMEM] * len(pieces),
        out_specs=(VMEM, VMEM, VMEM, VMEM),
        scratch_shapes=[pltpu.VMEM(weights.shape, weights.dtype), pltpu.SemaphoreType.DMA(())],
        compiler_params=KERNEL_PARAMS,
        cost_estimate=pl.CostEstimate(flops=flops, transcendentals=0, bytes_accessed=weights.size * 2 + att.size * 2 + 8 * block * local_width * 4),
    )(*ins)


def attention_weights(tick, initial_segment, digest_pointer, softness, window_inputs, summary_blocks, asker, lookup):
    block = summary_blocks.shape[1]
    local_width = asker.shape[1]
    heads_local = local_width // CHANNEL_WIDTH
    keys_total = (BAND + GLOB) * block
    feat = window_inputs.shape[1]
    flops = 2 * feat * local_width * (block + keys_total) + 12 * keys_total * block * local_width
    ins = [initial_segment, digest_pointer, softness, window_inputs, summary_blocks, asker, lookup]
    return pl.pallas_call(
        functools.partial(_weights_kernel, tick=tick, heads_local=heads_local, block=block),
        out_shape=jax.ShapeDtypeStruct((heads_local, (1 + GLOB) * block, block), jnp.bfloat16),
        in_specs=[VMEM] * len(ins),
        out_specs=VMEM,
        compiler_params=KERNEL_PARAMS,
        cost_estimate=pl.CostEstimate(flops=flops, transcendentals=keys_total * block * heads_local, bytes_accessed=keys_total * local_width * 2 + 4 * feat * local_width * 2),
    )(*ins)


def local(
    entering_deriv,
    objective_derivs,
    content_projection,
    asker_projection,
    lookup_projection,
    softness,
    window_inputs,
    digest_inputs,
    digest_pointer,
    initial_segment,
    prior_content_derivs,
):
    period_label = lax.axis_index("segment")
    phases = lax.axis_size("segment")
    head_group = lax.axis_index("head")
    heads = lax.axis_size("head")
    groups = heads // 2
    block_rows = entering_deriv.shape[0]
    local_width = content_projection.shape[1]
    summary_blocks = digest_inputs.reshape(SUMMARY, block_rows, digest_inputs.shape[1])
    weights = content_projection.reshape(groups, 2, local_width, local_width)
    summary_ids = jnp.arange(SUMMARY, dtype=jnp.int32)

    def live_of(tick_index):
        position = initial_segment[0] - period_label - tick_index
        return jnp.minimum(GLOB, 1 + GLOB * position // SEQ_BLOCKS)

    def digest_of(tick_index, glob):
        selector = (digest_pointer[tick_index][:, None] == summary_ids[None, :]).astype(jnp.float32)
        return jnp.sum(
            selector[:, :, None, None] * glob.reshape(GLOB, block_rows, local_width)[:, None], axis=0
        ).reshape(SUMMARY * block_rows, local_width)

    init = initial_segment.reshape(1, 1)
    keep0, send0, carried, glob0, grad0 = first_tick(
        init, digest_pointer, softness, window_inputs, summary_blocks,
        asker_projection, lookup_projection, prior_content_derivs, weights, entering_deriv,
    )
    feats = (window_inputs, asker_projection, lookup_projection)
    pieces, got0 = shift_down_sum(keep0, send0, grad0.astype(jnp.float32))
    _, feats = lax.optimization_barrier((got0, feats))
    later_att = attention_weights(
        1, init, digest_pointer, softness, feats[0], summary_blocks, feats[1], feats[2]
    )
    digest_running = digest_of(0, glob0)
    keep1, send1, glob1, grad1 = last_tick(
        later_att, carried, weights,
        lax.dynamic_slice_in_dim(objective_derivs[0:block_rows], head_group * local_width, local_width, 1),
        pieces, phases
    )
    digest_running = digest_running + digest_of(1, glob1)
    summed = across_groups_sum(core_pair_sum(keep1, send1))
    result = (grad1.astype(jnp.float32) + summed).astype(jnp.bfloat16)
    return (result, digest_running.astype(jnp.bfloat16))


def solution(mesh):
    in_specs = (
        P("segment", None),
        P(),
        P("segment", "head"),
        P("segment", "head"),
        P("segment", "head"),
        P("segment", "head"),
        P("segment", None),
        P(),
        P("segment", None),
        P(),
        P("segment", "head"),
    )
    out_specs = (P("segment", "head"), P("segment", "head"))
    return jax.shard_map(local, mesh=mesh, in_specs=in_specs, out_specs=out_specs, check_vma=False)
```

```python
import jax
import jax.numpy as jnp
from jax import lax
from jax.sharding import PartitionSpec as P
from jax.experimental import pallas as pl
from jax.experimental.pallas import tpu as pltpu
import functools

CHANNEL_WIDTH = 128
BAND = 4
GLOB = 2
SUMMARY = 2
SEQ_BLOCKS = 1024
TICKS = 2


EPS = 1e-06


def shifted(value, axis, steps):
    count = lax.axis_size(axis)
    first, last = (max(0, -steps), min(count, count - steps))
    return lax.ppermute(value, axis, [(source, source + steps) for source in range(first, last)])


def core_pair_sum(keep, send):
    heads = lax.axis_size("head")
    got = lax.ppermute(send, "head", [(h, h ^ 1) for h in range(heads)])
    return keep.astype(jnp.float32) + got.astype(jnp.float32)


def across_groups_sum(halves):
    head_group = lax.axis_index("head")
    heads = lax.axis_size("head")
    groups = heads // 2
    outer = head_group // 2
    total = lax.dynamic_index_in_dim(halves, outer, 0, keepdims=False)
    for step in range(1, groups):
        target = (outer + step) % groups
        piece = lax.dynamic_index_in_dim(halves, target, 0, keepdims=False).astype(jnp.bfloat16)
        pairs = [(h, (((h // 2) + step) % groups) * 2 + h % 2) for h in range(heads)]
        total = total + lax.ppermute(piece, "head", pairs).astype(jnp.float32)
    return total


def shift_down_sum(keep, send, entering):
    head_group = lax.axis_index("head")
    heads = lax.axis_size("head")
    segments = lax.axis_size("segment")
    groups = heads // 2
    outer = head_group // 2
    got = lax.ppermute(send, "head", [(h, h ^ 1) for h in range(heads)])
    total = []
    for step in range(groups):
        target = (outer + step) % groups
        piece = lax.dynamic_index_in_dim(keep, target, 0, keepdims=False).astype(jnp.float32) + lax.dynamic_index_in_dim(
            got, target, 0, keepdims=False
        ).astype(jnp.float32)
        if step == 0:
            piece = piece + entering
        pairs = []
        for s in range(1, segments):
            for h in range(heads):
                dest = (((h // 2) + step) % groups) * 2 + h % 2
                pairs.append((s * heads + h, (s - 1) * heads + dest))
        total.append(lax.ppermute(piece.astype(jnp.bfloat16), ("segment", "head"), pairs))
    return total, got
def row_norm(values):
    return values * lax.rsqrt(jnp.mean(values * values, axis=-1, keepdims=True) + EPS)


def _live_of(init_ref, tick):
    position = init_ref[...] - lax.axis_index("segment") - tick
    shift = SEQ_BLOCKS.bit_length() - 1
    return jnp.minimum(GLOB, 1 + lax.shift_right_arithmetic(GLOB * position, jnp.int32(shift)))


def _pick_columns(full_ref, width):
    head = jnp.zeros((1, 1), jnp.int32) + lax.axis_index("head")
    picked = full_ref[:, 0:width]
    for j in range(1, full_ref.shape[1] // width):
        picked = jnp.where(head == j, full_ref[:, j * width : (j + 1) * width], picked)
    return picked


def _attention_weights(init_ref, ptr_ref, soft_ref, win_ref, summ_ref, ask_ref, look_ref, *, tick, heads_local, block):
    band_rows = BAND * block
    live = _live_of(init_ref, tick)
    own = win_ref[tick * block : (tick + 1) * block, :]
    band = win_ref[tick * block : tick * block + band_rows, :]
    queries = jnp.dot(own, ask_ref[...], preferred_element_type=jnp.float32)
    band_keys = jnp.dot(band, look_ref[...], preferred_element_type=jnp.float32)
    summary_keys = [
        jnp.dot(summ_ref[m], look_ref[...], preferred_element_type=jnp.float32) for m in range(summ_ref.shape[0])
    ]
    glob_keys = []
    for g in range(GLOB):
        slot = ptr_ref[tick : tick + 1, g : g + 1]
        picked = summary_keys[0]
        for m in range(1, len(summary_keys)):
            picked = jnp.where(slot == m, summary_keys[m], picked)
        glob_keys.append(picked)
    keys_total = band_rows + GLOB * block
    key_ids = lax.broadcasted_iota(jnp.int32, (keys_total, block), 0)
    query_ids = lax.broadcasted_iota(jnp.int32, (keys_total, block), 1)
    slot_of = (key_ids - band_rows) // block
    admitted = ((key_ids < band_rows) & ((key_ids >= block) | (key_ids <= query_ids))) | (
        (key_ids >= band_rows) & (slot_of < live)
    )
    all_keys = jnp.concatenate([band_keys] + glob_keys, axis=0)
    contract = (((1,), (1,)), ((), ()))
    for h in range(heads_local):
        cols = slice(h * CHANNEL_WIDTH, (h + 1) * CHANNEL_WIDTH)
        scale = soft_ref[0:1, h : h + 1] * (1.0 / CHANNEL_WIDTH)
        qh = row_norm(queries[:, cols])
        kh = row_norm(all_keys[:, cols])
        sc = lax.dot_general(kh, qh, contract, precision=lax.Precision.HIGHEST, preferred_element_type=jnp.float32) * scale
        ex = jnp.where(admitted, jnp.exp(sc), 0.0)
        att = (ex / jnp.sum(ex, axis=0, keepdims=True)).astype(jnp.bfloat16)
        yield h, att[0:band_rows], [att[band_rows + g * block : band_rows + (g + 1) * block] for g in range(GLOB)]


def _weights_kernel(init_ref, ptr_ref, soft_ref, win_ref, summ_ref, ask_ref, look_ref, own_ref, glob_ref, *, tick, heads_local, block):
    for h, ab, ags in _attention_weights(
        init_ref, ptr_ref, soft_ref, win_ref, summ_ref, ask_ref, look_ref, tick=tick, heads_local=heads_local, block=block
    ):
        own_ref[h] = ab[0:block]
        for g, ag in enumerate(ags):
            glob_ref[h, g * block : (g + 1) * block, :] = ag


def _partial_into(value_grad, w_ref, keep_ref, send_ref):
    contract = (((1,), (1,)), ((), ()))
    core = jnp.zeros((1, 1), jnp.int32) + lax.axis_index("head") % 2
    for g in range(w_ref.shape[0]):
        even, odd = [
            lax.dot_general(value_grad, w_ref[g, p], contract, preferred_element_type=jnp.float32).astype(keep_ref.dtype)
            for p in range(2)
        ]
        keep_ref[g] = jnp.where(core == 0, even, odd)
        send_ref[g] = jnp.where(core == 0, odd, even)


def _first_tick_kernel(
    init_ref, ptr_ref, soft_ref, win_ref, summ_ref, ask_ref, look_ref, ent_hbm, prior_ref, w_hbm,
    keep_ref, send_ref, carried_ref, glob_ref, grad_out_ref, w_ref, w_sem, grad_buf, grad_sem, *, heads_local, block
):
    width = grad_buf.shape[1]
    start = pl.multiple_of(lax.axis_index("head") * width, CHANNEL_WIDTH)
    grad_copy = pltpu.make_async_copy(ent_hbm.at[:, pl.ds(start, width)], grad_buf, grad_sem)
    grad_copy.start()
    w_copy = pltpu.make_async_copy(w_hbm, w_ref, w_sem)
    w_copy.start()
    weights = list(_attention_weights(
        init_ref, ptr_ref, soft_ref, win_ref, summ_ref, ask_ref, look_ref, tick=0, heads_local=heads_local, block=block
    ))
    grad_copy.wait()
    grad = grad_buf[...]
    grad_out_ref[...] = grad
    value_cols = []
    for h, ab, ags in weights:
        cols = slice(h * CHANNEL_WIDTH, (h + 1) * CHANNEL_WIDTH)
        gh = grad[:, cols]
        band = jnp.dot(ab, gh, preferred_element_type=jnp.float32)
        own = prior_ref[0:block, cols].astype(jnp.float32) + band[0:block]
        value_cols.append(own.astype(jnp.bfloat16))
        carried_ref[:, cols] = prior_ref[block : 2 * block, cols].astype(jnp.float32) + band[block : 2 * block]
        for g, ag in enumerate(ags):
            glob_ref[g * block : (g + 1) * block, cols] = jnp.dot(ag, gh, preferred_element_type=jnp.float32)
    value_grad = value_cols[0] if len(value_cols) == 1 else jnp.concatenate(value_cols, axis=1)
    w_copy.wait()
    _partial_into(value_grad, w_ref, keep_ref, send_ref)


def _last_tick_kernel(obj_ref, att_ref, carried_ref, w_hbm, *rest, heads_local, block, groups, phases):
    pieces = rest[:groups]
    keep_ref, send_ref, grad_out_ref, w_ref, w_sem = rest[groups:]
    w_copy = pltpu.make_async_copy(w_hbm, w_ref, w_sem)
    w_copy.start()
    band_rows = BAND * block
    arrived = pieces[0][...].astype(jnp.float32)
    for piece in pieces[1:]:
        arrived = arrived + piece[...].astype(jnp.float32)
    last = jnp.zeros((1, 1), jnp.int32) + (lax.axis_index("segment") == phases - 1).astype(jnp.int32)
    fresh = obj_ref[...]
    grad = jnp.where(last > 0, fresh, arrived.astype(jnp.bfloat16))
    grad_out_ref[...] = grad
    value_cols = []
    for h in range(heads_local):
        cols = slice(h * CHANNEL_WIDTH, (h + 1) * CHANNEL_WIDTH)
        gh = grad[:, cols]
        own = carried_ref[:, cols] + jnp.dot(att_ref[h], gh, preferred_element_type=jnp.float32)
        value_cols.append(own.astype(jnp.bfloat16))
    value_grad = value_cols[0] if len(value_cols) == 1 else jnp.concatenate(value_cols, axis=1)
    w_copy.wait()
    _partial_into(value_grad, w_ref, keep_ref, send_ref)


def _glob_kernel(att_ref, grad_ref, out_ref, *, heads_local):
    for h in range(heads_local):
        cols = slice(h * CHANNEL_WIDTH, (h + 1) * CHANNEL_WIDTH)
        out_ref[:, cols] = jnp.dot(att_ref[h], grad_ref[:, cols], preferred_element_type=jnp.float32)


def glob_contrib(att, grad):
    heads_local, rows, block = att.shape
    local_width = grad.shape[1]
    return pl.pallas_call(
        functools.partial(_glob_kernel, heads_local=heads_local),
        out_shape=jax.ShapeDtypeStruct((rows, local_width), jnp.float32),
        in_specs=[VMEM, VMEM],
        out_specs=VMEM,
        cost_estimate=pl.CostEstimate(flops=2 * rows * block * local_width, transcendentals=0, bytes_accessed=rows * local_width * 6),
    )(att, grad)


ANY = pl.BlockSpec(memory_space=pl.ANY)
VMEM = pl.BlockSpec(memory_space=pltpu.VMEM)
KERNEL_PARAMS = pltpu.CompilerParams()


def first_tick(initial_segment, digest_pointer, softness, window_inputs, summary_blocks, asker, lookup, prior, weights, entering):
    block = summary_blocks.shape[1]
    local_width = asker.shape[1]
    heads_local = local_width // CHANNEL_WIDTH
    groups = weights.shape[0]
    keys_total = (BAND + GLOB) * block
    feat = window_inputs.shape[1]
    flops = 2 * feat * local_width * (block + keys_total) + 14 * keys_total * block * local_width + 4 * block * local_width * groups * local_width
    ins = [initial_segment, digest_pointer, softness, window_inputs, summary_blocks, asker, lookup, entering, prior, weights]
    return pl.pallas_call(
        functools.partial(_first_tick_kernel, heads_local=heads_local, block=block),
        out_shape=(
            jax.ShapeDtypeStruct((groups, block, local_width), jnp.bfloat16),
            jax.ShapeDtypeStruct((groups, block, local_width), jnp.bfloat16),
            jax.ShapeDtypeStruct((block, local_width), jnp.float32),
            jax.ShapeDtypeStruct((GLOB * block, local_width), jnp.float32),
            jax.ShapeDtypeStruct((block, local_width), entering.dtype),
        ),
        in_specs=[VMEM] * 7 + [ANY, VMEM, ANY],
        out_specs=(VMEM, VMEM, VMEM, VMEM, VMEM),
        scratch_shapes=[
            pltpu.VMEM(weights.shape, weights.dtype),
            pltpu.SemaphoreType.DMA(()),
            pltpu.VMEM((block, local_width), entering.dtype),
            pltpu.SemaphoreType.DMA(()),
        ],
        compiler_params=KERNEL_PARAMS,
        cost_estimate=pl.CostEstimate(flops=flops, transcendentals=keys_total * block * heads_local, bytes_accessed=weights.size * 2 + 8 * block * local_width * 4),
    )(*ins)


def last_tick(att, carried, weights, objective, pieces, phases):
    heads_local, keys_total, block = att.shape
    local_width = carried.shape[1]
    groups = weights.shape[0]
    flops = 2 * keys_total * block * local_width + 4 * block * local_width * groups * local_width
    ins = [objective, att, carried, weights] + list(pieces)
    return pl.pallas_call(
        functools.partial(_last_tick_kernel, heads_local=heads_local, block=block, groups=len(pieces), phases=phases),
        out_shape=(
            jax.ShapeDtypeStruct((groups, block, local_width), jnp.bfloat16),
            jax.ShapeDtypeStruct((groups, block, local_width), jnp.bfloat16),
            jax.ShapeDtypeStruct((block, local_width), objective.dtype),
        ),
        in_specs=[VMEM, VMEM, VMEM, ANY] + [VMEM] * len(pieces),
        out_specs=(VMEM, VMEM, VMEM),
        scratch_shapes=[pltpu.VMEM(weights.shape, weights.dtype), pltpu.SemaphoreType.DMA(())],
        compiler_params=KERNEL_PARAMS,
        cost_estimate=pl.CostEstimate(flops=flops, transcendentals=0, bytes_accessed=weights.size * 2 + att.size * 2 + 8 * block * local_width * 4),
    )(*ins)


def attention_weights(tick, initial_segment, digest_pointer, softness, window_inputs, summary_blocks, asker, lookup):
    block = summary_blocks.shape[1]
    local_width = asker.shape[1]
    heads_local = local_width // CHANNEL_WIDTH
    keys_total = (BAND + GLOB) * block
    feat = window_inputs.shape[1]
    flops = 2 * feat * local_width * (block + keys_total) + 12 * keys_total * block * local_width
    ins = [initial_segment, digest_pointer, softness, window_inputs, summary_blocks, asker, lookup]
    return pl.pallas_call(
        functools.partial(_weights_kernel, tick=tick, heads_local=heads_local, block=block),
        out_shape=(
            jax.ShapeDtypeStruct((heads_local, block, block), jnp.bfloat16),
            jax.ShapeDtypeStruct((heads_local, GLOB * block, block), jnp.bfloat16),
        ),
        in_specs=[VMEM] * len(ins),
        out_specs=(VMEM, VMEM),
        compiler_params=KERNEL_PARAMS,
        cost_estimate=pl.CostEstimate(flops=flops, transcendentals=keys_total * block * heads_local, bytes_accessed=keys_total * local_width * 2 + 4 * feat * local_width * 2),
    )(*ins)


def local(
    entering_deriv,
    objective_derivs,
    content_projection,
    asker_projection,
    lookup_projection,
    softness,
    window_inputs,
    digest_inputs,
    digest_pointer,
    initial_segment,
    prior_content_derivs,
):
    period_label = lax.axis_index("segment")
    phases = lax.axis_size("segment")
    head_group = lax.axis_index("head")
    heads = lax.axis_size("head")
    groups = heads // 2
    block_rows = entering_deriv.shape[0]
    local_width = content_projection.shape[1]
    summary_blocks = digest_inputs.reshape(SUMMARY, block_rows, digest_inputs.shape[1])
    weights = content_projection.reshape(groups, 2, local_width, local_width)
    summary_ids = jnp.arange(SUMMARY, dtype=jnp.int32)

    def live_of(tick_index):
        position = initial_segment[0] - period_label - tick_index
        return jnp.minimum(GLOB, 1 + GLOB * position // SEQ_BLOCKS)

    def digest_of(tick_index, glob):
        selector = (digest_pointer[tick_index][:, None] == summary_ids[None, :]).astype(jnp.float32)
        return jnp.sum(
            selector[:, :, None, None] * glob.reshape(GLOB, block_rows, local_width)[:, None], axis=0
        ).reshape(SUMMARY * block_rows, local_width)

    init = initial_segment.reshape(1, 1)
    keep0, send0, carried, glob0, grad0 = first_tick(
        init, digest_pointer, softness, window_inputs, summary_blocks,
        asker_projection, lookup_projection, prior_content_derivs, weights, entering_deriv,
    )
    feats = (window_inputs, asker_projection, lookup_projection)
    pieces, got0 = shift_down_sum(keep0, send0, grad0.astype(jnp.float32))
    _, feats = lax.optimization_barrier((got0, feats))
    later_att = attention_weights(
        1, init, digest_pointer, softness, feats[0], summary_blocks, feats[1], feats[2]
    )
    digest_running = digest_of(0, glob0)
    att_own, att_glob = later_att
    keep1, send1, grad1 = last_tick(
        att_own, carried, weights,
        lax.dynamic_slice_in_dim(objective_derivs[0:block_rows], head_group * local_width, local_width, 1),
        pieces, phases
    )
    halves1 = core_pair_sum(keep1, send1)
    halves1, grad_held = lax.optimization_barrier((halves1, grad1))
    glob1 = glob_contrib(att_glob, grad_held)
    digest_running = digest_running + digest_of(1, glob1)
    summed = across_groups_sum(halves1)
    result = (grad1.astype(jnp.float32) + summed).astype(jnp.bfloat16)
    return (result, digest_running.astype(jnp.bfloat16))


def solution(mesh):
    in_specs = (
        P("segment", None),
        P(),
        P("segment", "head"),
        P("segment", "head"),
        P("segment", "head"),
        P("segment", "head"),
        P("segment", None),
        P(),
        P("segment", None),
        P(),
        P("segment", "head"),
    )
    out_specs = (P("segment", "head"), P("segment", "head"))
    return jax.shard_map(local, mesh=mesh, in_specs=in_specs, out_specs=out_specs, check_vma=False)
```

```python
import jax
import jax.numpy as jnp
from jax import lax
from jax.sharding import PartitionSpec as P
from jax.experimental import pallas as pl
from jax.experimental.pallas import tpu as pltpu
import functools

CHANNEL_WIDTH = 128
BAND = 4
GLOB = 2
SUMMARY = 2
SEQ_BLOCKS = 1024
TICKS = 2


EPS = 1e-06


def shifted(value, axis, steps):
    count = lax.axis_size(axis)
    first, last = (max(0, -steps), min(count, count - steps))
    return lax.ppermute(value, axis, [(source, source + steps) for source in range(first, last)])


def core_pair_sum(keep, send):
    heads = lax.axis_size("head")
    got = lax.ppermute(send, "head", [(h, h ^ 1) for h in range(heads)])
    return keep.astype(jnp.float32) + got.astype(jnp.float32)


def across_groups_sum(halves):
    head_group = lax.axis_index("head")
    heads = lax.axis_size("head")
    groups = heads // 2
    outer = head_group // 2
    total = lax.dynamic_index_in_dim(halves, outer, 0, keepdims=False)
    for step in range(1, groups):
        target = (outer + step) % groups
        piece = lax.dynamic_index_in_dim(halves, target, 0, keepdims=False).astype(jnp.bfloat16)
        pairs = [(h, (((h // 2) + step) % groups) * 2 + h % 2) for h in range(heads)]
        total = total + lax.ppermute(piece, "head", pairs).astype(jnp.float32)
    return total


def shift_down_sum(keep, send, entering):
    head_group = lax.axis_index("head")
    heads = lax.axis_size("head")
    segments = lax.axis_size("segment")
    groups = heads // 2
    outer = head_group // 2
    got = lax.ppermute(send, "head", [(h, h ^ 1) for h in range(heads)])
    total = []
    for step in range(groups):
        target = (outer + step) % groups
        piece = lax.dynamic_index_in_dim(keep, target, 0, keepdims=False).astype(jnp.float32) + lax.dynamic_index_in_dim(
            got, target, 0, keepdims=False
        ).astype(jnp.float32)
        if step == 0:
            piece = piece + entering
        pairs = []
        for s in range(1, segments):
            for h in range(heads):
                dest = (((h // 2) + step) % groups) * 2 + h % 2
                pairs.append((s * heads + h, (s - 1) * heads + dest))
        total.append(lax.ppermute(piece.astype(jnp.bfloat16), ("segment", "head"), pairs))
    return total, got
def row_norm(values):
    return values * lax.rsqrt(jnp.mean(values * values, axis=-1, keepdims=True) + EPS)


def _live_of(init_ref, tick):
    position = init_ref[...] - lax.axis_index("segment") - tick
    shift = SEQ_BLOCKS.bit_length() - 1
    return jnp.minimum(GLOB, 1 + lax.shift_right_arithmetic(GLOB * position, jnp.int32(shift)))


def _pick_columns(full_ref, width):
    head = jnp.zeros((1, 1), jnp.int32) + lax.axis_index("head")
    picked = full_ref[:, 0:width]
    for j in range(1, full_ref.shape[1] // width):
        picked = jnp.where(head == j, full_ref[:, j * width : (j + 1) * width], picked)
    return picked


def _attention_weights(init_ref, ptr_ref, soft_ref, win_ref, summ_ref, ask_ref, look_ref, *, tick, heads_local, block):
    band_rows = BAND * block
    live = _live_of(init_ref, tick)
    own = win_ref[tick * block : (tick + 1) * block, :]
    band = win_ref[tick * block : tick * block + band_rows, :]
    queries = jnp.dot(own, ask_ref[...], preferred_element_type=jnp.float32)
    band_keys = jnp.dot(band, look_ref[...], preferred_element_type=jnp.float32)
    summary_keys = [
        jnp.dot(summ_ref[m], look_ref[...], preferred_element_type=jnp.float32) for m in range(summ_ref.shape[0])
    ]
    glob_keys = []
    for g in range(GLOB):
        slot = ptr_ref[tick : tick + 1, g : g + 1]
        picked = summary_keys[0]
        for m in range(1, len(summary_keys)):
            picked = jnp.where(slot == m, summary_keys[m], picked)
        glob_keys.append(picked)
    keys_total = band_rows + GLOB * block
    key_ids = lax.broadcasted_iota(jnp.int32, (keys_total, block), 0)
    query_ids = lax.broadcasted_iota(jnp.int32, (keys_total, block), 1)
    slot_of = (key_ids - band_rows) // block
    admitted = ((key_ids < band_rows) & ((key_ids >= block) | (key_ids <= query_ids))) | (
        (key_ids >= band_rows) & (slot_of < live)
    )
    all_keys = jnp.concatenate([band_keys] + glob_keys, axis=0)
    contract = (((1,), (1,)), ((), ()))
    for h in range(heads_local):
        cols = slice(h * CHANNEL_WIDTH, (h + 1) * CHANNEL_WIDTH)
        scale = soft_ref[0:1, h : h + 1] * (1.0 / CHANNEL_WIDTH)
        qh = row_norm(queries[:, cols])
        kh = row_norm(all_keys[:, cols])
        sc = lax.dot_general(kh, qh, contract, precision=lax.Precision.HIGHEST, preferred_element_type=jnp.float32) * scale
        ex = jnp.where(admitted, jnp.exp(sc), 0.0)
        att = (ex / jnp.sum(ex, axis=0, keepdims=True)).astype(jnp.bfloat16)
        yield h, att[0:band_rows], [att[band_rows + g * block : band_rows + (g + 1) * block] for g in range(GLOB)]


def _weights_kernel(init_ref, ptr_ref, soft_ref, win_ref, summ_ref, ask_ref, look_ref, own_ref, glob_ref, *, tick, heads_local, block):
    for h, ab, ags in _attention_weights(
        init_ref, ptr_ref, soft_ref, win_ref, summ_ref, ask_ref, look_ref, tick=tick, heads_local=heads_local, block=block
    ):
        own_ref[h] = ab[0:block]
        for g, ag in enumerate(ags):
            glob_ref[h, g * block : (g + 1) * block, :] = ag


def _partial_into(value_grad, w_ref, keep_ref, send_ref, transposed=False):
    contract = (((1,), (0 if transposed else 1,)), ((), ()))
    core = jnp.zeros((1, 1), jnp.int32) + lax.axis_index("head") % 2
    for g in range(w_ref.shape[0]):
        even, odd = [
            lax.dot_general(value_grad, w_ref[g, p], contract, preferred_element_type=jnp.float32).astype(keep_ref.dtype)
            for p in range(2)
        ]
        keep_ref[g] = jnp.where(core == 0, even, odd)
        send_ref[g] = jnp.where(core == 0, odd, even)


def _first_tick_kernel(
    init_ref, ptr_ref, soft_ref, win_ref, summ_ref, ask_ref, look_ref, ent_hbm, prior_ref, w_hbm,
    keep_ref, send_ref, carried_ref, glob_ref, grad_out_ref, w_ref, w_sem, grad_buf, grad_sem, *, heads_local, block
):
    width = grad_buf.shape[1]
    start = pl.multiple_of(lax.axis_index("head") * width, CHANNEL_WIDTH)
    grad_copy = pltpu.make_async_copy(ent_hbm.at[:, pl.ds(start, width)], grad_buf, grad_sem)
    grad_copy.start()
    w_copy = pltpu.make_async_copy(w_hbm, w_ref, w_sem)
    w_copy.start()
    weights = list(_attention_weights(
        init_ref, ptr_ref, soft_ref, win_ref, summ_ref, ask_ref, look_ref, tick=0, heads_local=heads_local, block=block
    ))
    grad_copy.wait()
    grad = grad_buf[...]
    grad_out_ref[...] = grad
    value_cols = []
    for h, ab, ags in weights:
        cols = slice(h * CHANNEL_WIDTH, (h + 1) * CHANNEL_WIDTH)
        gh = grad[:, cols]
        band = jnp.dot(ab, gh, preferred_element_type=jnp.float32)
        own = prior_ref[0:block, cols].astype(jnp.float32) + band[0:block]
        value_cols.append(own.astype(jnp.bfloat16))
        carried_ref[:, cols] = prior_ref[block : 2 * block, cols].astype(jnp.float32) + band[block : 2 * block]
        for g, ag in enumerate(ags):
            glob_ref[g * block : (g + 1) * block, cols] = jnp.dot(ag, gh, preferred_element_type=jnp.float32)
    value_grad = value_cols[0] if len(value_cols) == 1 else jnp.concatenate(value_cols, axis=1)
    w_copy.wait()
    _partial_into(value_grad, w_ref, keep_ref, send_ref)


def _last_tick_kernel(obj_ref, att_ref, carried_ref, w_hbm, *rest, heads_local, block, groups, phases):
    pieces = rest[:groups]
    keep_ref, send_ref, grad_out_ref, w_ref, w_sem = rest[groups:]
    w_copy = pltpu.make_async_copy(w_hbm, w_ref, w_sem)
    w_copy.start()
    band_rows = BAND * block
    arrived = pieces[0][...].astype(jnp.float32)
    for piece in pieces[1:]:
        arrived = arrived + piece[...].astype(jnp.float32)
    last = jnp.zeros((1, 1), jnp.int32) + (lax.axis_index("segment") == phases - 1).astype(jnp.int32)
    fresh = obj_ref[...]
    grad = jnp.where(last > 0, fresh, arrived.astype(jnp.bfloat16))
    grad_out_ref[...] = grad
    value_cols = []
    for h in range(heads_local):
        cols = slice(h * CHANNEL_WIDTH, (h + 1) * CHANNEL_WIDTH)
        gh = grad[:, cols]
        own = carried_ref[:, cols] + jnp.dot(att_ref[h], gh, preferred_element_type=jnp.float32)
        value_cols.append(own.astype(jnp.bfloat16))
    value_grad = value_cols[0] if len(value_cols) == 1 else jnp.concatenate(value_cols, axis=1)
    w_copy.wait()
    _partial_into(value_grad, w_ref, keep_ref, send_ref, transposed=True)


def _glob_kernel(att_ref, grad_ref, out_ref, *, heads_local):
    for h in range(heads_local):
        cols = slice(h * CHANNEL_WIDTH, (h + 1) * CHANNEL_WIDTH)
        out_ref[:, cols] = jnp.dot(att_ref[h], grad_ref[:, cols], preferred_element_type=jnp.float32)


def glob_contrib(att, grad):
    heads_local, rows, block = att.shape
    local_width = grad.shape[1]
    return pl.pallas_call(
        functools.partial(_glob_kernel, heads_local=heads_local),
        out_shape=jax.ShapeDtypeStruct((rows, local_width), jnp.float32),
        in_specs=[VMEM, VMEM],
        out_specs=VMEM,
        cost_estimate=pl.CostEstimate(flops=2 * rows * block * local_width, transcendentals=0, bytes_accessed=rows * local_width * 6),
    )(att, grad)


ANY = pl.BlockSpec(memory_space=pl.ANY)
VMEM = pl.BlockSpec(memory_space=pltpu.VMEM)
KERNEL_PARAMS = pltpu.CompilerParams()


def first_tick(initial_segment, digest_pointer, softness, window_inputs, summary_blocks, asker, lookup, prior, weights, entering):
    block = summary_blocks.shape[1]
    local_width = asker.shape[1]
    heads_local = local_width // CHANNEL_WIDTH
    groups = weights.shape[0]
    keys_total = (BAND + GLOB) * block
    feat = window_inputs.shape[1]
    flops = 2 * feat * local_width * (block + keys_total) + 14 * keys_total * block * local_width + 4 * block * local_width * groups * local_width
    ins = [initial_segment, digest_pointer, softness, window_inputs, summary_blocks, asker, lookup, entering, prior, weights]
    return pl.pallas_call(
        functools.partial(_first_tick_kernel, heads_local=heads_local, block=block),
        out_shape=(
            jax.ShapeDtypeStruct((groups, block, local_width), jnp.bfloat16),
            jax.ShapeDtypeStruct((groups, block, local_width), jnp.bfloat16),
            jax.ShapeDtypeStruct((block, local_width), jnp.float32),
            jax.ShapeDtypeStruct((GLOB * block, local_width), jnp.float32),
            jax.ShapeDtypeStruct((block, local_width), entering.dtype),
        ),
        in_specs=[VMEM] * 7 + [ANY, VMEM, ANY],
        out_specs=(VMEM, VMEM, VMEM, VMEM, VMEM),
        scratch_shapes=[
            pltpu.VMEM(weights.shape, weights.dtype),
            pltpu.SemaphoreType.DMA(()),
            pltpu.VMEM((block, local_width), entering.dtype),
            pltpu.SemaphoreType.DMA(()),
        ],
        compiler_params=KERNEL_PARAMS,
        cost_estimate=pl.CostEstimate(flops=flops, transcendentals=keys_total * block * heads_local, bytes_accessed=weights.size * 2 + 8 * block * local_width * 4),
    )(*ins)


def last_tick(att, carried, weights, objective, pieces, phases):
    heads_local, keys_total, block = att.shape
    local_width = carried.shape[1]
    groups = weights.shape[0]
    flops = 2 * keys_total * block * local_width + 4 * block * local_width * groups * local_width
    ins = [objective, att, carried, weights] + list(pieces)
    return pl.pallas_call(
        functools.partial(_last_tick_kernel, heads_local=heads_local, block=block, groups=len(pieces), phases=phases),
        out_shape=(
            jax.ShapeDtypeStruct((groups, block, local_width), jnp.bfloat16),
            jax.ShapeDtypeStruct((groups, block, local_width), jnp.bfloat16),
            jax.ShapeDtypeStruct((block, local_width), objective.dtype),
        ),
        in_specs=[VMEM, VMEM, VMEM, ANY] + [VMEM] * len(pieces),
        out_specs=(VMEM, VMEM, VMEM),
        scratch_shapes=[pltpu.VMEM(weights.shape, weights.dtype), pltpu.SemaphoreType.DMA(())],
        compiler_params=KERNEL_PARAMS,
        cost_estimate=pl.CostEstimate(flops=flops, transcendentals=0, bytes_accessed=weights.size * 2 + att.size * 2 + 8 * block * local_width * 4),
    )(*ins)


def attention_weights(tick, initial_segment, digest_pointer, softness, window_inputs, summary_blocks, asker, lookup):
    block = summary_blocks.shape[1]
    local_width = asker.shape[1]
    heads_local = local_width // CHANNEL_WIDTH
    keys_total = (BAND + GLOB) * block
    feat = window_inputs.shape[1]
    flops = 2 * feat * local_width * (block + keys_total) + 12 * keys_total * block * local_width
    ins = [initial_segment, digest_pointer, softness, window_inputs, summary_blocks, asker, lookup]
    return pl.pallas_call(
        functools.partial(_weights_kernel, tick=tick, heads_local=heads_local, block=block),
        out_shape=(
            jax.ShapeDtypeStruct((heads_local, block, block), jnp.bfloat16),
            jax.ShapeDtypeStruct((heads_local, GLOB * block, block), jnp.bfloat16),
        ),
        in_specs=[VMEM] * len(ins),
        out_specs=(VMEM, VMEM),
        compiler_params=KERNEL_PARAMS,
        cost_estimate=pl.CostEstimate(flops=flops, transcendentals=keys_total * block * heads_local, bytes_accessed=keys_total * local_width * 2 + 4 * feat * local_width * 2),
    )(*ins)


def local(
    entering_deriv,
    objective_derivs,
    content_projection,
    asker_projection,
    lookup_projection,
    softness,
    window_inputs,
    digest_inputs,
    digest_pointer,
    initial_segment,
    prior_content_derivs,
):
    period_label = lax.axis_index("segment")
    phases = lax.axis_size("segment")
    head_group = lax.axis_index("head")
    heads = lax.axis_size("head")
    groups = heads // 2
    block_rows = entering_deriv.shape[0]
    local_width = content_projection.shape[1]
    summary_blocks = digest_inputs.reshape(SUMMARY, block_rows, digest_inputs.shape[1])
    weights = content_projection.reshape(groups, 2, local_width, local_width)
    summary_ids = jnp.arange(SUMMARY, dtype=jnp.int32)

    def live_of(tick_index):
        position = initial_segment[0] - period_label - tick_index
        return jnp.minimum(GLOB, 1 + GLOB * position // SEQ_BLOCKS)

    def digest_of(tick_index, glob):
        selector = (digest_pointer[tick_index][:, None] == summary_ids[None, :]).astype(jnp.float32)
        return jnp.sum(
            selector[:, :, None, None] * glob.reshape(GLOB, block_rows, local_width)[:, None], axis=0
        ).reshape(SUMMARY * block_rows, local_width)

    init = initial_segment.reshape(1, 1)
    keep0, send0, carried, glob0, grad0 = first_tick(
        init, digest_pointer, softness, window_inputs, summary_blocks,
        asker_projection, lookup_projection, prior_content_derivs, weights, entering_deriv,
    )
    feats = (window_inputs, asker_projection, lookup_projection)
    pieces, got0 = shift_down_sum(keep0, send0, grad0.astype(jnp.float32))
    _, feats = lax.optimization_barrier((got0, feats))
    later_att = attention_weights(
        1, init, digest_pointer, softness, feats[0], summary_blocks, feats[1], feats[2]
    )
    digest_running = digest_of(0, glob0)
    att_own, att_glob = later_att
    _, weights_held = lax.optimization_barrier((got0, weights))
    weights_t = jnp.swapaxes(weights_held, 2, 3)
    keep1, send1, grad1 = last_tick(
        att_own, carried, weights_t,
        lax.dynamic_slice_in_dim(objective_derivs[0:block_rows], head_group * local_width, local_width, 1),
        pieces, phases
    )
    halves1 = core_pair_sum(keep1, send1)
    halves1, grad_held = lax.optimization_barrier((halves1, grad1))
    glob1 = glob_contrib(att_glob, grad_held)
    digest_running = digest_running + digest_of(1, glob1)
    summed = across_groups_sum(halves1)
    result = (grad1.astype(jnp.float32) + summed).astype(jnp.bfloat16)
    return (result, digest_running.astype(jnp.bfloat16))


def solution(mesh):
    in_specs = (
        P("segment", None),
        P(),
        P("segment", "head"),
        P("segment", "head"),
        P("segment", "head"),
        P("segment", "head"),
        P("segment", None),
        P(),
        P("segment", None),
        P(),
        P("segment", "head"),
    )
    out_specs = (P("segment", "head"), P("segment", "head"))
    return jax.shard_map(local, mesh=mesh, in_specs=in_specs, out_specs=out_specs, check_vma=False)
```

```python
import jax
import jax.numpy as jnp
from jax import lax
from jax.sharding import PartitionSpec as P
from jax.experimental import pallas as pl
from jax.experimental.pallas import tpu as pltpu
import functools

CHANNEL_WIDTH = 128
BAND = 4
GLOB = 2
SUMMARY = 2
SEQ_BLOCKS = 1024
TICKS = 2


EPS = 1e-06


def shifted(value, axis, steps):
    count = lax.axis_size(axis)
    first, last = (max(0, -steps), min(count, count - steps))
    return lax.ppermute(value, axis, [(source, source + steps) for source in range(first, last)])


def core_pair_sum(keep, send):
    heads = lax.axis_size("head")
    got = lax.ppermute(send, "head", [(h, h ^ 1) for h in range(heads)])
    return keep.astype(jnp.float32) + got.astype(jnp.float32)


def across_groups_sum(halves):
    head_group = lax.axis_index("head")
    heads = lax.axis_size("head")
    groups = heads // 2
    outer = head_group // 2
    total = lax.dynamic_index_in_dim(halves, outer, 0, keepdims=False)
    for step in range(1, groups):
        target = (outer + step) % groups
        piece = lax.dynamic_index_in_dim(halves, target, 0, keepdims=False).astype(jnp.bfloat16)
        pairs = [(h, (((h // 2) + step) % groups) * 2 + h % 2) for h in range(heads)]
        total = total + lax.ppermute(piece, "head", pairs).astype(jnp.float32)
    return total


def shift_down_sum(keep, send, entering):
    head_group = lax.axis_index("head")
    heads = lax.axis_size("head")
    segments = lax.axis_size("segment")
    groups = heads // 2
    outer = head_group // 2
    got = lax.ppermute(send, "head", [(h, h ^ 1) for h in range(heads)])
    total = []
    for step in range(groups):
        target = (outer + step) % groups
        piece = lax.dynamic_index_in_dim(keep, target, 0, keepdims=False).astype(jnp.float32) + lax.dynamic_index_in_dim(
            got, target, 0, keepdims=False
        ).astype(jnp.float32)
        if step == 0:
            piece = piece + entering
        pairs = []
        for s in range(1, segments):
            for h in range(heads):
                dest = (((h // 2) + step) % groups) * 2 + h % 2
                pairs.append((s * heads + h, (s - 1) * heads + dest))
        total.append(lax.ppermute(piece.astype(jnp.bfloat16), ("segment", "head"), pairs))
    return total, got
def row_norm(values):
    return values * lax.rsqrt(jnp.mean(values * values, axis=-1, keepdims=True) + EPS)


def _live_of(init_ref, tick):
    position = init_ref[...] - lax.axis_index("segment") - tick
    shift = SEQ_BLOCKS.bit_length() - 1
    return jnp.minimum(GLOB, 1 + lax.shift_right_arithmetic(GLOB * position, jnp.int32(shift)))


def _pick_columns(full_ref, width):
    head = jnp.zeros((1, 1), jnp.int32) + lax.axis_index("head")
    picked = full_ref[:, 0:width]
    for j in range(1, full_ref.shape[1] // width):
        picked = jnp.where(head == j, full_ref[:, j * width : (j + 1) * width], picked)
    return picked


def _attention_weights(init_ref, ptr_ref, soft_ref, win_ref, summ_ref, ask_ref, look_ref, *, tick, heads_local, block):
    band_rows = BAND * block
    live = _live_of(init_ref, tick)
    own = win_ref[tick * block : (tick + 1) * block, :]
    band = win_ref[tick * block : tick * block + band_rows, :]
    queries = jnp.dot(own, ask_ref[...], preferred_element_type=jnp.float32)
    band_keys = jnp.dot(band, look_ref[...], preferred_element_type=jnp.float32)
    summary_keys = [
        jnp.dot(summ_ref[m], look_ref[...], preferred_element_type=jnp.float32) for m in range(summ_ref.shape[0])
    ]
    glob_keys = []
    for g in range(GLOB):
        slot = ptr_ref[tick : tick + 1, g : g + 1]
        picked = summary_keys[0]
        for m in range(1, len(summary_keys)):
            picked = jnp.where(slot == m, summary_keys[m], picked)
        glob_keys.append(picked)
    keys_total = band_rows + GLOB * block
    key_ids = lax.broadcasted_iota(jnp.int32, (keys_total, block), 0)
    query_ids = lax.broadcasted_iota(jnp.int32, (keys_total, block), 1)
    slot_of = (key_ids - band_rows) // block
    admitted = ((key_ids < band_rows) & ((key_ids >= block) | (key_ids <= query_ids))) | (
        (key_ids >= band_rows) & (slot_of < live)
    )
    all_keys = jnp.concatenate([band_keys] + glob_keys, axis=0)
    contract = (((1,), (1,)), ((), ()))
    for h in range(heads_local):
        cols = slice(h * CHANNEL_WIDTH, (h + 1) * CHANNEL_WIDTH)
        scale = soft_ref[0:1, h : h + 1] * (1.0 / CHANNEL_WIDTH)
        qh = row_norm(queries[:, cols])
        kh = row_norm(all_keys[:, cols])
        sc = lax.dot_general(kh, qh, contract, precision=lax.Precision.HIGHEST, preferred_element_type=jnp.float32) * scale
        ex = jnp.where(admitted, jnp.exp(sc), 0.0)
        att = (ex / jnp.sum(ex, axis=0, keepdims=True)).astype(jnp.bfloat16)
        yield h, att[0:band_rows], [att[band_rows + g * block : band_rows + (g + 1) * block] for g in range(GLOB)]


def _weights_kernel(init_ref, ptr_ref, soft_ref, win_ref, summ_ref, ask_ref, look_ref, own_ref, glob_ref, *, tick, heads_local, block):
    for h, ab, ags in _attention_weights(
        init_ref, ptr_ref, soft_ref, win_ref, summ_ref, ask_ref, look_ref, tick=tick, heads_local=heads_local, block=block
    ):
        own_ref[h] = ab[0:block]
        for g, ag in enumerate(ags):
            glob_ref[h, g * block : (g + 1) * block, :] = ag


def _partial_into(value_grad, w_ref, keep_ref, send_ref):
    contract = (((1,), (1,)), ((), ()))
    core = jnp.zeros((1, 1), jnp.int32) + lax.axis_index("head") % 2
    for g in range(w_ref.shape[0]):
        even, odd = [
            lax.dot_general(value_grad, w_ref[g, p], contract, preferred_element_type=jnp.float32).astype(keep_ref.dtype)
            for p in range(2)
        ]
        keep_ref[g] = jnp.where(core == 0, even, odd)
        send_ref[g] = jnp.where(core == 0, odd, even)


def _first_tick_kernel(
    init_ref, ptr_ref, soft_ref, win_ref, summ_ref, ask_ref, look_ref, ent_hbm, prior_ref, w_hbm,
    keep_ref, send_ref, carried_ref, glob_ref, grad_out_ref, w_ref, w_sem, grad_buf, grad_sem, *, heads_local, block
):
    width = grad_buf.shape[1]
    start = pl.multiple_of(lax.axis_index("head") * width, CHANNEL_WIDTH)
    grad_copy = pltpu.make_async_copy(ent_hbm.at[:, pl.ds(start, width)], grad_buf, grad_sem)
    grad_copy.start()
    w_copy = pltpu.make_async_copy(w_hbm, w_ref, w_sem)
    w_copy.start()
    weights = list(_attention_weights(
        init_ref, ptr_ref, soft_ref, win_ref, summ_ref, ask_ref, look_ref, tick=0, heads_local=heads_local, block=block
    ))
    grad_copy.wait()
    grad = grad_buf[...]
    grad_out_ref[...] = grad
    value_cols = []
    for h, ab, ags in weights:
        cols = slice(h * CHANNEL_WIDTH, (h + 1) * CHANNEL_WIDTH)
        gh = grad[:, cols]
        band = jnp.dot(ab, gh, preferred_element_type=jnp.float32)
        own = prior_ref[0:block, cols].astype(jnp.float32) + band[0:block]
        value_cols.append(own.astype(jnp.bfloat16))
        carried_ref[:, cols] = prior_ref[block : 2 * block, cols].astype(jnp.float32) + band[block : 2 * block]
        for g, ag in enumerate(ags):
            glob_ref[h, g * block : (g + 1) * block, :] = ag
    value_grad = value_cols[0] if len(value_cols) == 1 else jnp.concatenate(value_cols, axis=1)
    w_copy.wait()
    _partial_into(value_grad, w_ref, keep_ref, send_ref)


def _last_tick_kernel(obj_ref, att_ref, carried_ref, w_hbm, *rest, heads_local, block, groups, phases):
    pieces = rest[:groups]
    keep_ref, send_ref, grad_out_ref, w_ref, w_sem = rest[groups:]
    w_copy = pltpu.make_async_copy(w_hbm, w_ref, w_sem)
    w_copy.start()
    band_rows = BAND * block
    arrived = pieces[0][...].astype(jnp.float32)
    for piece in pieces[1:]:
        arrived = arrived + piece[...].astype(jnp.float32)
    last = jnp.zeros((1, 1), jnp.int32) + (lax.axis_index("segment") == phases - 1).astype(jnp.int32)
    fresh = obj_ref[...]
    grad = jnp.where(last > 0, fresh, arrived.astype(jnp.bfloat16))
    grad_out_ref[...] = grad
    value_cols = []
    for h in range(heads_local):
        cols = slice(h * CHANNEL_WIDTH, (h + 1) * CHANNEL_WIDTH)
        gh = grad[:, cols]
        own = carried_ref[:, cols] + jnp.dot(att_ref[h], gh, preferred_element_type=jnp.float32)
        value_cols.append(own.astype(jnp.bfloat16))
    value_grad = value_cols[0] if len(value_cols) == 1 else jnp.concatenate(value_cols, axis=1)
    w_copy.wait()
    _partial_into(value_grad, w_ref, keep_ref, send_ref)


def _glob_kernel(att_ref, grad_ref, out_ref, *, heads_local):
    for h in range(heads_local):
        cols = slice(h * CHANNEL_WIDTH, (h + 1) * CHANNEL_WIDTH)
        out_ref[:, cols] = jnp.dot(att_ref[h], grad_ref[:, cols], preferred_element_type=jnp.float32)


def glob_contrib(att, grad):
    heads_local, rows, block = att.shape
    local_width = grad.shape[1]
    return pl.pallas_call(
        functools.partial(_glob_kernel, heads_local=heads_local),
        out_shape=jax.ShapeDtypeStruct((rows, local_width), jnp.float32),
        in_specs=[VMEM, VMEM],
        out_specs=VMEM,
        cost_estimate=pl.CostEstimate(flops=2 * rows * block * local_width, transcendentals=0, bytes_accessed=rows * local_width * 6),
    )(att, grad)


ANY = pl.BlockSpec(memory_space=pl.ANY)
VMEM = pl.BlockSpec(memory_space=pltpu.VMEM)
KERNEL_PARAMS = pltpu.CompilerParams()


def first_tick(initial_segment, digest_pointer, softness, window_inputs, summary_blocks, asker, lookup, prior, weights, entering):
    block = summary_blocks.shape[1]
    local_width = asker.shape[1]
    heads_local = local_width // CHANNEL_WIDTH
    groups = weights.shape[0]
    keys_total = (BAND + GLOB) * block
    feat = window_inputs.shape[1]
    flops = 2 * feat * local_width * (block + keys_total) + 14 * keys_total * block * local_width + 4 * block * local_width * groups * local_width
    ins = [initial_segment, digest_pointer, softness, window_inputs, summary_blocks, asker, lookup, entering, prior, weights]
    return pl.pallas_call(
        functools.partial(_first_tick_kernel, heads_local=heads_local, block=block),
        out_shape=(
            jax.ShapeDtypeStruct((groups, block, local_width), jnp.bfloat16),
            jax.ShapeDtypeStruct((groups, block, local_width), jnp.bfloat16),
            jax.ShapeDtypeStruct((block, local_width), jnp.float32),
            jax.ShapeDtypeStruct((heads_local, GLOB * block, block), jnp.bfloat16),
            jax.ShapeDtypeStruct((block, local_width), entering.dtype),
        ),
        in_specs=[VMEM] * 7 + [ANY, VMEM, ANY],
        out_specs=(VMEM, VMEM, VMEM, VMEM, VMEM),
        scratch_shapes=[
            pltpu.VMEM(weights.shape, weights.dtype),
            pltpu.SemaphoreType.DMA(()),
            pltpu.VMEM((block, local_width), entering.dtype),
            pltpu.SemaphoreType.DMA(()),
        ],
        compiler_params=KERNEL_PARAMS,
        cost_estimate=pl.CostEstimate(flops=flops, transcendentals=keys_total * block * heads_local, bytes_accessed=weights.size * 2 + 8 * block * local_width * 4),
    )(*ins)


def last_tick(att, carried, weights, objective, pieces, phases):
    heads_local, keys_total, block = att.shape
    local_width = carried.shape[1]
    groups = weights.shape[0]
    flops = 2 * keys_total * block * local_width + 4 * block * local_width * groups * local_width
    ins = [objective, att, carried, weights] + list(pieces)
    return pl.pallas_call(
        functools.partial(_last_tick_kernel, heads_local=heads_local, block=block, groups=len(pieces), phases=phases),
        out_shape=(
            jax.ShapeDtypeStruct((groups, block, local_width), jnp.bfloat16),
            jax.ShapeDtypeStruct((groups, block, local_width), jnp.bfloat16),
            jax.ShapeDtypeStruct((block, local_width), objective.dtype),
        ),
        in_specs=[VMEM, VMEM, VMEM, ANY] + [VMEM] * len(pieces),
        out_specs=(VMEM, VMEM, VMEM),
        scratch_shapes=[pltpu.VMEM(weights.shape, weights.dtype), pltpu.SemaphoreType.DMA(())],
        compiler_params=KERNEL_PARAMS,
        cost_estimate=pl.CostEstimate(flops=flops, transcendentals=0, bytes_accessed=weights.size * 2 + att.size * 2 + 8 * block * local_width * 4),
    )(*ins)


def attention_weights(tick, initial_segment, digest_pointer, softness, window_inputs, summary_blocks, asker, lookup):
    block = summary_blocks.shape[1]
    local_width = asker.shape[1]
    heads_local = local_width // CHANNEL_WIDTH
    keys_total = (BAND + GLOB) * block
    feat = window_inputs.shape[1]
    flops = 2 * feat * local_width * (block + keys_total) + 12 * keys_total * block * local_width
    ins = [initial_segment, digest_pointer, softness, window_inputs, summary_blocks, asker, lookup]
    return pl.pallas_call(
        functools.partial(_weights_kernel, tick=tick, heads_local=heads_local, block=block),
        out_shape=(
            jax.ShapeDtypeStruct((heads_local, block, block), jnp.bfloat16),
            jax.ShapeDtypeStruct((heads_local, GLOB * block, block), jnp.bfloat16),
        ),
        in_specs=[VMEM] * len(ins),
        out_specs=(VMEM, VMEM),
        compiler_params=KERNEL_PARAMS,
        cost_estimate=pl.CostEstimate(flops=flops, transcendentals=keys_total * block * heads_local, bytes_accessed=keys_total * local_width * 2 + 4 * feat * local_width * 2),
    )(*ins)


def local(
    entering_deriv,
    objective_derivs,
    content_projection,
    asker_projection,
    lookup_projection,
    softness,
    window_inputs,
    digest_inputs,
    digest_pointer,
    initial_segment,
    prior_content_derivs,
):
    period_label = lax.axis_index("segment")
    phases = lax.axis_size("segment")
    head_group = lax.axis_index("head")
    heads = lax.axis_size("head")
    groups = heads // 2
    block_rows = entering_deriv.shape[0]
    local_width = content_projection.shape[1]
    summary_blocks = digest_inputs.reshape(SUMMARY, block_rows, digest_inputs.shape[1])
    weights = content_projection.reshape(groups, 2, local_width, local_width)
    summary_ids = jnp.arange(SUMMARY, dtype=jnp.int32)

    def live_of(tick_index):
        position = initial_segment[0] - period_label - tick_index
        return jnp.minimum(GLOB, 1 + GLOB * position // SEQ_BLOCKS)

    def digest_of(tick_index, glob):
        selector = (digest_pointer[tick_index][:, None] == summary_ids[None, :]).astype(jnp.float32)
        return jnp.sum(
            selector[:, :, None, None] * glob.reshape(GLOB, block_rows, local_width)[:, None], axis=0
        ).reshape(SUMMARY * block_rows, local_width)

    init = initial_segment.reshape(1, 1)
    keep0, send0, carried, glob0, grad0 = first_tick(
        init, digest_pointer, softness, window_inputs, summary_blocks,
        asker_projection, lookup_projection, prior_content_derivs, weights, entering_deriv,
    )
    feats = (window_inputs, asker_projection, lookup_projection)
    pieces, got0 = shift_down_sum(keep0, send0, grad0.astype(jnp.float32))
    _, feats = lax.optimization_barrier((got0, feats))
    later_att = attention_weights(
        1, init, digest_pointer, softness, feats[0], summary_blocks, feats[1], feats[2]
    )
    _, att_glob0, grad_held0 = lax.optimization_barrier((got0, glob0, grad0))
    glob0_contrib, carried = lax.optimization_barrier((glob_contrib(att_glob0, grad_held0), carried))
    digest_running = digest_of(0, glob0_contrib)
    att_own, att_glob = later_att
    keep1, send1, grad1 = last_tick(
        att_own, carried, weights,
        lax.dynamic_slice_in_dim(objective_derivs[0:block_rows], head_group * local_width, local_width, 1),
        pieces, phases
    )
    halves1 = core_pair_sum(keep1, send1)
    halves1, grad_held = lax.optimization_barrier((halves1, grad1))
    glob1 = glob_contrib(att_glob, grad_held)
    digest_running = digest_running + digest_of(1, glob1)
    summed = across_groups_sum(halves1)
    result = (grad1.astype(jnp.float32) + summed).astype(jnp.bfloat16)
    return (result, digest_running.astype(jnp.bfloat16))


def solution(mesh):
    in_specs = (
        P("segment", None),
        P(),
        P("segment", "head"),
        P("segment", "head"),
        P("segment", "head"),
        P("segment", "head"),
        P("segment", None),
        P(),
        P("segment", None),
        P(),
        P("segment", "head"),
    )
    out_specs = (P("segment", "head"), P("segment", "head"))
    return jax.shard_map(local, mesh=mesh, in_specs=in_specs, out_specs=out_specs, check_vma=False)
```

```python
import jax
import jax.numpy as jnp
from jax import lax
from jax.sharding import PartitionSpec as P
from jax.experimental import pallas as pl
from jax.experimental.pallas import tpu as pltpu
import functools

CHANNEL_WIDTH = 128
BAND = 4
GLOB = 2
SUMMARY = 2
SEQ_BLOCKS = 1024
TICKS = 2


EPS = 1e-06


def shifted(value, axis, steps):
    count = lax.axis_size(axis)
    first, last = (max(0, -steps), min(count, count - steps))
    return lax.ppermute(value, axis, [(source, source + steps) for source in range(first, last)])


def core_pair_sum(keep, send):
    heads = lax.axis_size("head")
    got = lax.ppermute(send, "head", [(h, h ^ 1) for h in range(heads)])
    return keep.astype(jnp.float32) + got.astype(jnp.float32)


def across_groups_sum(halves):
    head_group = lax.axis_index("head")
    heads = lax.axis_size("head")
    groups = heads // 2
    outer = head_group // 2
    total = lax.dynamic_index_in_dim(halves, outer, 0, keepdims=False)
    for step in range(1, groups):
        target = (outer + step) % groups
        piece = lax.dynamic_index_in_dim(halves, target, 0, keepdims=False).astype(jnp.bfloat16)
        pairs = [(h, (((h // 2) + step) % groups) * 2 + h % 2) for h in range(heads)]
        total = total + lax.ppermute(piece, "head", pairs).astype(jnp.float32)
    return total


def shift_down_sum(keep, send, entering):
    head_group = lax.axis_index("head")
    heads = lax.axis_size("head")
    segments = lax.axis_size("segment")
    groups = heads // 2
    outer = head_group // 2
    got = lax.ppermute(send, "head", [(h, h ^ 1) for h in range(heads)])
    total = []
    for step in range(groups):
        target = (outer + step) % groups
        piece = lax.dynamic_index_in_dim(keep, target, 0, keepdims=False).astype(jnp.float32) + lax.dynamic_index_in_dim(
            got, target, 0, keepdims=False
        ).astype(jnp.float32)
        if step == 0:
            piece = piece + entering
        pairs = []
        for s in range(1, segments):
            for h in range(heads):
                dest = (((h // 2) + step) % groups) * 2 + h % 2
                pairs.append((s * heads + h, (s - 1) * heads + dest))
        total.append(lax.ppermute(piece.astype(jnp.bfloat16), ("segment", "head"), pairs))
    return total, got
def row_norm(values):
    return values * lax.rsqrt(jnp.mean(values * values, axis=-1, keepdims=True) + EPS)


def _live_of(init_ref, tick):
    position = init_ref[...] - lax.axis_index("segment") - tick
    shift = SEQ_BLOCKS.bit_length() - 1
    return jnp.minimum(GLOB, 1 + lax.shift_right_arithmetic(GLOB * position, jnp.int32(shift)))


def _pick_columns(full_ref, width):
    head = jnp.zeros((1, 1), jnp.int32) + lax.axis_index("head")
    picked = full_ref[:, 0:width]
    for j in range(1, full_ref.shape[1] // width):
        picked = jnp.where(head == j, full_ref[:, j * width : (j + 1) * width], picked)
    return picked


def _attention_weights(init_ref, ptr_ref, soft_ref, win_ref, summ_ref, ask_ref, look_ref, *, tick, heads_local, block):
    band_rows = BAND * block
    live = _live_of(init_ref, tick)
    own = win_ref[tick * block : (tick + 1) * block, :]
    band = win_ref[tick * block : tick * block + band_rows, :]
    queries = jnp.dot(own, ask_ref[...], preferred_element_type=jnp.float32)
    band_keys = jnp.dot(band, look_ref[...], preferred_element_type=jnp.float32)
    summary_keys = [
        jnp.dot(summ_ref[m], look_ref[...], preferred_element_type=jnp.float32) for m in range(summ_ref.shape[0])
    ]
    glob_keys = []
    for g in range(GLOB):
        slot = ptr_ref[tick : tick + 1, g : g + 1]
        picked = summary_keys[0]
        for m in range(1, len(summary_keys)):
            picked = jnp.where(slot == m, summary_keys[m], picked)
        glob_keys.append(picked)
    keys_total = band_rows + GLOB * block
    key_ids = lax.broadcasted_iota(jnp.int32, (keys_total, block), 0)
    query_ids = lax.broadcasted_iota(jnp.int32, (keys_total, block), 1)
    slot_of = (key_ids - band_rows) // block
    admitted = ((key_ids < band_rows) & ((key_ids >= block) | (key_ids <= query_ids))) | (
        (key_ids >= band_rows) & (slot_of < live)
    )
    all_keys = jnp.concatenate([band_keys] + glob_keys, axis=0)
    contract = (((1,), (1,)), ((), ()))
    for h in range(heads_local):
        cols = slice(h * CHANNEL_WIDTH, (h + 1) * CHANNEL_WIDTH)
        scale = soft_ref[0:1, h : h + 1] * (1.0 / CHANNEL_WIDTH)
        qh = row_norm(queries[:, cols])
        kh = row_norm(all_keys[:, cols])
        sc = lax.dot_general(kh, qh, contract, precision=lax.Precision.HIGHEST, preferred_element_type=jnp.float32) * scale
        ex = jnp.where(admitted, jnp.exp(sc), 0.0)
        att = (ex / jnp.sum(ex, axis=0, keepdims=True)).astype(jnp.bfloat16)
        yield h, att[0:band_rows], [att[band_rows + g * block : band_rows + (g + 1) * block] for g in range(GLOB)]


def _weights_kernel(init_ref, ptr_ref, soft_ref, win_ref, summ_ref, ask_ref, look_ref, own_ref, glob_ref, *, tick, heads_local, block):
    for h, ab, ags in _attention_weights(
        init_ref, ptr_ref, soft_ref, win_ref, summ_ref, ask_ref, look_ref, tick=tick, heads_local=heads_local, block=block
    ):
        own_ref[h] = ab[0:block]
        for g, ag in enumerate(ags):
            glob_ref[h, g * block : (g + 1) * block, :] = ag


def _partial_into(value_grad, w_ref, keep_ref, send_ref):
    contract = (((1,), (1,)), ((), ()))
    core = jnp.zeros((1, 1), jnp.int32) + lax.axis_index("head") % 2
    for g in range(w_ref.shape[0]):
        even, odd = [
            lax.dot_general(value_grad, w_ref[g, p], contract, preferred_element_type=jnp.float32).astype(keep_ref.dtype)
            for p in range(2)
        ]
        keep_ref[g] = jnp.where(core == 0, even, odd)
        send_ref[g] = jnp.where(core == 0, odd, even)


def _first_tick_kernel(
    init_ref, ptr_ref, soft_ref, win_ref, summ_ref, ask_ref, look_ref, ent_hbm, prior_ref, w_hbm,
    keep_ref, send_ref, carried_ref, glob_ref, grad_out_ref, w_ref, w_sem, grad_buf, grad_sem, *, heads_local, block
):
    width = grad_buf.shape[1]
    start = pl.multiple_of(lax.axis_index("head") * width, CHANNEL_WIDTH)
    grad_copy = pltpu.make_async_copy(ent_hbm.at[:, pl.ds(start, width)], grad_buf, grad_sem)
    grad_copy.start()
    w_copy = pltpu.make_async_copy(w_hbm, w_ref, w_sem)
    w_copy.start()
    weights = list(_attention_weights(
        init_ref, ptr_ref, soft_ref, win_ref, summ_ref, ask_ref, look_ref, tick=0, heads_local=heads_local, block=block
    ))
    grad_copy.wait()
    grad = grad_buf[...]
    grad_out_ref[...] = grad
    value_cols = []
    for h, ab, ags in weights:
        cols = slice(h * CHANNEL_WIDTH, (h + 1) * CHANNEL_WIDTH)
        gh = grad[:, cols]
        band = jnp.dot(ab[0 : 2 * block], gh, preferred_element_type=jnp.float32)
        own = prior_ref[0:block, cols].astype(jnp.float32) + band[0:block]
        value_cols.append(own.astype(jnp.bfloat16))
        carried_ref[:, cols] = prior_ref[block : 2 * block, cols].astype(jnp.float32) + band[block : 2 * block]
        for g, ag in enumerate(ags):
            glob_ref[g * block : (g + 1) * block, cols] = jnp.dot(ag, gh, preferred_element_type=jnp.float32)
    value_grad = value_cols[0] if len(value_cols) == 1 else jnp.concatenate(value_cols, axis=1)
    w_copy.wait()
    _partial_into(value_grad, w_ref, keep_ref, send_ref)


def _last_tick_kernel(obj_ref, att_ref, carried_ref, w_hbm, *rest, heads_local, block, groups, phases):
    pieces = rest[:groups]
    keep_ref, send_ref, grad_out_ref, w_ref, w_sem = rest[groups:]
    w_copy = pltpu.make_async_copy(w_hbm, w_ref, w_sem)
    w_copy.start()
    band_rows = BAND * block
    arrived = pieces[0][...].astype(jnp.float32)
    for piece in pieces[1:]:
        arrived = arrived + piece[...].astype(jnp.float32)
    last = jnp.zeros((1, 1), jnp.int32) + (lax.axis_index("segment") == phases - 1).astype(jnp.int32)
    fresh = obj_ref[...]
    grad = jnp.where(last > 0, fresh, arrived.astype(jnp.bfloat16))
    grad_out_ref[...] = grad
    value_cols = []
    for h in range(heads_local):
        cols = slice(h * CHANNEL_WIDTH, (h + 1) * CHANNEL_WIDTH)
        gh = grad[:, cols]
        own = carried_ref[:, cols] + jnp.dot(att_ref[h], gh, preferred_element_type=jnp.float32)
        value_cols.append(own.astype(jnp.bfloat16))
    value_grad = value_cols[0] if len(value_cols) == 1 else jnp.concatenate(value_cols, axis=1)
    w_copy.wait()
    _partial_into(value_grad, w_ref, keep_ref, send_ref)


def _glob_kernel(att_ref, grad_ref, out_ref, *, heads_local):
    for h in range(heads_local):
        cols = slice(h * CHANNEL_WIDTH, (h + 1) * CHANNEL_WIDTH)
        out_ref[:, cols] = jnp.dot(att_ref[h], grad_ref[:, cols], preferred_element_type=jnp.float32)


def glob_contrib(att, grad):
    heads_local, rows, block = att.shape
    local_width = grad.shape[1]
    return pl.pallas_call(
        functools.partial(_glob_kernel, heads_local=heads_local),
        out_shape=jax.ShapeDtypeStruct((rows, local_width), jnp.float32),
        in_specs=[VMEM, VMEM],
        out_specs=VMEM,
        cost_estimate=pl.CostEstimate(flops=2 * rows * block * local_width, transcendentals=0, bytes_accessed=rows * local_width * 6),
    )(att, grad)


ANY = pl.BlockSpec(memory_space=pl.ANY)
VMEM = pl.BlockSpec(memory_space=pltpu.VMEM)
KERNEL_PARAMS = pltpu.CompilerParams()


def first_tick(initial_segment, digest_pointer, softness, window_inputs, summary_blocks, asker, lookup, prior, weights, entering):
    block = summary_blocks.shape[1]
    local_width = asker.shape[1]
    heads_local = local_width // CHANNEL_WIDTH
    groups = weights.shape[0]
    keys_total = (BAND + GLOB) * block
    feat = window_inputs.shape[1]
    flops = 2 * feat * local_width * (block + keys_total) + 14 * keys_total * block * local_width + 4 * block * local_width * groups * local_width
    ins = [initial_segment, digest_pointer, softness, window_inputs, summary_blocks, asker, lookup, entering, prior, weights]
    return pl.pallas_call(
        functools.partial(_first_tick_kernel, heads_local=heads_local, block=block),
        out_shape=(
            jax.ShapeDtypeStruct((groups, block, local_width), jnp.bfloat16),
            jax.ShapeDtypeStruct((groups, block, local_width), jnp.bfloat16),
            jax.ShapeDtypeStruct((block, local_width), jnp.float32),
            jax.ShapeDtypeStruct((GLOB * block, local_width), jnp.float32),
            jax.ShapeDtypeStruct((block, local_width), entering.dtype),
        ),
        in_specs=[VMEM] * 7 + [ANY, VMEM, ANY],
        out_specs=(VMEM, VMEM, VMEM, VMEM, VMEM),
        scratch_shapes=[
            pltpu.VMEM(weights.shape, weights.dtype),
            pltpu.SemaphoreType.DMA(()),
            pltpu.VMEM((block, local_width), entering.dtype),
            pltpu.SemaphoreType.DMA(()),
        ],
        compiler_params=KERNEL_PARAMS,
        cost_estimate=pl.CostEstimate(flops=flops, transcendentals=keys_total * block * heads_local, bytes_accessed=weights.size * 2 + 8 * block * local_width * 4),
    )(*ins)


def last_tick(att, carried, weights, objective, pieces, phases):
    heads_local, keys_total, block = att.shape
    local_width = carried.shape[1]
    groups = weights.shape[0]
    flops = 2 * keys_total * block * local_width + 4 * block * local_width * groups * local_width
    ins = [objective, att, carried, weights] + list(pieces)
    return pl.pallas_call(
        functools.partial(_last_tick_kernel, heads_local=heads_local, block=block, groups=len(pieces), phases=phases),
        out_shape=(
            jax.ShapeDtypeStruct((groups, block, local_width), jnp.bfloat16),
            jax.ShapeDtypeStruct((groups, block, local_width), jnp.bfloat16),
            jax.ShapeDtypeStruct((block, local_width), objective.dtype),
        ),
        in_specs=[VMEM, VMEM, VMEM, ANY] + [VMEM] * len(pieces),
        out_specs=(VMEM, VMEM, VMEM),
        scratch_shapes=[pltpu.VMEM(weights.shape, weights.dtype), pltpu.SemaphoreType.DMA(())],
        compiler_params=KERNEL_PARAMS,
        cost_estimate=pl.CostEstimate(flops=flops, transcendentals=0, bytes_accessed=weights.size * 2 + att.size * 2 + 8 * block * local_width * 4),
    )(*ins)


def attention_weights(tick, initial_segment, digest_pointer, softness, window_inputs, summary_blocks, asker, lookup):
    block = summary_blocks.shape[1]
    local_width = asker.shape[1]
    heads_local = local_width // CHANNEL_WIDTH
    keys_total = (BAND + GLOB) * block
    feat = window_inputs.shape[1]
    flops = 2 * feat * local_width * (block + keys_total) + 12 * keys_total * block * local_width
    ins = [initial_segment, digest_pointer, softness, window_inputs, summary_blocks, asker, lookup]
    return pl.pallas_call(
        functools.partial(_weights_kernel, tick=tick, heads_local=heads_local, block=block),
        out_shape=(
            jax.ShapeDtypeStruct((heads_local, block, block), jnp.bfloat16),
            jax.ShapeDtypeStruct((heads_local, GLOB * block, block), jnp.bfloat16),
        ),
        in_specs=[VMEM] * len(ins),
        out_specs=(VMEM, VMEM),
        compiler_params=KERNEL_PARAMS,
        cost_estimate=pl.CostEstimate(flops=flops, transcendentals=keys_total * block * heads_local, bytes_accessed=keys_total * local_width * 2 + 4 * feat * local_width * 2),
    )(*ins)


def local(
    entering_deriv,
    objective_derivs,
    content_projection,
    asker_projection,
    lookup_projection,
    softness,
    window_inputs,
    digest_inputs,
    digest_pointer,
    initial_segment,
    prior_content_derivs,
):
    period_label = lax.axis_index("segment")
    phases = lax.axis_size("segment")
    head_group = lax.axis_index("head")
    heads = lax.axis_size("head")
    groups = heads // 2
    block_rows = entering_deriv.shape[0]
    local_width = content_projection.shape[1]
    summary_blocks = digest_inputs.reshape(SUMMARY, block_rows, digest_inputs.shape[1])
    weights = content_projection.reshape(groups, 2, local_width, local_width)
    summary_ids = jnp.arange(SUMMARY, dtype=jnp.int32)

    def live_of(tick_index):
        position = initial_segment[0] - period_label - tick_index
        return jnp.minimum(GLOB, 1 + GLOB * position // SEQ_BLOCKS)

    def digest_of(tick_index, glob):
        selector = (digest_pointer[tick_index][:, None] == summary_ids[None, :]).astype(jnp.float32)
        return jnp.sum(
            selector[:, :, None, None] * glob.reshape(GLOB, block_rows, local_width)[:, None], axis=0
        ).reshape(SUMMARY * block_rows, local_width)

    init = initial_segment.reshape(1, 1)
    keep0, send0, carried, glob0, grad0 = first_tick(
        init, digest_pointer, softness, window_inputs, summary_blocks,
        asker_projection, lookup_projection, prior_content_derivs, weights, entering_deriv,
    )
    feats = (window_inputs, asker_projection, lookup_projection)
    pieces, got0 = shift_down_sum(keep0, send0, grad0.astype(jnp.float32))
    _, feats = lax.optimization_barrier((got0, feats))
    later_att = attention_weights(
        1, init, digest_pointer, softness, feats[0], summary_blocks, feats[1], feats[2]
    )
    digest_running = digest_of(0, glob0)
    att_own, att_glob = later_att
    keep1, send1, grad1 = last_tick(
        att_own, carried, weights,
        lax.dynamic_slice_in_dim(objective_derivs[0:block_rows], head_group * local_width, local_width, 1),
        pieces, phases
    )
    halves1 = core_pair_sum(keep1, send1)
    halves1, grad_held = lax.optimization_barrier((halves1, grad1))
    glob1 = glob_contrib(att_glob, grad_held)
    digest_running = digest_running + digest_of(1, glob1)
    summed = across_groups_sum(halves1)
    result = (grad1.astype(jnp.float32) + summed).astype(jnp.bfloat16)
    return (result, digest_running.astype(jnp.bfloat16))


def solution(mesh):
    in_specs = (
        P("segment", None),
        P(),
        P("segment", "head"),
        P("segment", "head"),
        P("segment", "head"),
        P("segment", "head"),
        P("segment", None),
        P(),
        P("segment", None),
        P(),
        P("segment", "head"),
    )
    out_specs = (P("segment", "head"), P("segment", "head"))
    return jax.shard_map(local, mesh=mesh, in_specs=in_specs, out_specs=out_specs, check_vma=False)
```

```python
import jax
import jax.numpy as jnp
from jax import lax
from jax.sharding import PartitionSpec as P
from jax.experimental import pallas as pl
from jax.experimental.pallas import tpu as pltpu
import functools

CHANNEL_WIDTH = 128
BAND = 4
GLOB = 2
SUMMARY = 2
SEQ_BLOCKS = 1024
TICKS = 2


EPS = 1e-06


def shifted(value, axis, steps):
    count = lax.axis_size(axis)
    first, last = (max(0, -steps), min(count, count - steps))
    return lax.ppermute(value, axis, [(source, source + steps) for source in range(first, last)])


def core_pair_sum(keep, send):
    heads = lax.axis_size("head")
    got = lax.ppermute(send, "head", [(h, h ^ 1) for h in range(heads)])
    return keep.astype(jnp.float32) + got.astype(jnp.float32)


def across_groups_sum(halves):
    head_group = lax.axis_index("head")
    heads = lax.axis_size("head")
    groups = heads // 2
    outer = head_group // 2
    total = lax.dynamic_index_in_dim(halves, outer, 0, keepdims=False)
    for step in range(1, groups):
        target = (outer + step) % groups
        piece = lax.dynamic_index_in_dim(halves, target, 0, keepdims=False).astype(jnp.bfloat16)
        pairs = [(h, (((h // 2) + step) % groups) * 2 + h % 2) for h in range(heads)]
        total = total + lax.ppermute(piece, "head", pairs).astype(jnp.float32)
    return total


def shift_down_sum(keep, send, entering):
    head_group = lax.axis_index("head")
    heads = lax.axis_size("head")
    segments = lax.axis_size("segment")
    groups = heads // 2
    outer = head_group // 2
    got = lax.ppermute(send, "head", [(h, h ^ 1) for h in range(heads)])
    total = []
    for step in range(groups):
        target = (outer + step) % groups
        piece = lax.dynamic_index_in_dim(keep, target, 0, keepdims=False).astype(jnp.float32) + lax.dynamic_index_in_dim(
            got, target, 0, keepdims=False
        ).astype(jnp.float32)
        if step == 0:
            piece = piece + entering
        pairs = []
        for s in range(1, segments):
            for h in range(heads):
                dest = (((h // 2) + step) % groups) * 2 + h % 2
                pairs.append((s * heads + h, (s - 1) * heads + dest))
        total.append(lax.ppermute(piece.astype(jnp.bfloat16), ("segment", "head"), pairs))
    return total, got
def row_norm(values):
    return values * lax.rsqrt(jnp.mean(values * values, axis=-1, keepdims=True) + EPS)


def _live_of(init_ref, tick):
    position = init_ref[...] - lax.axis_index("segment") - tick
    shift = SEQ_BLOCKS.bit_length() - 1
    return jnp.minimum(GLOB, 1 + lax.shift_right_arithmetic(GLOB * position, jnp.int32(shift)))


def _pick_columns(full_ref, width):
    head = jnp.zeros((1, 1), jnp.int32) + lax.axis_index("head")
    picked = full_ref[:, 0:width]
    for j in range(1, full_ref.shape[1] // width):
        picked = jnp.where(head == j, full_ref[:, j * width : (j + 1) * width], picked)
    return picked


def _attention_weights(init_ref, ptr_ref, soft_ref, win_ref, summ_ref, ask_ref, look_ref, *, tick, heads_local, block):
    band_rows = BAND * block
    live = _live_of(init_ref, tick)
    own = win_ref[tick * block : (tick + 1) * block, :]
    band = win_ref[tick * block : tick * block + band_rows, :]
    queries = jnp.dot(own, ask_ref[...], preferred_element_type=jnp.float32)
    band_keys = jnp.dot(band, look_ref[...], preferred_element_type=jnp.float32)
    summary_keys = [
        jnp.dot(summ_ref[m], look_ref[...], preferred_element_type=jnp.float32) for m in range(summ_ref.shape[0])
    ]
    glob_keys = []
    for g in range(GLOB):
        slot = ptr_ref[tick : tick + 1, g : g + 1]
        picked = summary_keys[0]
        for m in range(1, len(summary_keys)):
            picked = jnp.where(slot == m, summary_keys[m], picked)
        glob_keys.append(picked)
    keys_total = band_rows + GLOB * block
    key_ids = lax.broadcasted_iota(jnp.int32, (keys_total, block), 0)
    query_ids = lax.broadcasted_iota(jnp.int32, (keys_total, block), 1)
    slot_of = (key_ids - band_rows) // block
    admitted = ((key_ids < band_rows) & ((key_ids >= block) | (key_ids <= query_ids))) | (
        (key_ids >= band_rows) & (slot_of < live)
    )
    all_keys = jnp.concatenate([band_keys] + glob_keys, axis=0)
    contract = (((1,), (1,)), ((), ()))
    for h in range(heads_local):
        cols = slice(h * CHANNEL_WIDTH, (h + 1) * CHANNEL_WIDTH)
        scale = soft_ref[0:1, h : h + 1] * (1.0 / CHANNEL_WIDTH)
        qh = row_norm(queries[:, cols])
        kh = row_norm(all_keys[:, cols])
        sc = lax.dot_general(kh, qh, contract, precision=lax.Precision.HIGHEST, preferred_element_type=jnp.float32) * scale
        ex = jnp.where(admitted, jnp.exp(sc), 0.0)
        att = (ex / jnp.sum(ex, axis=0, keepdims=True)).astype(jnp.bfloat16)
        yield h, att[0:band_rows], [att[band_rows + g * block : band_rows + (g + 1) * block] for g in range(GLOB)]


def _weights_kernel(init_ref, ptr_ref, soft_ref, win_ref, summ_ref, ask_ref, look_ref, own_ref, glob_ref, *, tick, heads_local, block):
    for h, ab, ags in _attention_weights(
        init_ref, ptr_ref, soft_ref, win_ref, summ_ref, ask_ref, look_ref, tick=tick, heads_local=heads_local, block=block
    ):
        own_ref[h] = ab[0:block]
        for g, ag in enumerate(ags):
            glob_ref[h, g * block : (g + 1) * block, :] = ag


def _partial_into(value_grad, w_ref, keep_ref, send_ref):
    contract = (((1,), (1,)), ((), ()))
    core = jnp.zeros((1, 1), jnp.int32) + lax.axis_index("head") % 2
    for g in range(w_ref.shape[0]):
        even, odd = [
            lax.dot_general(value_grad, w_ref[g, p], contract, preferred_element_type=jnp.float32).astype(keep_ref.dtype)
            for p in range(2)
        ]
        keep_ref[g] = jnp.where(core == 0, even, odd)
        send_ref[g] = jnp.where(core == 0, odd, even)


def _first_tick_kernel(
    init_ref, ptr_ref, soft_ref, win_ref, summ_ref, ask_ref, look_ref, ent_hbm, prior_ref, w_hbm,
    keep_ref, send_ref, carried_ref, glob_ref, grad_out_ref, w_ref, w_sem, grad_buf, grad_sem, *, heads_local, block
):
    width = grad_buf.shape[1]
    start = pl.multiple_of(lax.axis_index("head") * width, CHANNEL_WIDTH)
    grad_copy = pltpu.make_async_copy(ent_hbm.at[:, pl.ds(start, width)], grad_buf, grad_sem)
    grad_copy.start()
    w_copy = pltpu.make_async_copy(w_hbm, w_ref, w_sem)
    w_copy.start()
    weights = list(_attention_weights(
        init_ref, ptr_ref, soft_ref, win_ref, summ_ref, ask_ref, look_ref, tick=0, heads_local=heads_local, block=block
    ))
    grad_copy.wait()
    grad = grad_buf[...]
    grad_out_ref[...] = grad
    value_cols = []
    for h, ab, ags in weights:
        cols = slice(h * CHANNEL_WIDTH, (h + 1) * CHANNEL_WIDTH)
        gh = grad[:, cols]
        band = jnp.dot(ab[0 : 2 * block], gh, preferred_element_type=jnp.float32)
        own = prior_ref[0:block, cols].astype(jnp.float32) + band[0:block]
        value_cols.append(own.astype(jnp.bfloat16))
        carried_ref[:, cols] = prior_ref[block : 2 * block, cols].astype(jnp.float32) + band[block : 2 * block]
        for g, ag in enumerate(ags):
            glob_ref[g * block : (g + 1) * block, cols] = jnp.dot(ag, gh, preferred_element_type=jnp.float32)
    value_grad = value_cols[0] if len(value_cols) == 1 else jnp.concatenate(value_cols, axis=1)
    w_copy.wait()
    _partial_into(value_grad, w_ref, keep_ref, send_ref)


def _last_tick_kernel(obj_ref, att_ref, carried_ref, w_hbm, *rest, heads_local, block, groups, phases):
    pieces = rest[:groups]
    keep_ref, send_ref, grad_out_ref, w_ref, w_sem = rest[groups:]
    w_copy = pltpu.make_async_copy(w_hbm, w_ref, w_sem)
    w_copy.start()
    band_rows = BAND * block
    arrived = pieces[0][...].astype(jnp.float32)
    for piece in pieces[1:]:
        arrived = arrived + piece[...].astype(jnp.float32)
    last = jnp.zeros((1, 1), jnp.int32) + (lax.axis_index("segment") == phases - 1).astype(jnp.int32)
    fresh = obj_ref[...]
    grad = jnp.where(last > 0, fresh, arrived.astype(jnp.bfloat16))
    grad_out_ref[...] = grad
    value_cols = []
    for h in range(heads_local):
        cols = slice(h * CHANNEL_WIDTH, (h + 1) * CHANNEL_WIDTH)
        gh = grad[:, cols]
        own = carried_ref[:, cols] + jnp.dot(att_ref[h], gh, preferred_element_type=jnp.float32)
        value_cols.append(own.astype(jnp.bfloat16))
    value_grad = value_cols[0] if len(value_cols) == 1 else jnp.concatenate(value_cols, axis=1)
    w_copy.wait()
    _partial_into(value_grad, w_ref, keep_ref, send_ref)


def _glob_kernel(att_ref, grad_ref, out_ref, *, heads_local):
    for h in range(heads_local):
        cols = slice(h * CHANNEL_WIDTH, (h + 1) * CHANNEL_WIDTH)
        out_ref[:, cols] = jnp.dot(att_ref[h], grad_ref[:, cols], preferred_element_type=jnp.float32)


def glob_contrib(att, grad):
    heads_local, rows, block = att.shape
    local_width = grad.shape[1]
    return pl.pallas_call(
        functools.partial(_glob_kernel, heads_local=heads_local),
        out_shape=jax.ShapeDtypeStruct((rows, local_width), jnp.float32),
        in_specs=[VMEM, VMEM],
        out_specs=VMEM,
        cost_estimate=pl.CostEstimate(flops=2 * rows * block * local_width, transcendentals=0, bytes_accessed=rows * local_width * 6),
    )(att, grad)


ANY = pl.BlockSpec(memory_space=pl.ANY)
VMEM = pl.BlockSpec(memory_space=pltpu.VMEM)
KERNEL_PARAMS = pltpu.CompilerParams()
CRITICAL_PARAMS = pltpu.CompilerParams()


def first_tick(initial_segment, digest_pointer, softness, window_inputs, summary_blocks, asker, lookup, prior, weights, entering):
    block = summary_blocks.shape[1]
    local_width = asker.shape[1]
    heads_local = local_width // CHANNEL_WIDTH
    groups = weights.shape[0]
    keys_total = (BAND + GLOB) * block
    feat = window_inputs.shape[1]
    flops = 2 * feat * local_width * (block + keys_total) + 14 * keys_total * block * local_width + 4 * block * local_width * groups * local_width
    ins = [initial_segment, digest_pointer, softness, window_inputs, summary_blocks, asker, lookup, entering, prior, weights]
    return pl.pallas_call(
        functools.partial(_first_tick_kernel, heads_local=heads_local, block=block),
        out_shape=(
            jax.ShapeDtypeStruct((groups, block, local_width), jnp.bfloat16),
            jax.ShapeDtypeStruct((groups, block, local_width), jnp.bfloat16),
            jax.ShapeDtypeStruct((block, local_width), jnp.float32),
            jax.ShapeDtypeStruct((GLOB * block, local_width), jnp.float32),
            jax.ShapeDtypeStruct((block, local_width), entering.dtype),
        ),
        in_specs=[VMEM] * 7 + [ANY, VMEM, ANY],
        out_specs=(VMEM, VMEM, VMEM, VMEM, VMEM),
        scratch_shapes=[
            pltpu.VMEM(weights.shape, weights.dtype),
            pltpu.SemaphoreType.DMA(()),
            pltpu.VMEM((block, local_width), entering.dtype),
            pltpu.SemaphoreType.DMA(()),
        ],
        compiler_params=CRITICAL_PARAMS,
        cost_estimate=pl.CostEstimate(flops=flops, transcendentals=keys_total * block * heads_local, bytes_accessed=weights.size * 2 + 8 * block * local_width * 4),
    )(*ins)


def last_tick(att, carried, weights, objective, pieces, phases):
    heads_local, keys_total, block = att.shape
    local_width = carried.shape[1]
    groups = weights.shape[0]
    flops = 2 * keys_total * block * local_width + 4 * block * local_width * groups * local_width
    ins = [objective, att, carried, weights] + list(pieces)
    return pl.pallas_call(
        functools.partial(_last_tick_kernel, heads_local=heads_local, block=block, groups=len(pieces), phases=phases),
        out_shape=(
            jax.ShapeDtypeStruct((groups, block, local_width), jnp.bfloat16),
            jax.ShapeDtypeStruct((groups, block, local_width), jnp.bfloat16),
            jax.ShapeDtypeStruct((block, local_width), objective.dtype),
        ),
        in_specs=[VMEM, VMEM, VMEM, ANY] + [VMEM] * len(pieces),
        out_specs=(VMEM, VMEM, VMEM),
        scratch_shapes=[pltpu.VMEM(weights.shape, weights.dtype), pltpu.SemaphoreType.DMA(())],
        compiler_params=CRITICAL_PARAMS,
        cost_estimate=pl.CostEstimate(flops=flops, transcendentals=0, bytes_accessed=weights.size * 2 + att.size * 2 + 8 * block * local_width * 4),
    )(*ins)


def attention_weights(tick, initial_segment, digest_pointer, softness, window_inputs, summary_blocks, asker, lookup):
    block = summary_blocks.shape[1]
    local_width = asker.shape[1]
    heads_local = local_width // CHANNEL_WIDTH
    keys_total = (BAND + GLOB) * block
    feat = window_inputs.shape[1]
    flops = 2 * feat * local_width * (block + keys_total) + 12 * keys_total * block * local_width
    ins = [initial_segment, digest_pointer, softness, window_inputs, summary_blocks, asker, lookup]
    return pl.pallas_call(
        functools.partial(_weights_kernel, tick=tick, heads_local=heads_local, block=block),
        out_shape=(
            jax.ShapeDtypeStruct((heads_local, block, block), jnp.bfloat16),
            jax.ShapeDtypeStruct((heads_local, GLOB * block, block), jnp.bfloat16),
        ),
        in_specs=[VMEM] * len(ins),
        out_specs=(VMEM, VMEM),
        compiler_params=KERNEL_PARAMS,
        cost_estimate=pl.CostEstimate(flops=flops, transcendentals=keys_total * block * heads_local, bytes_accessed=keys_total * local_width * 2 + 4 * feat * local_width * 2),
    )(*ins)


def local(
    entering_deriv,
    objective_derivs,
    content_projection,
    asker_projection,
    lookup_projection,
    softness,
    window_inputs,
    digest_inputs,
    digest_pointer,
    initial_segment,
    prior_content_derivs,
):
    period_label = lax.axis_index("segment")
    phases = lax.axis_size("segment")
    head_group = lax.axis_index("head")
    heads = lax.axis_size("head")
    groups = heads // 2
    block_rows = entering_deriv.shape[0]
    local_width = content_projection.shape[1]
    summary_blocks = digest_inputs.reshape(SUMMARY, block_rows, digest_inputs.shape[1])
    weights = content_projection.reshape(groups, 2, local_width, local_width)
    summary_ids = jnp.arange(SUMMARY, dtype=jnp.int32)

    def live_of(tick_index):
        position = initial_segment[0] - period_label - tick_index
        return jnp.minimum(GLOB, 1 + GLOB * position // SEQ_BLOCKS)

    def digest_of(tick_index, glob):
        selector = (digest_pointer[tick_index][:, None] == summary_ids[None, :]).astype(jnp.float32)
        return jnp.sum(
            selector[:, :, None, None] * glob.reshape(GLOB, block_rows, local_width)[:, None], axis=0
        ).reshape(SUMMARY * block_rows, local_width)

    init = initial_segment.reshape(1, 1)
    keep0, send0, carried, glob0, grad0 = first_tick(
        init, digest_pointer, softness, window_inputs, summary_blocks,
        asker_projection, lookup_projection, prior_content_derivs, weights, entering_deriv,
    )
    feats = (window_inputs, asker_projection, lookup_projection)
    pieces, got0 = shift_down_sum(keep0, send0, grad0.astype(jnp.float32))
    _, feats = lax.optimization_barrier((got0, feats))
    later_att = attention_weights(
        1, init, digest_pointer, softness, feats[0], summary_blocks, feats[1], feats[2]
    )
    digest_running = digest_of(0, glob0)
    att_own, att_glob = later_att
    keep1, send1, grad1 = last_tick(
        att_own, carried, weights,
        lax.dynamic_slice_in_dim(objective_derivs[0:block_rows], head_group * local_width, local_width, 1),
        pieces, phases
    )
    halves1 = core_pair_sum(keep1, send1)
    halves1, grad_held = lax.optimization_barrier((halves1, grad1))
    glob1 = glob_contrib(att_glob, grad_held)
    digest_running = digest_running + digest_of(1, glob1)
    summed = across_groups_sum(halves1)
    result = (grad1.astype(jnp.float32) + summed).astype(jnp.bfloat16)
    return (result, digest_running.astype(jnp.bfloat16))


def solution(mesh):
    in_specs = (
        P("segment", None),
        P(),
        P("segment", "head"),
        P("segment", "head"),
        P("segment", "head"),
        P("segment", "head"),
        P("segment", None),
        P(),
        P("segment", None),
        P(),
        P("segment", "head"),
    )
    out_specs = (P("segment", "head"), P("segment", "head"))
    return jax.shard_map(local, mesh=mesh, in_specs=in_specs, out_specs=out_specs, check_vma=False)
```
